32 devices in a mesh: groups: 2 (over x), seq: 16 (over z, y, core).
Axes of the slice: x: 2, y: 2, z: 4, core: 2. Of those that a mesh axis runs over, the one named last changes fastest.
Arguments:
- frames_in: bfloat16 [4096, 1024], P(('groups', 'seq')), parts along dimension 0, may hold values from -6 to 6
- query_proj: bfloat16 [4096, 512], P(('groups', 'seq')), parts along dimension 0, may hold values from -6 to 6
- key_proj: bfloat16 [4096, 512], P(('groups', 'seq')), parts along dimension 0, may hold values from -6 to 6
- value_proj: bfloat16 [4096, 512], P(('groups', 'seq')), parts along dimension 0, may hold values from -6 to 6
- utterance_lengths: int32 [32], P('groups'), parts along dimension 0, may hold values from 1 to 256, 2048 in all
- bucket_table: int32 [767], replicated, may hold values from 0 to 31
- bucket_bias: float32 [32, 8], replicated, may hold values from -4 to 4
- out_weight: bfloat16 [512, 1024], replicated, may hold values from -0.25 to 0.25
- norm_gain: float32 [1024], replicated, may hold values from 0.1 to 1.9
- expand_weight: bfloat16 [1024, 2048], replicated, may hold values from -0.1875 to 0.1875
- depth_taps: float32 [31, 1024], replicated, may hold values from -1 to 1
- inner_gain: float32 [1024], replicated, may hold values from 0.1 to 1.9
- shrink_weight: bfloat16 [1024, 1024], replicated, may hold values from -0.1875 to 0.1875
Outputs:
- block_out: bfloat16 [4096, 1024], P(('groups', 'seq')), parts along dimension 0
The draws below stay inside these ranges and needn't reach their ends.
There are 2 independent parts, one for each index of `groups`. The reference program is written for one: setup_inputs(seed, part) draws one part's arguments, and reference() takes and returns one part's arrays. A program takes and returns all parts, laid end to end along the dimension named above; an argument that names none is the same for every part. Nothing has to cross between parts.
Inputs may be any that keep to these rules, and one draw needn't show every extreme that they name: `utterance_lengths`: they sum to 2048, and one is exactly 256.
All inputs are finite; a program needn't handle non-finite values.
Results may differ from the reference program's by a relative error of at most 0.014.
Values may be sent and summed in bfloat16 or wider, within the bound.
No kernel may reach another device: no remote copies, remote signals or barrier semaphores. Data moves between devices by JAX's collectives and lax.ppermute only.
A program may use at most 64 MiB of HBM per device.

```python
import math
import jax
import jax.numpy as jnp
import numpy as np
from jax import lax

D = 1024
HEADS = 8
HEAD_DIM = 64
KERNEL = 31
DILATION = 4
NB = 32
REACH = 2
ROWS = 128
FRAMES = 2048
UTT_MAX = 256
NUTT = 16
NREL = 767
N_SEQ = 16


def draw_frames_in(key, part):
    base_key = jax.random.fold_in(key, 21)
    row_key = jax.random.fold_in(key, 22)
    col_key = jax.random.fold_in(key, 23)
    row_scale = jnp.exp(jax.random.uniform(row_key, (FRAMES, 1), jnp.float32, math.log(0.3), math.log(3.0)))
    col_scale = jnp.exp(jax.random.uniform(col_key, (1, D), jnp.float32, math.log(0.3), math.log(3.0)))
    base_draw = jax.random.normal(base_key, (FRAMES, D), jnp.float32)
    values = base_draw * row_scale * col_scale
    return jnp.clip(values, -6.0, 6.0).astype(jnp.bfloat16)


def drawn_pair(key):
    width_all = HEADS * HEAD_DIM
    query_key = jax.random.fold_in(key, 31)
    key_key = jax.random.fold_in(key, 32)
    query_out = jnp.clip(1.4 * jax.random.normal(query_key, (FRAMES, width_all), jnp.float32), -6.0, 6.0)
    key_out = jnp.clip(1.4 * jax.random.normal(key_key, (FRAMES, width_all), jnp.float32), -6.0, 6.0)
    return (query_out, key_out)


def draw_query_proj(key, part):
    return drawn_pair(key)[0].astype(jnp.bfloat16)


def draw_key_proj(key, part):
    return drawn_pair(key)[1].astype(jnp.bfloat16)


def touch_ends(result, key, low, largest):
    place = [jax.random.randint(jax.random.fold_in(key, axis), (), 0, length) for axis, length in enumerate(result.shape)]
    main_axis = result.shape.index(max(result.shape))
    next_to = place[:main_axis] + [(place[main_axis] + 1) % result.shape[main_axis]] + place[main_axis + 1:]
    return result.at[tuple(place)].set(low).at[tuple(next_to)].set(largest)


def levels(own_key, dims, shards, low, high):
    loudness = 1.0
    for axis_at, shards_of in shards:
        heights = jax.random.uniform(jax.random.fold_in(jax.random.fold_in(own_key, 6), axis_at), (shards_of,), jnp.float32, low / len(shards), high / len(shards))
        loudness = loudness * jnp.repeat(jnp.exp(heights), dims[axis_at] // shards_of).reshape((-1,) + (1,) * (len(dims) - 1 - axis_at))
    return loudness


def length_profile(number_of, total, bound, slope):
    portions = [(1 << 20) // math.isqrt(rank ** slope) + 1 for rank in range(2, number_of + 1)]
    rest, counts = total - bound - (number_of - 1), [1] * (number_of - 1)
    while rest > 0:
        free = [i for i in range(number_of - 1) if counts[i] < bound]
        mass, budget = sum([portions[i] for i in free]), rest
        for i in free:
            extra = min(bound - counts[i], max(1, budget * portions[i] // mass), rest)
            counts[i] = counts[i] + extra
            rest = rest - extra
    return np.array([bound] + counts)


def ragged(own_key, number_of, total, reach, slope):
    if number_of == 2:
        one = jax.random.randint(own_key, (), max(1, total - reach), min(reach, total - 1) + 1)
        return jnp.stack([one, total - one])
    lengths = jnp.asarray(length_profile(number_of, total, reach, slope), jnp.int32)
    pairs = (number_of - 1) // 2
    giver, taker = lengths[1:1 + 2 * pairs:2], lengths[2:2 + 2 * pairs:2]
    room = jnp.minimum(giver - 1, reach - taker)
    moved = jax.random.randint(jax.random.fold_in(own_key, 1), (pairs,), 0, 1 << 20) % (room + 1)
    lengths = lengths.at[1:1 + 2 * pairs:2].set(giver - moved).at[2:2 + 2 * pairs:2].set(taker + moved)
    return lengths[jax.random.permutation(jax.random.fold_in(own_key, 2), number_of)]


def normal_values(stream_key, extent, width, reach, split=(), kind=jnp.bfloat16):
    loudness = levels(stream_key, extent, split, -0.22, 0.18) if split else 1.0
    values = jax.random.normal(stream_key, extent, jnp.float32) * width * loudness
    return jnp.minimum(jnp.maximum(values, -reach), reach).astype(kind)


def setup_inputs(seed: int = 0, part: int = 0) -> dict:
    splits = jax.random.split(jax.random.key(seed), 14)
    part_splits = jax.random.split(jax.random.fold_in(splits[13], part), 14)
    frames_in = draw_frames_in(jax.random.fold_in(jax.random.fold_in(splits[13], part), 71), part)
    query_proj = draw_query_proj(jax.random.fold_in(jax.random.fold_in(splits[13], part), 71), part)
    key_proj = draw_key_proj(jax.random.fold_in(jax.random.fold_in(splits[13], part), 71), part)
    value_proj = normal_values(part_splits[3], (FRAMES, HEADS * HEAD_DIM), 1.0, 6.0, ((0, 16),))
    utterance_lengths = ragged(part_splits[4], NUTT, FRAMES, UTT_MAX, 2).astype(jnp.int32)
    bucket_table = touch_ends(jax.random.randint(splits[5], (NREL,), 0, NB), jax.random.fold_in(splits[5], 1), 0, NB - 1).astype(jnp.int32)
    bucket_bias = normal_values(splits[6], (NB, HEADS), 1.0, 4.0, (), jnp.float32)
    out_weight = normal_values(splits[7], (HEADS * HEAD_DIM, D), (HEADS * HEAD_DIM) ** -0.5, 0.25)
    norm_gain = jnp.clip(1.0 + 0.18 * jax.random.normal(splits[8], (D,), jnp.float32), 0.1, 1.9)
    expand_weight = normal_values(splits[9], (D, 2 * D), D ** -0.5, 0.1875)
    depth_taps = normal_values(splits[10], (KERNEL, D), KERNEL ** -0.5, 1.0, (), jnp.float32)
    inner_gain = jnp.clip(1.0 + 0.18 * jax.random.normal(splits[11], (D,), jnp.float32), 0.1, 1.9)
    shrink_weight = normal_values(splits[12], (D, D), D ** -0.5, 0.1875)
    return {"frames_in": frames_in, "query_proj": query_proj, "key_proj": key_proj, "value_proj": value_proj, "utterance_lengths": utterance_lengths, "bucket_table": bucket_table, "bucket_bias": bucket_bias, "out_weight": out_weight, "norm_gain": norm_gain, "expand_weight": expand_weight, "depth_taps": depth_taps, "inner_gain": inner_gain, "shrink_weight": shrink_weight}


norm_epsilon = 1e-05
masked_score = -1e+30

def segment_of(positions, bounds):
    inside = lax.optimization_barrier(jnp.sum((positions[:, None] >= bounds[None, :]).astype(jnp.int32), axis=1))
    return jnp.where(positions < 0, -1, inside).astype(jnp.int32)

def layer_norm(values, gain_vec):
    row_mean = lax.optimization_barrier(jnp.mean(values, axis=-1, keepdims=True))
    centred = values - row_mean
    spread = lax.optimization_barrier(jnp.mean(centred * centred, axis=-1, keepdims=True))
    return centred * lax.rsqrt(spread + norm_epsilon) * gain_vec

def gated_units(mid, norm_gain, expand_weight):
    model_width = mid.shape[1]
    normed = layer_norm(mid.astype(jnp.float32), norm_gain).astype(jnp.bfloat16)
    hidden = jnp.dot(normed, expand_weight, preferred_element_type=jnp.float32)
    return (hidden[:, :model_width] * jax.nn.sigmoid(hidden[:, model_width:])).astype(jnp.bfloat16)

def reference(frames_in, query_proj, key_proj, value_proj, utterance_lengths, bucket_table, bucket_bias, out_weight, norm_gain, expand_weight, depth_taps, inner_gain, shrink_weight):
    total_rows = ROWS * N_SEQ
    att_width = HEADS * HEAD_DIM
    bounds = jnp.cumsum(utterance_lengths).astype(jnp.int32)
    segments = segment_of(jnp.arange(total_rows, dtype=jnp.int32), bounds)
    margin = REACH * ROWS
    window_rows = (2 * REACH + 1) * ROWS
    key_pad = jnp.pad(key_proj, ((margin, margin), (0, 0)))
    value_pad = jnp.pad(value_proj, ((margin, margin), (0, 0)))
    segment_pad = jnp.pad(segments, (margin, margin), constant_values=-1)
    bias_line = bucket_bias[bucket_table].T
    rel_index = (jnp.arange(window_rows, dtype=jnp.int32)[None, :] - jnp.arange(ROWS, dtype=jnp.int32)[:, None] + ROWS - 1).astype(jnp.int32)
    block_bias = bias_line[:, rel_index]
    scaling = HEAD_DIM ** (-0.5)

    def one_block(block_index):
        first_row = (block_index * ROWS).astype(jnp.int32)
        queries = lax.dynamic_slice_in_dim(query_proj, first_row, ROWS, 0).astype(jnp.float32).reshape(ROWS, HEADS, HEAD_DIM)
        keys_here = lax.dynamic_slice_in_dim(key_pad, first_row, window_rows, 0).astype(jnp.float32).reshape(window_rows, HEADS, HEAD_DIM)
        values_here = lax.dynamic_slice_in_dim(value_pad, first_row, window_rows, 0).astype(jnp.float32).reshape(window_rows, HEADS, HEAD_DIM)
        query_segment = lax.dynamic_slice_in_dim(segments, first_row, ROWS, 0)
        key_segment = lax.dynamic_slice_in_dim(segment_pad, first_row, window_rows, 0)
        scores = jnp.einsum('rhd,chd->hrc', queries, keys_here) * scaling + block_bias
        same_utterance = (query_segment[:, None] == key_segment[None, :])[None]
        scores = jnp.where(same_utterance, scores, masked_score)
        row_max = lax.optimization_barrier(jnp.max(scores, axis=2, keepdims=True))
        weights = jnp.exp(scores - row_max)
        row_total = lax.optimization_barrier(jnp.sum(weights, axis=2))
        rounded = lax.optimization_barrier(weights.astype(jnp.bfloat16)).astype(jnp.float32)
        weighted = jnp.einsum('hrc,chd->rhd', rounded, values_here)
        return (weighted / row_total.T[:, :, None]).astype(jnp.bfloat16).reshape(ROWS, att_width)
    attended = lax.map(one_block, jnp.arange(N_SEQ, dtype=jnp.int32)).reshape(total_rows, att_width)
    mid = (frames_in.astype(jnp.float32) + jnp.dot(attended, out_weight, preferred_element_type=jnp.float32)).astype(jnp.bfloat16)
    gated = gated_units(mid, norm_gain, expand_weight)
    halo_rows = DILATION * (KERNEL - 1) // 2
    widened = jnp.pad(gated, ((halo_rows, halo_rows), (0, 0))).astype(jnp.float32)
    conv_sum = jnp.zeros((total_rows, D), jnp.float32)
    for tap_index in range(KERNEL):
        conv_sum = conv_sum + depth_taps[tap_index] * widened[DILATION * tap_index:DILATION * tap_index + total_rows]
    inner_normed = layer_norm(conv_sum, inner_gain)
    activated = (inner_normed * jax.nn.sigmoid(inner_normed)).astype(jnp.bfloat16)
    return (mid.astype(jnp.float32) + jnp.dot(activated, shrink_weight, preferred_element_type=jnp.float32)).astype(jnp.bfloat16)
```

```python
import jax
import jax.numpy as jnp
from jax import lax
from jax.experimental import pallas as pl
from jax.experimental.pallas import tpu as pltpu
from jax.sharding import PartitionSpec as P

KERNEL = 31
DILATION = 4
REACH = 2
LANES = 128

norm_epsilon = 1e-05
masked_score = -1e30


def shifted(value, axis, steps):
    count = lax.axis_size(axis)
    leading, last = (max(0, -steps), min(count, count - steps))
    return lax.ppermute(value, axis, [(source, source + steps) for source in range(leading, last)])


def layer_norm(values, gain_vec):
    row_mean = jnp.mean(values, axis=-1, keepdims=True)
    centred = values - row_mean
    spread = jnp.mean(centred * centred, axis=-1, keepdims=True)
    return centred * lax.rsqrt(spread + norm_epsilon) * gain_vec


def sigmoid(values):
    return 1.0 / (1.0 + jnp.exp(-values))


def attention_kernel(
    meta_ref, len_ref, table_ref, bias_t_ref, q_ref,
    k0, k1, k2, k3, k4, v0, v1, v2, v3, v4,
    x_ref, gain_ref, ow_hbm, ew_hbm,
    mid_ref, head_ref, tail_ref,
    ow_vmem, ew_vmem, sems, att_ref,
):
    ow_copy = pltpu.make_async_copy(ow_hbm, ow_vmem, sems.at[0])
    ew_copy = pltpu.make_async_copy(ew_hbm, ew_vmem, sems.at[1])
    ow_copy.start()
    ew_copy.start()
    k_refs = (k0, k1, k2, k3, k4)
    v_refs = (v0, v1, v2, v3, v4)
    rows, att_width = q_ref.shape
    heads = bias_t_ref.shape[0]
    buckets = bias_t_ref.shape[1]
    head_width = att_width // heads
    width = len(k_refs) * rows
    line_len = table_ref.shape[1]

    base = meta_ref[0]
    qpos = base + lax.broadcasted_iota(jnp.int32, (rows, 1), 0)
    kpos = base - REACH * rows + lax.broadcasted_iota(jnp.int32, (1, width), 1)

    def seg_step(u, carry):
        run, qs, ks = carry
        run = run + len_ref[u]
        return run, qs + (qpos >= run).astype(jnp.int32), ks + (kpos >= run).astype(jnp.int32)

    _, qseg, kseg = lax.fori_loop(
        0, len_ref.shape[0], seg_step,
        (jnp.int32(0), jnp.zeros((rows, 1), jnp.int32), jnp.zeros((1, width), jnp.int32)),
    )
    kseg = jnp.where(kpos < 0, -1, kseg)
    same = qseg == kseg

    table = table_ref[...]
    bias_t = bias_t_ref[...]
    line = jnp.zeros((heads, line_len), jnp.float32)
    for b in range(buckets):
        line = jnp.where(table == b, bias_t[:, b:b + 1], line)

    scaling = head_width ** (-0.5)
    lane = lax.broadcasted_iota(jnp.int32, (rows, LANES), 1)
    per_pair = LANES // head_width
    for pair in range(att_width // LANES):
        cols = slice(pair * LANES, (pair + 1) * LANES)
        q_pair = q_ref[:, cols]
        k_pair = jnp.concatenate([r[:, cols] for r in k_refs], axis=0)
        v_pair = jnp.concatenate([r[:, cols] for r in v_refs], axis=0)
        result = None
        for sub in range(per_pair):
            head = pair * per_pair + sub
            in_head = (lane >= sub * head_width) & (lane < (sub + 1) * head_width)
            q_head = jnp.where(in_head, q_pair, jnp.zeros_like(q_pair))
            spread = jnp.broadcast_to(line[head:head + 1, :], (rows, line_len))
            skew = pltpu.roll(spread, line_len - rows + 1, 1, stride=1, stride_axis=0)[:, :width]
            bias = jnp.where(same, skew, masked_score)
            scores = lax.dot_general(
                q_head, k_pair, (((1,), (1,)), ((), ())), preferred_element_type=jnp.float32
            )
            scores = scores * scaling + bias
            top = jnp.max(scores, axis=1, keepdims=True)
            weights = jnp.exp(scores - top)
            total = jnp.sum(weights, axis=1, keepdims=True)
            summed = jnp.dot(weights.astype(jnp.bfloat16), v_pair, preferred_element_type=jnp.float32)
            part = summed / total
            result = part if result is None else jnp.where(in_head, part, result)
        att_ref[:, cols] = result.astype(jnp.bfloat16)

    ow_copy.wait()
    projected = jnp.dot(att_ref[...], ow_vmem[...], preferred_element_type=jnp.float32)
    mid = (x_ref[...].astype(jnp.float32) + projected).astype(jnp.bfloat16)
    mid_ref[...] = mid
    normed = layer_norm(mid.astype(jnp.float32), gain_ref[...]).astype(jnp.bfloat16)
    model_width = mid.shape[1]
    ew_copy.wait()
    value_half = jnp.dot(normed, ew_vmem[:, :model_width], preferred_element_type=jnp.float32)
    gate_half = jnp.dot(normed, ew_vmem[:, model_width:], preferred_element_type=jnp.float32)
    gated = (value_half * sigmoid(gate_half)).astype(jnp.bfloat16)
    half = head_ref.shape[0]
    head_ref[...] = gated[:half]
    tail_ref[...] = gated[half:]


def conv_kernel(
    prev_ref, head_ref, tail_ref, next_ref, taps_ref, gain_ref, mid_ref, sw_hbm,
    out_ref, win_ref, conv_ref, sw_vmem, sems,
):
    sw_copy = pltpu.make_async_copy(sw_hbm, sw_vmem, sems.at[0])
    sw_copy.start()
    half = head_ref.shape[0]
    rows, model_width = mid_ref.shape
    win_ref[0:half, :] = prev_ref[...].astype(jnp.float32)
    win_ref[half:2 * half, :] = head_ref[...].astype(jnp.float32)
    win_ref[2 * half:3 * half, :] = tail_ref[...].astype(jnp.float32)
    win_ref[3 * half:4 * half, :] = next_ref[...].astype(jnp.float32)
    reach = DILATION * (KERNEL - 1) // 2
    start = half - reach

    def chunk(c, carry):
        lanes = pl.ds(pl.multiple_of(c * LANES, LANES), LANES)
        acc = jnp.zeros((rows, LANES), jnp.float32)
        for tap in range(KERNEL):
            first = start + DILATION * tap
            acc = acc + taps_ref[tap:tap + 1, lanes] * win_ref[first:first + rows, lanes]
        conv_ref[:, lanes] = acc
        return carry

    lax.fori_loop(0, model_width // LANES, chunk, 0)
    inner = layer_norm(conv_ref[...], gain_ref[...])
    activated = (inner * sigmoid(inner)).astype(jnp.bfloat16)
    sw_copy.wait()
    shrunk = jnp.dot(activated, sw_vmem[...], preferred_element_type=jnp.float32)
    out_ref[...] = (mid_ref[...].astype(jnp.float32) + shrunk).astype(out_ref.dtype)


def on_device(
    frames_in,
    query_proj,
    key_proj,
    value_proj,
    utterance_lengths,
    bucket_table,
    bucket_bias,
    out_weight,
    norm_gain,
    expand_weight,
    depth_taps,
    inner_gain,
    shrink_weight,
):
    rows, att_width = query_proj.shape
    model_width = frames_in.shape[1]
    heads = bucket_bias.shape[1]
    device_index = lax.axis_index("seq")
    meta = (device_index * rows).astype(jnp.int32).reshape(1)
    line_len = -(-bucket_table.shape[0] // LANES) * LANES
    table = jnp.pad(bucket_table, (0, line_len - bucket_table.shape[0])).reshape(1, line_len)
    bias_t = bucket_bias.T

    received = {0: (key_proj, value_proj)}
    for hop in range(1, REACH + 1):
        received[hop] = shifted((key_proj, value_proj), "seq", -hop)
        received[-hop] = shifted((key_proj, value_proj), "seq", hop)
    order = list(range(-REACH, REACH + 1))
    k_blocks = [received[h][0] for h in order]
    v_blocks = [received[h][1] for h in order]

    half = rows // 2
    vmem = pl.BlockSpec(memory_space=pltpu.VMEM)
    smem = pl.BlockSpec(memory_space=pltpu.SMEM)
    anywhere = pl.BlockSpec(memory_space=pl.ANY)
    window = len(order) * rows
    attn_flops = 2 * 2 * heads * rows * window * LANES + 2 * rows * att_width * model_width + 2 * rows * model_width * 2 * model_width
    attn_bytes = 2 * (rows * att_width * (1 + 2 * len(order)) + rows * model_width * 2 + att_width * model_width + model_width * 2 * model_width)
    mid, g_head, g_tail = pl.pallas_call(
        attention_kernel,
        out_shape=(
            jax.ShapeDtypeStruct((rows, model_width), jnp.bfloat16),
            jax.ShapeDtypeStruct((half, model_width), jnp.bfloat16),
            jax.ShapeDtypeStruct((rows - half, model_width), jnp.bfloat16),
        ),
        in_specs=[smem, smem] + [vmem] * (3 + 2 * len(order)) + [vmem, vmem, anywhere, anywhere],
        out_specs=(vmem, vmem, vmem),
        scratch_shapes=[
            pltpu.VMEM((att_width, model_width), jnp.bfloat16),
            pltpu.VMEM((model_width, 2 * model_width), jnp.bfloat16),
            pltpu.SemaphoreType.DMA((2,)),
            pltpu.VMEM((rows, att_width), jnp.bfloat16),
        ],
        cost_estimate=pl.CostEstimate(
            flops=attn_flops, transcendentals=heads * rows * window + rows * model_width, bytes_accessed=attn_bytes
        ),
        name="attention_glu",
    )(
        meta, utterance_lengths, table, bias_t, query_proj, *k_blocks, *v_blocks,
        frames_in, norm_gain.reshape(1, -1), out_weight, expand_weight,
    )

    prev_tail = shifted(g_tail, "seq", 1)
    next_head = shifted(g_head, "seq", -1)
    conv_flops = 2 * KERNEL * rows * model_width + 2 * rows * model_width * model_width
    conv_bytes = 2 * (4 * half * model_width + rows * model_width * 2 + model_width * model_width) + 4 * KERNEL * model_width
    return pl.pallas_call(
        conv_kernel,
        out_shape=jax.ShapeDtypeStruct((rows, model_width), jnp.bfloat16),
        in_specs=[vmem] * 7 + [anywhere],
        out_specs=vmem,
        scratch_shapes=[
            pltpu.VMEM((4 * half, model_width), jnp.float32),
            pltpu.VMEM((rows, model_width), jnp.float32),
            pltpu.VMEM((model_width, model_width), jnp.bfloat16),
            pltpu.SemaphoreType.DMA((1,)),
        ],
        cost_estimate=pl.CostEstimate(
            flops=conv_flops, transcendentals=rows * model_width, bytes_accessed=conv_bytes
        ),
        name="conv_shrink",
    )(prev_tail, g_head, g_tail, next_head, depth_taps, inner_gain.reshape(1, -1), mid, shrink_weight)


def solution(mesh):
    placed = (
        P(("groups", "seq"), None),
        P(("groups", "seq"), None),
        P(("groups", "seq"), None),
        P(("groups", "seq"), None),
        P("groups"),
        P(),
        P(),
        P(),
        P(),
        P(),
        P(),
        P(),
        P(),
    )
    return jax.shard_map(
        on_device, mesh=mesh, in_specs=placed, out_specs=P(("groups", "seq"), None), check_vma=False
    )
```

```python
import jax
import jax.numpy as jnp
from jax import lax
from jax.experimental import pallas as pl
from jax.experimental.pallas import tpu as pltpu
from jax.sharding import PartitionSpec as P

KERNEL = 31
DILATION = 4
REACH = 2
LANES = 128

norm_epsilon = 1e-05
masked_score = -1e30


def shifted(value, axis, steps):
    count = lax.axis_size(axis)
    leading, last = (max(0, -steps), min(count, count - steps))
    return lax.ppermute(value, axis, [(source, source + steps) for source in range(leading, last)])


def layer_norm(values, gain_vec):
    row_mean = jnp.mean(values, axis=-1, keepdims=True)
    centred = values - row_mean
    spread = jnp.mean(centred * centred, axis=-1, keepdims=True)
    return centred * lax.rsqrt(spread + norm_epsilon) * gain_vec


def sigmoid(values):
    return 1.0 / (1.0 + jnp.exp(-values))


def attention_kernel(
    meta_ref, len_ref, table_ref, bias_t_ref, q_ref,
    kv0, kv1, kv2, kv3, kv4,
    x_ref, gain_ref, ow_hbm, ew_hbm,
    mid_ref, head_ref, tail_ref,
    ow_vmem, ew_vmem, sems, att_ref,
):
    ow_copy = pltpu.make_async_copy(ow_hbm, ow_vmem, sems.at[0])
    ew_copy = pltpu.make_async_copy(ew_hbm, ew_vmem, sems.at[1])
    ow_copy.start()
    ew_copy.start()
    kv_refs = (kv0, kv1, kv2, kv3, kv4)
    rows, att_width = q_ref.shape
    heads = bias_t_ref.shape[0]
    buckets = bias_t_ref.shape[1]
    head_width = att_width // heads
    width = len(kv_refs) * rows
    line_len = table_ref.shape[1]

    base = meta_ref[0]
    qpos = base + lax.broadcasted_iota(jnp.int32, (rows, 1), 0)
    kpos = base - REACH * rows + lax.broadcasted_iota(jnp.int32, (1, width), 1)

    def seg_step(u, carry):
        run, qs, ks = carry
        run = run + len_ref[u]
        return run, qs + (qpos >= run).astype(jnp.int32), ks + (kpos >= run).astype(jnp.int32)

    _, qseg, kseg = lax.fori_loop(
        0, len_ref.shape[0], seg_step,
        (jnp.int32(0), jnp.zeros((rows, 1), jnp.int32), jnp.zeros((1, width), jnp.int32)),
    )
    kseg = jnp.where(kpos < 0, -1, kseg)
    same = qseg == kseg

    table = table_ref[...]
    bias_t = bias_t_ref[...]
    line = jnp.zeros((heads, line_len), jnp.float32)
    for b in range(buckets):
        line = jnp.where(table == b, bias_t[:, b:b + 1], line)

    scaling = head_width ** (-0.5)
    lane = lax.broadcasted_iota(jnp.int32, (rows, LANES), 1)
    per_pair = LANES // head_width
    for pair in range(att_width // LANES):
        cols = slice(pair * LANES, (pair + 1) * LANES)
        q_pair = q_ref[:, cols]
        v_cols = slice(att_width + pair * LANES, att_width + (pair + 1) * LANES)
        k_pair = jnp.concatenate([r[:, cols] for r in kv_refs], axis=0)
        v_pair = jnp.concatenate([r[:, v_cols] for r in kv_refs], axis=0)
        result = None
        for sub in range(per_pair):
            head = pair * per_pair + sub
            in_head = (lane >= sub * head_width) & (lane < (sub + 1) * head_width)
            q_head = jnp.where(in_head, q_pair, jnp.zeros_like(q_pair))
            spread = jnp.broadcast_to(line[head:head + 1, :], (rows, line_len))
            skew = pltpu.roll(spread, line_len - rows + 1, 1, stride=1, stride_axis=0)[:, :width]
            bias = jnp.where(same, skew, masked_score)
            scores = lax.dot_general(
                q_head, k_pair, (((1,), (1,)), ((), ())), preferred_element_type=jnp.float32
            )
            scores = scores * scaling + bias
            top = jnp.max(scores, axis=1, keepdims=True)
            weights = jnp.exp(scores - top)
            total = jnp.sum(weights, axis=1, keepdims=True)
            summed = jnp.dot(weights.astype(jnp.bfloat16), v_pair, preferred_element_type=jnp.float32)
            part = summed / total
            result = part if result is None else jnp.where(in_head, part, result)
        att_ref[:, cols] = result.astype(jnp.bfloat16)

    ow_copy.wait()
    projected = jnp.dot(att_ref[...], ow_vmem[...], preferred_element_type=jnp.float32)
    mid = (x_ref[...].astype(jnp.float32) + projected).astype(jnp.bfloat16)
    mid_ref[...] = mid
    normed = layer_norm(mid.astype(jnp.float32), gain_ref[...]).astype(jnp.bfloat16)
    model_width = mid.shape[1]
    ew_copy.wait()
    value_half = jnp.dot(normed, ew_vmem[:, :model_width], preferred_element_type=jnp.float32)
    gate_half = jnp.dot(normed, ew_vmem[:, model_width:], preferred_element_type=jnp.float32)
    gated = (value_half * sigmoid(gate_half)).astype(jnp.bfloat16)
    half = head_ref.shape[0]
    head_ref[...] = gated[:half]
    tail_ref[...] = gated[half:]


def conv_kernel(
    prev_ref, head_ref, tail_ref, next_ref, taps_ref, gain_ref, mid_ref, sw_hbm,
    out_ref, win_ref, conv_ref, sw_vmem, sems,
):
    sw_copy = pltpu.make_async_copy(sw_hbm, sw_vmem, sems.at[0])
    sw_copy.start()
    half = head_ref.shape[0]
    rows, model_width = mid_ref.shape
    win_ref[0:half, :] = prev_ref[...].astype(jnp.float32)
    win_ref[half:2 * half, :] = head_ref[...].astype(jnp.float32)
    win_ref[2 * half:3 * half, :] = tail_ref[...].astype(jnp.float32)
    win_ref[3 * half:4 * half, :] = next_ref[...].astype(jnp.float32)
    reach = DILATION * (KERNEL - 1) // 2
    start = half - reach

    def chunk(c, carry):
        lanes = pl.ds(pl.multiple_of(c * LANES, LANES), LANES)
        acc = jnp.zeros((rows, LANES), jnp.float32)
        for tap in range(KERNEL):
            first = start + DILATION * tap
            acc = acc + taps_ref[tap:tap + 1, lanes] * win_ref[first:first + rows, lanes]
        conv_ref[:, lanes] = acc
        return carry

    lax.fori_loop(0, model_width // LANES, chunk, 0)
    inner = layer_norm(conv_ref[...], gain_ref[...])
    activated = (inner * sigmoid(inner)).astype(jnp.bfloat16)
    sw_copy.wait()
    shrunk = jnp.dot(activated, sw_vmem[...], preferred_element_type=jnp.float32)
    out_ref[...] = (mid_ref[...].astype(jnp.float32) + shrunk).astype(out_ref.dtype)


def on_device(
    frames_in,
    query_proj,
    key_proj,
    value_proj,
    utterance_lengths,
    bucket_table,
    bucket_bias,
    out_weight,
    norm_gain,
    expand_weight,
    depth_taps,
    inner_gain,
    shrink_weight,
):
    rows, att_width = query_proj.shape
    model_width = frames_in.shape[1]
    heads = bucket_bias.shape[1]
    device_index = lax.axis_index("seq")
    meta = (device_index * rows).astype(jnp.int32).reshape(1)
    line_len = -(-bucket_table.shape[0] // LANES) * LANES
    table = jnp.pad(bucket_table, (0, line_len - bucket_table.shape[0])).reshape(1, line_len)
    bias_t = bucket_bias.T

    packed = jnp.concatenate([key_proj, value_proj], axis=1)
    received = {0: packed}
    for hop in range(REACH, 0, -1):
        received[hop] = shifted(packed, "seq", -hop)
        received[-hop] = shifted(packed, "seq", hop)
    order = list(range(-REACH, REACH + 1))
    kv_blocks = [received[h] for h in order]

    half = rows // 2
    vmem = pl.BlockSpec(memory_space=pltpu.VMEM)
    smem = pl.BlockSpec(memory_space=pltpu.SMEM)
    anywhere = pl.BlockSpec(memory_space=pl.ANY)
    window = len(order) * rows
    attn_flops = 2 * 2 * heads * rows * window * LANES + 2 * rows * att_width * model_width + 2 * rows * model_width * 2 * model_width
    attn_bytes = 2 * (rows * att_width * (1 + 2 * len(order)) + rows * model_width * 2 + att_width * model_width + model_width * 2 * model_width)
    mid, g_head, g_tail = pl.pallas_call(
        attention_kernel,
        out_shape=(
            jax.ShapeDtypeStruct((rows, model_width), jnp.bfloat16),
            jax.ShapeDtypeStruct((half, model_width), jnp.bfloat16),
            jax.ShapeDtypeStruct((rows - half, model_width), jnp.bfloat16),
        ),
        in_specs=[smem, smem] + [vmem] * (3 + len(order)) + [vmem, vmem, anywhere, anywhere],
        out_specs=(vmem, vmem, vmem),
        scratch_shapes=[
            pltpu.VMEM((att_width, model_width), jnp.bfloat16),
            pltpu.VMEM((model_width, 2 * model_width), jnp.bfloat16),
            pltpu.SemaphoreType.DMA((2,)),
            pltpu.VMEM((rows, att_width), jnp.bfloat16),
        ],
        cost_estimate=pl.CostEstimate(
            flops=attn_flops, transcendentals=heads * rows * window + rows * model_width, bytes_accessed=attn_bytes
        ),
        name="attention_glu",
    )(
        meta, utterance_lengths, table, bias_t, query_proj, *kv_blocks,
        frames_in, norm_gain.reshape(1, -1), out_weight, expand_weight,
    )

    prev_tail = shifted(g_tail, "seq", 1)
    next_head = shifted(g_head, "seq", -1)
    conv_flops = 2 * KERNEL * rows * model_width + 2 * rows * model_width * model_width
    conv_bytes = 2 * (4 * half * model_width + rows * model_width * 2 + model_width * model_width) + 4 * KERNEL * model_width
    return pl.pallas_call(
        conv_kernel,
        out_shape=jax.ShapeDtypeStruct((rows, model_width), jnp.bfloat16),
        in_specs=[vmem] * 7 + [anywhere],
        out_specs=vmem,
        scratch_shapes=[
            pltpu.VMEM((4 * half, model_width), jnp.float32),
            pltpu.VMEM((rows, model_width), jnp.float32),
            pltpu.VMEM((model_width, model_width), jnp.bfloat16),
            pltpu.SemaphoreType.DMA((1,)),
        ],
        cost_estimate=pl.CostEstimate(
            flops=conv_flops, transcendentals=rows * model_width, bytes_accessed=conv_bytes
        ),
        name="conv_shrink",
    )(prev_tail, g_head, g_tail, next_head, depth_taps, inner_gain.reshape(1, -1), mid, shrink_weight)


def solution(mesh):
    placed = (
        P(("groups", "seq"), None),
        P(("groups", "seq"), None),
        P(("groups", "seq"), None),
        P(("groups", "seq"), None),
        P("groups"),
        P(),
        P(),
        P(),
        P(),
        P(),
        P(),
        P(),
        P(),
    )
    return jax.shard_map(
        on_device, mesh=mesh, in_specs=placed, out_specs=P(("groups", "seq"), None), check_vma=False
    )
```

```python
import jax
import jax.numpy as jnp
from jax import lax
from jax.experimental import pallas as pl
from jax.experimental.pallas import tpu as pltpu
from jax.sharding import PartitionSpec as P

KERNEL = 31
DILATION = 4
REACH = 2
LANES = 128

norm_epsilon = 1e-05
masked_score = -1e30


def shifted(value, axis, steps):
    count = lax.axis_size(axis)
    leading, last = (max(0, -steps), min(count, count - steps))
    return lax.ppermute(value, axis, [(source, source + steps) for source in range(leading, last)])


def layer_norm(values, gain_vec):
    row_mean = jnp.mean(values, axis=-1, keepdims=True)
    centred = values - row_mean
    spread = jnp.mean(centred * centred, axis=-1, keepdims=True)
    return centred * lax.rsqrt(spread + norm_epsilon) * gain_vec


def sigmoid(values):
    return 1.0 / (1.0 + jnp.exp(-values))


def attention_kernel(
    meta_ref, len_ref, table_ref, bias_t_ref, q_ref,
    pair_hbm, far_hbm,
    x_ref, gain_ref, ow_hbm, ew_hbm,
    mid_ref, gated_ref, cross_ref, partner_ref,
    ow_vmem, ew_vmem, sems, att_ref, win_ref,
):
    rows, att_width = q_ref.shape
    chip_rows = pair_hbm.shape[0]
    side = far_hbm.shape[0] // 2
    copies = [
        pltpu.make_async_copy(far_hbm.at[0:side], win_ref.at[0:side], sems.at[2]),
        pltpu.make_async_copy(pair_hbm, win_ref.at[side:side + chip_rows], sems.at[3]),
        pltpu.make_async_copy(far_hbm.at[side:2 * side], win_ref.at[side + chip_rows:2 * side + chip_rows], sems.at[4]),
    ]
    for copy in copies:
        copy.start()
    ow_copy = pltpu.make_async_copy(ow_hbm, ow_vmem, sems.at[0])
    ew_copy = pltpu.make_async_copy(ew_hbm, ew_vmem, sems.at[1])
    ow_copy.start()
    ew_copy.start()
    heads = bias_t_ref.shape[0]
    buckets = bias_t_ref.shape[1]
    head_width = att_width // heads
    width = (2 * REACH + 1) * rows
    line_len = table_ref.shape[1]

    base = meta_ref[0]
    core = meta_ref[1]
    first_row = pl.multiple_of(core * rows, rows)
    qpos = base + lax.broadcasted_iota(jnp.int32, (rows, 1), 0)
    kpos = base - REACH * rows + lax.broadcasted_iota(jnp.int32, (1, width), 1)

    def seg_step(u, carry):
        run, qs, ks = carry
        run = run + len_ref[u]
        return run, qs + (qpos >= run).astype(jnp.int32), ks + (kpos >= run).astype(jnp.int32)

    _, qseg, kseg = lax.fori_loop(
        0, len_ref.shape[0], seg_step,
        (jnp.int32(0), jnp.zeros((rows, 1), jnp.int32), jnp.zeros((1, width), jnp.int32)),
    )
    kseg = jnp.where(kpos < 0, -1, kseg)
    same = qseg == kseg

    table = table_ref[...]
    bias_t = bias_t_ref[...]
    line = jnp.zeros((heads, line_len), jnp.float32)
    for b in range(buckets):
        line = jnp.where(table == b, bias_t[:, b:b + 1], line)

    for copy in copies:
        copy.wait()
    scaling = head_width ** (-0.5)
    lane = lax.broadcasted_iota(jnp.int32, (rows, LANES), 1)
    per_pair = LANES // head_width
    for pair in range(att_width // LANES):
        cols = slice(pair * LANES, (pair + 1) * LANES)
        q_pair = q_ref[:, cols]
        v_cols = slice(att_width + pair * LANES, att_width + (pair + 1) * LANES)
        k_pair = win_ref[pl.ds(first_row, width), cols]
        v_pair = win_ref[pl.ds(first_row, width), v_cols]
        result = None
        for sub in range(per_pair):
            head = pair * per_pair + sub
            in_head = (lane >= sub * head_width) & (lane < (sub + 1) * head_width)
            q_head = jnp.where(in_head, q_pair, jnp.zeros_like(q_pair))
            spread = jnp.broadcast_to(line[head:head + 1, :], (rows, line_len))
            skew = pltpu.roll(spread, line_len - rows + 1, 1, stride=1, stride_axis=0)[:, :width]
            bias = jnp.where(same, skew, masked_score)
            scores = lax.dot_general(
                q_head, k_pair, (((1,), (1,)), ((), ())), preferred_element_type=jnp.float32
            )
            scores = scores * scaling + bias
            top = jnp.max(scores, axis=1, keepdims=True)
            weights = jnp.exp(scores - top)
            total = jnp.sum(weights, axis=1, keepdims=True)
            summed = jnp.dot(weights.astype(jnp.bfloat16), v_pair, preferred_element_type=jnp.float32)
            part = summed / total
            result = part if result is None else jnp.where(in_head, part, result)
        att_ref[:, cols] = result.astype(jnp.bfloat16)

    ow_copy.wait()
    projected = jnp.dot(att_ref[...], ow_vmem[...], preferred_element_type=jnp.float32)
    mid = (x_ref[...].astype(jnp.float32) + projected).astype(jnp.bfloat16)
    mid_ref[...] = mid
    normed = layer_norm(mid.astype(jnp.float32), gain_ref[...]).astype(jnp.bfloat16)
    model_width = mid.shape[1]
    ew_copy.wait()
    value_half = jnp.dot(normed, ew_vmem[:, :model_width], preferred_element_type=jnp.float32)
    gate_half = jnp.dot(normed, ew_vmem[:, model_width:], preferred_element_type=jnp.float32)
    gated = (value_half * sigmoid(gate_half)).astype(jnp.bfloat16)
    gated_ref[...] = gated
    half = cross_ref.shape[0]
    cross_ref[...] = gated_ref[pl.ds(pl.multiple_of(core * half, half), half), :]
    partner_ref[...] = gated_ref[pl.ds(pl.multiple_of((1 - core) * half, half), half), :]


def conv_kernel(
    meta_ref, gated_ref, cross_ref, pairg_ref, taps_ref, gain_ref, mid_ref, sw_hbm,
    out_ref, win_ref, conv_ref, sw_vmem, sems,
):
    sw_copy = pltpu.make_async_copy(sw_hbm, sw_vmem, sems.at[0])
    sw_copy.start()
    half = cross_ref.shape[0]
    rows, model_width = mid_ref.shape
    first_core = meta_ref[1] == 0
    cross = cross_ref[...]
    win_ref[0:half, :] = jnp.where(first_core, cross, pairg_ref[0:half, :]).astype(jnp.float32)
    win_ref[half:half + rows, :] = gated_ref[...].astype(jnp.float32)
    win_ref[half + rows:2 * half + rows, :] = jnp.where(first_core, pairg_ref[half:2 * half, :], cross).astype(jnp.float32)
    reach = DILATION * (KERNEL - 1) // 2
    start = half - reach

    def chunk(c, carry):
        lanes = pl.ds(pl.multiple_of(c * LANES, LANES), LANES)
        acc = jnp.zeros((rows, LANES), jnp.float32)
        for tap in range(KERNEL):
            first = start + DILATION * tap
            acc = acc + taps_ref[tap:tap + 1, lanes] * win_ref[first:first + rows, lanes]
        conv_ref[:, lanes] = acc
        return carry

    lax.fori_loop(0, model_width // LANES, chunk, 0)
    inner = layer_norm(conv_ref[...], gain_ref[...])
    activated = (inner * sigmoid(inner)).astype(jnp.bfloat16)
    sw_copy.wait()
    shrunk = jnp.dot(activated, sw_vmem[...], preferred_element_type=jnp.float32)
    out_ref[...] = (mid_ref[...].astype(jnp.float32) + shrunk).astype(out_ref.dtype)


def on_device(
    frames_in,
    query_proj,
    key_proj,
    value_proj,
    utterance_lengths,
    bucket_table,
    bucket_bias,
    out_weight,
    norm_gain,
    expand_weight,
    depth_taps,
    inner_gain,
    shrink_weight,
):
    rows, att_width = query_proj.shape
    model_width = frames_in.shape[1]
    heads = bucket_bias.shape[1]
    chip = lax.axis_index("chip")
    core = lax.axis_index("core")
    chips = lax.axis_size("chip")
    cores = lax.axis_size("core")
    meta = jnp.stack([(chip * cores + core) * rows, core]).astype(jnp.int32)
    line_len = -(-bucket_table.shape[0] // LANES) * LANES
    table = jnp.pad(bucket_table, (0, line_len - bucket_table.shape[0])).reshape(1, line_len)
    bias_t = bucket_bias.T

    packed = jnp.concatenate([key_proj, value_proj], axis=1)
    pair = lax.all_gather(packed, "core", tiled=True)
    outward = [(2 * (c - 1), 2 * c) for c in range(1, chips)] + [(2 * (c + 1) + 1, 2 * c + 1) for c in range(chips - 1)]
    far = lax.ppermute(pair, ("chip", "core"), outward)
    far = lax.all_gather(far, "core", tiled=True)
    order = list(range(-REACH, REACH + 1))

    half = rows // 2
    vmem = pl.BlockSpec(memory_space=pltpu.VMEM)
    smem = pl.BlockSpec(memory_space=pltpu.SMEM)
    anywhere = pl.BlockSpec(memory_space=pl.ANY)
    window = len(order) * rows
    attn_flops = 2 * 2 * heads * rows * window * LANES + 2 * rows * att_width * model_width + 2 * rows * model_width * 2 * model_width
    attn_bytes = 2 * (rows * att_width * (1 + 2 * len(order)) + rows * model_width * 2 + att_width * model_width + model_width * 2 * model_width)
    mid, gated, cross_send, partner_send = pl.pallas_call(
        attention_kernel,
        out_shape=(
            jax.ShapeDtypeStruct((rows, model_width), jnp.bfloat16),
            jax.ShapeDtypeStruct((rows, model_width), jnp.bfloat16),
            jax.ShapeDtypeStruct((half, model_width), jnp.bfloat16),
            jax.ShapeDtypeStruct((half, model_width), jnp.bfloat16),
        ),
        in_specs=[smem, smem, vmem, vmem, vmem, anywhere, anywhere, vmem, vmem, anywhere, anywhere],
        out_specs=(vmem, vmem, vmem, vmem),
        scratch_shapes=[
            pltpu.VMEM((att_width, model_width), jnp.bfloat16),
            pltpu.VMEM((model_width, 2 * model_width), jnp.bfloat16),
            pltpu.SemaphoreType.DMA((5,)),
            pltpu.VMEM((rows, att_width), jnp.bfloat16),
            pltpu.VMEM((pair.shape[0] + far.shape[0], 2 * att_width), jnp.bfloat16),
        ],
        cost_estimate=pl.CostEstimate(
            flops=attn_flops, transcendentals=heads * rows * window + rows * model_width, bytes_accessed=attn_bytes
        ),
        name="attention_glu",
    )(
        meta, utterance_lengths, table, bias_t, query_proj, pair, far,
        frames_in, norm_gain.reshape(1, -1), out_weight, expand_weight,
    )

    inward = [(2 * c + 1, 2 * c + 2) for c in range(chips - 1)] + [(2 * c, 2 * c - 1) for c in range(1, chips)]
    cross_recv = lax.ppermute(cross_send, ("chip", "core"), inward)
    partner_recv = lax.all_gather(partner_send, "core", tiled=True)
    conv_flops = 2 * KERNEL * rows * model_width + 2 * rows * model_width * model_width
    conv_bytes = 2 * (4 * half * model_width + rows * model_width * 2 + model_width * model_width) + 4 * KERNEL * model_width
    return pl.pallas_call(
        conv_kernel,
        out_shape=jax.ShapeDtypeStruct((rows, model_width), jnp.bfloat16),
        in_specs=[smem] + [vmem] * 6 + [anywhere],
        out_specs=vmem,
        scratch_shapes=[
            pltpu.VMEM((rows + 2 * half, model_width), jnp.float32),
            pltpu.VMEM((rows, model_width), jnp.float32),
            pltpu.VMEM((model_width, model_width), jnp.bfloat16),
            pltpu.SemaphoreType.DMA((1,)),
        ],
        cost_estimate=pl.CostEstimate(
            flops=conv_flops, transcendentals=rows * model_width, bytes_accessed=conv_bytes
        ),
        name="conv_shrink",
    )(meta, gated, cross_recv, partner_recv, depth_taps, inner_gain.reshape(1, -1), mid, shrink_weight)


def solution(mesh):
    groups, seq = mesh.devices.shape
    chip_mesh = jax.sharding.Mesh(mesh.devices.reshape(groups, seq // 2, 2), ("groups", "chip", "core"))
    rows_spec = P(("groups", "chip", "core"), None)
    placed = (
        rows_spec,
        rows_spec,
        rows_spec,
        rows_spec,
        P("groups"),
        P(),
        P(),
        P(),
        P(),
        P(),
        P(),
        P(),
        P(),
    )
    return jax.shard_map(
        on_device, mesh=chip_mesh, in_specs=placed, out_specs=rows_spec, check_vma=False
    )
```

```python
import jax
import jax.numpy as jnp
from jax import lax
from jax.experimental import pallas as pl
from jax.experimental.pallas import tpu as pltpu
from jax.sharding import PartitionSpec as P

KERNEL = 31
DILATION = 4
REACH = 2
LANES = 128

norm_epsilon = 1e-05
masked_score = -1e30


def shifted(value, axis, steps):
    count = lax.axis_size(axis)
    leading, last = (max(0, -steps), min(count, count - steps))
    return lax.ppermute(value, axis, [(source, source + steps) for source in range(leading, last)])


def layer_norm(values, gain_vec):
    row_mean = jnp.mean(values, axis=-1, keepdims=True)
    centred = values - row_mean
    spread = jnp.mean(centred * centred, axis=-1, keepdims=True)
    return centred * lax.rsqrt(spread + norm_epsilon) * gain_vec


def sigmoid(values):
    return 1.0 / (1.0 + jnp.exp(-values))


def attention_kernel(
    meta_ref, len_ref, table_ref, bias_t_ref, q_ref,
    prev_hbm, next_hbm, own_hbm, sel_hbm,
    x_ref, gain_ref, ow_hbm, ew_hbm,
    mid_ref, head_ref, tail_ref,
    ow_vmem, ew_vmem, sems, att_ref, win_ref,
):
    base = meta_ref[0]
    core = meta_ref[1]
    planes = prev_hbm.shape[0]
    mine = pl.ds(pl.multiple_of(core * planes, planes), planes)
    other = pl.ds(pl.multiple_of((1 - core) * planes, planes), planes)
    copies = [
        pltpu.make_async_copy(prev_hbm, win_ref.at[pl.ds(0, planes)], sems.at[2]),
        pltpu.make_async_copy(own_hbm.at[mine], win_ref.at[pl.ds(2 * planes, planes)], sems.at[3]),
        pltpu.make_async_copy(next_hbm, win_ref.at[pl.ds(4 * planes, planes)], sems.at[4]),
        pltpu.make_async_copy(
            sel_hbm.at[other], win_ref.at[pl.ds(pl.multiple_of((1 + 2 * core) * planes, planes), planes)], sems.at[5]
        ),
        pltpu.make_async_copy(
            own_hbm.at[other], win_ref.at[pl.ds(pl.multiple_of((3 - 2 * core) * planes, planes), planes)], sems.at[6]
        ),
    ]
    for copy in copies:
        copy.start()
    ow_copy = pltpu.make_async_copy(ow_hbm, ow_vmem, sems.at[0])
    ew_copy = pltpu.make_async_copy(ew_hbm, ew_vmem, sems.at[1])
    ow_copy.start()
    ew_copy.start()
    blocks = win_ref.shape[0] // planes
    rows, att_width = q_ref.shape
    heads = bias_t_ref.shape[0]
    buckets = bias_t_ref.shape[1]
    head_width = att_width // heads
    width = blocks * rows
    line_len = table_ref.shape[1]

    qpos = base + lax.broadcasted_iota(jnp.int32, (rows, 1), 0)
    kpos = base - REACH * rows + lax.broadcasted_iota(jnp.int32, (1, width), 1)

    def seg_step(u, carry):
        run, qs, ks = carry
        run = run + len_ref[u]
        return run, qs + (qpos >= run).astype(jnp.int32), ks + (kpos >= run).astype(jnp.int32)

    _, qseg, kseg = lax.fori_loop(
        0, len_ref.shape[0], seg_step,
        (jnp.int32(0), jnp.zeros((rows, 1), jnp.int32), jnp.zeros((1, width), jnp.int32)),
    )
    kseg = jnp.where(kpos < 0, -1, kseg)
    same = qseg == kseg

    table = table_ref[...]
    bias_t = bias_t_ref[...]
    line = jnp.zeros((heads, line_len), jnp.float32)
    for b in range(buckets):
        line = jnp.where(table == b, bias_t[:, b:b + 1], line)

    for copy in copies:
        copy.wait()
    scaling = head_width ** (-0.5)
    lane = lax.broadcasted_iota(jnp.int32, (rows, LANES), 1)
    per_pair = LANES // head_width
    for pair in range(att_width // LANES):
        cols = slice(pair * LANES, (pair + 1) * LANES)
        q_pair = q_ref[:, cols]
        k_pair = jnp.concatenate([win_ref[planes * j, :, cols] for j in range(blocks)], axis=0)
        v_pair = jnp.concatenate([win_ref[planes * j + 1, :, cols] for j in range(blocks)], axis=0)
        result = None
        for sub in range(per_pair):
            head = pair * per_pair + sub
            in_head = (lane >= sub * head_width) & (lane < (sub + 1) * head_width)
            q_head = jnp.where(in_head, q_pair, jnp.zeros_like(q_pair))
            spread = jnp.broadcast_to(line[head:head + 1, :], (rows, line_len))
            skew = pltpu.roll(spread, line_len - rows + 1, 1, stride=1, stride_axis=0)[:, :width]
            bias = jnp.where(same, skew, masked_score)
            scores = lax.dot_general(
                q_head, k_pair, (((1,), (1,)), ((), ())), preferred_element_type=jnp.float32
            )
            scores = scores * scaling + bias
            top = jnp.max(scores, axis=1, keepdims=True)
            weights = jnp.exp(scores - top)
            total = jnp.sum(weights, axis=1, keepdims=True)
            summed = jnp.dot(weights.astype(jnp.bfloat16), v_pair, preferred_element_type=jnp.float32)
            part = summed / total
            result = part if result is None else jnp.where(in_head, part, result)
        att_ref[:, cols] = result.astype(jnp.bfloat16)

    ow_copy.wait()
    projected = jnp.dot(att_ref[...], ow_vmem[...], preferred_element_type=jnp.float32)
    mid = (x_ref[...].astype(jnp.float32) + projected).astype(jnp.bfloat16)
    mid_ref[...] = mid
    normed = layer_norm(mid.astype(jnp.float32), gain_ref[...]).astype(jnp.bfloat16)
    model_width = mid.shape[1]
    ew_copy.wait()
    value_half = jnp.dot(normed, ew_vmem[:, :model_width], preferred_element_type=jnp.float32)
    gate_half = jnp.dot(normed, ew_vmem[:, model_width:], preferred_element_type=jnp.float32)
    gated = (value_half * sigmoid(gate_half)).astype(jnp.bfloat16)
    half = head_ref.shape[0]
    head_ref[...] = gated[:half]
    tail_ref[...] = gated[half:]


def conv_kernel(
    prev_ref, head_ref, tail_ref, next_ref, taps_ref, gain_ref, mid_ref, sw_hbm,
    out_ref, win_ref, conv_ref, sw_vmem, sems,
):
    sw_copy = pltpu.make_async_copy(sw_hbm, sw_vmem, sems.at[0])
    sw_copy.start()
    half = head_ref.shape[0]
    rows, model_width = mid_ref.shape
    win_ref[0:half, :] = prev_ref[...].astype(jnp.float32)
    win_ref[half:2 * half, :] = head_ref[...].astype(jnp.float32)
    win_ref[2 * half:3 * half, :] = tail_ref[...].astype(jnp.float32)
    win_ref[3 * half:4 * half, :] = next_ref[...].astype(jnp.float32)
    reach = DILATION * (KERNEL - 1) // 2
    start = half - reach

    def chunk(c, carry):
        lanes = pl.ds(pl.multiple_of(c * LANES, LANES), LANES)
        acc = jnp.zeros((rows, LANES), jnp.float32)
        for tap in range(KERNEL):
            first = start + DILATION * tap
            acc = acc + taps_ref[tap:tap + 1, lanes] * win_ref[first:first + rows, lanes]
        conv_ref[:, lanes] = acc
        return carry

    lax.fori_loop(0, model_width // LANES, chunk, 0)
    inner = layer_norm(conv_ref[...], gain_ref[...])
    activated = (inner * sigmoid(inner)).astype(jnp.bfloat16)
    sw_copy.wait()
    shrunk = jnp.dot(activated, sw_vmem[...], preferred_element_type=jnp.float32)
    out_ref[...] = (mid_ref[...].astype(jnp.float32) + shrunk).astype(out_ref.dtype)


def on_device(
    frames_in,
    query_proj,
    key_proj,
    value_proj,
    utterance_lengths,
    bucket_table,
    bucket_bias,
    out_weight,
    norm_gain,
    expand_weight,
    depth_taps,
    inner_gain,
    shrink_weight,
):
    rows, att_width = query_proj.shape
    model_width = frames_in.shape[1]
    heads = bucket_bias.shape[1]
    core = lax.axis_index("core")
    cores = lax.axis_size("core")
    count = lax.axis_size("chip") * cores
    device_index = lax.axis_index("chip") * cores + core
    meta = jnp.stack([device_index * rows, core]).astype(jnp.int32)

    def lin_shift(value, steps):
        leading, last = (max(0, -steps), min(count, count - steps))
        return lax.ppermute(value, ("chip", "core"), [(s, s + steps) for s in range(leading, last)])

    line_len = -(-bucket_table.shape[0] // LANES) * LANES
    table = jnp.pad(bucket_table, (0, line_len - bucket_table.shape[0])).reshape(1, line_len)
    bias_t = bucket_bias.T

    packed = jnp.stack([key_proj, value_proj])
    from_prev = lin_shift(packed, REACH)
    from_next = lin_shift(packed, -REACH)
    own_pair = lax.all_gather(packed, "core", tiled=True)
    sel = jnp.where(core == 0, from_next, from_prev)
    sel_pair = lax.all_gather(sel, "core", tiled=True)
    order = list(range(-REACH, REACH + 1))

    half = rows // 2
    vmem = pl.BlockSpec(memory_space=pltpu.VMEM)
    smem = pl.BlockSpec(memory_space=pltpu.SMEM)
    anywhere = pl.BlockSpec(memory_space=pl.ANY)
    window = len(order) * rows
    attn_flops = 2 * 2 * heads * rows * window * LANES + 2 * rows * att_width * model_width + 2 * rows * model_width * 2 * model_width
    attn_bytes = 2 * (rows * att_width * (1 + 2 * len(order)) + rows * model_width * 2 + att_width * model_width + model_width * 2 * model_width)
    mid, g_head, g_tail = pl.pallas_call(
        attention_kernel,
        out_shape=(
            jax.ShapeDtypeStruct((rows, model_width), jnp.bfloat16),
            jax.ShapeDtypeStruct((half, model_width), jnp.bfloat16),
            jax.ShapeDtypeStruct((rows - half, model_width), jnp.bfloat16),
        ),
        in_specs=[smem, smem, vmem, vmem, vmem] + [anywhere] * 4 + [vmem, vmem, anywhere, anywhere],
        out_specs=(vmem, vmem, vmem),
        scratch_shapes=[
            pltpu.VMEM((att_width, model_width), jnp.bfloat16),
            pltpu.VMEM((model_width, 2 * model_width), jnp.bfloat16),
            pltpu.SemaphoreType.DMA((7,)),
            pltpu.VMEM((rows, att_width), jnp.bfloat16),
            pltpu.VMEM((len(order) * packed.shape[0], rows, att_width), jnp.bfloat16),
        ],
        cost_estimate=pl.CostEstimate(
            flops=attn_flops, transcendentals=heads * rows * window + rows * model_width, bytes_accessed=attn_bytes
        ),
        name="attention_glu",
    )(
        meta, utterance_lengths, table, bias_t, query_proj, from_prev, from_next, own_pair, sel_pair,
        frames_in, norm_gain.reshape(1, -1), out_weight, expand_weight,
    )

    prev_tail = lin_shift(g_tail, 1)
    next_head = lin_shift(g_head, -1)
    conv_flops = 2 * KERNEL * rows * model_width + 2 * rows * model_width * model_width
    conv_bytes = 2 * (4 * half * model_width + rows * model_width * 2 + model_width * model_width) + 4 * KERNEL * model_width
    return pl.pallas_call(
        conv_kernel,
        out_shape=jax.ShapeDtypeStruct((rows, model_width), jnp.bfloat16),
        in_specs=[vmem] * 7 + [anywhere],
        out_specs=vmem,
        scratch_shapes=[
            pltpu.VMEM((4 * half, model_width), jnp.float32),
            pltpu.VMEM((rows, model_width), jnp.float32),
            pltpu.VMEM((model_width, model_width), jnp.bfloat16),
            pltpu.SemaphoreType.DMA((1,)),
        ],
        cost_estimate=pl.CostEstimate(
            flops=conv_flops, transcendentals=rows * model_width, bytes_accessed=conv_bytes
        ),
        name="conv_shrink",
    )(prev_tail, g_head, g_tail, next_head, depth_taps, inner_gain.reshape(1, -1), mid, shrink_weight)


def solution(mesh):
    groups, seq = mesh.devices.shape
    chip_mesh = jax.sharding.Mesh(mesh.devices.reshape(groups, seq // 2, 2), ("groups", "chip", "core"))
    rows_spec = P(("groups", "chip", "core"), None)
    placed = (
        rows_spec,
        rows_spec,
        rows_spec,
        rows_spec,
        P("groups"),
        P(),
        P(),
        P(),
        P(),
        P(),
        P(),
        P(),
        P(),
    )
    return jax.shard_map(
        on_device, mesh=chip_mesh, in_specs=placed, out_specs=rows_spec, check_vma=False
    )
```

```python
import jax
import jax.numpy as jnp
from jax import lax
from jax.experimental import pallas as pl
from jax.experimental.pallas import tpu as pltpu
from jax.sharding import PartitionSpec as P

KERNEL = 31
DILATION = 4
REACH = 2
LANES = 128

norm_epsilon = 1e-05
masked_score = -1e30


def shifted(value, axis, steps):
    count = lax.axis_size(axis)
    leading, last = (max(0, -steps), min(count, count - steps))
    return lax.ppermute(value, axis, [(source, source + steps) for source in range(leading, last)])


def layer_norm(values, gain_vec):
    row_mean = jnp.mean(values, axis=-1, keepdims=True)
    centred = values - row_mean
    spread = jnp.mean(centred * centred, axis=-1, keepdims=True)
    return centred * lax.rsqrt(spread + norm_epsilon) * gain_vec


def sigmoid(values):
    return 1.0 / (1.0 + jnp.exp(-values))


def attention_kernel(
    meta_ref, len_ref, table_ref, bias_t_ref, q_ref,
    prev_hbm, next_hbm, own_hbm, sel_hbm,
    x_ref, gain_ref, ow_hbm, ew_hbm,
    mid_ref, gated_ref, cross_ref, partner_ref,
    ow_vmem, ew_vmem, sems, att_ref, win_ref,
):
    base = meta_ref[0]
    core = meta_ref[1]
    planes = prev_hbm.shape[0]
    mine = pl.ds(pl.multiple_of(core * planes, planes), planes)
    other = pl.ds(pl.multiple_of((1 - core) * planes, planes), planes)
    copies = [
        pltpu.make_async_copy(prev_hbm, win_ref.at[pl.ds(0, planes)], sems.at[2]),
        pltpu.make_async_copy(own_hbm.at[mine], win_ref.at[pl.ds(2 * planes, planes)], sems.at[3]),
        pltpu.make_async_copy(next_hbm, win_ref.at[pl.ds(4 * planes, planes)], sems.at[4]),
        pltpu.make_async_copy(
            sel_hbm.at[other], win_ref.at[pl.ds(pl.multiple_of((1 + 2 * core) * planes, planes), planes)], sems.at[5]
        ),
        pltpu.make_async_copy(
            own_hbm.at[other], win_ref.at[pl.ds(pl.multiple_of((3 - 2 * core) * planes, planes), planes)], sems.at[6]
        ),
    ]
    for copy in copies:
        copy.start()
    ow_copy = pltpu.make_async_copy(ow_hbm, ow_vmem, sems.at[0])
    ew_copy = pltpu.make_async_copy(ew_hbm, ew_vmem, sems.at[1])
    ow_copy.start()
    ew_copy.start()
    blocks = win_ref.shape[0] // planes
    rows, att_width = q_ref.shape
    heads = bias_t_ref.shape[0]
    buckets = bias_t_ref.shape[1]
    head_width = att_width // heads
    width = blocks * rows
    line_len = table_ref.shape[1]

    qpos = base + lax.broadcasted_iota(jnp.int32, (rows, 1), 0)
    kpos = base - REACH * rows + lax.broadcasted_iota(jnp.int32, (1, width), 1)

    def seg_step(u, carry):
        run, qs, ks = carry
        run = run + len_ref[u]
        return run, qs + (qpos >= run).astype(jnp.int32), ks + (kpos >= run).astype(jnp.int32)

    _, qseg, kseg = lax.fori_loop(
        0, len_ref.shape[0], seg_step,
        (jnp.int32(0), jnp.zeros((rows, 1), jnp.int32), jnp.zeros((1, width), jnp.int32)),
    )
    kseg = jnp.where(kpos < 0, -1, kseg)
    same = qseg == kseg

    table = table_ref[...]
    bias_t = bias_t_ref[...]
    line = jnp.zeros((heads, line_len), jnp.float32)
    for b in range(buckets):
        line = jnp.where(table == b, bias_t[:, b:b + 1], line)

    for copy in copies:
        copy.wait()
    scaling = head_width ** (-0.5)
    lane = lax.broadcasted_iota(jnp.int32, (rows, LANES), 1)
    per_pair = LANES // head_width
    for pair in range(att_width // LANES):
        cols = slice(pair * LANES, (pair + 1) * LANES)
        q_pair = q_ref[:, cols]
        k_pair = jnp.concatenate([win_ref[planes * j, :, cols] for j in range(blocks)], axis=0)
        v_pair = jnp.concatenate([win_ref[planes * j + 1, :, cols] for j in range(blocks)], axis=0)
        result = None
        for sub in range(per_pair):
            head = pair * per_pair + sub
            in_head = (lane >= sub * head_width) & (lane < (sub + 1) * head_width)
            q_head = jnp.where(in_head, q_pair, jnp.zeros_like(q_pair))
            spread = jnp.broadcast_to(line[head:head + 1, :], (rows, line_len))
            skew = pltpu.roll(spread, line_len - rows + 1, 1, stride=1, stride_axis=0)[:, :width]
            bias = jnp.where(same, skew, masked_score)
            scores = lax.dot_general(
                q_head, k_pair, (((1,), (1,)), ((), ())), preferred_element_type=jnp.float32
            )
            scores = scores * scaling + bias
            top = jnp.max(scores, axis=1, keepdims=True)
            weights = jnp.exp(scores - top)
            total = jnp.sum(weights, axis=1, keepdims=True)
            summed = jnp.dot(weights.astype(jnp.bfloat16), v_pair, preferred_element_type=jnp.float32)
            part = summed / total
            result = part if result is None else jnp.where(in_head, part, result)
        att_ref[:, cols] = result.astype(jnp.bfloat16)

    ow_copy.wait()
    projected = jnp.dot(att_ref[...], ow_vmem[...], preferred_element_type=jnp.float32)
    mid = (x_ref[...].astype(jnp.float32) + projected).astype(jnp.bfloat16)
    mid_ref[...] = mid
    normed = layer_norm(mid.astype(jnp.float32), gain_ref[...]).astype(jnp.bfloat16)
    model_width = mid.shape[1]
    ew_copy.wait()
    value_half = jnp.dot(normed, ew_vmem[:, :model_width], preferred_element_type=jnp.float32)
    gate_half = jnp.dot(normed, ew_vmem[:, model_width:], preferred_element_type=jnp.float32)
    gated = (value_half * sigmoid(gate_half)).astype(jnp.bfloat16)
    gated_ref[...] = gated
    half = cross_ref.shape[0]
    cross_ref[...] = gated_ref[pl.ds(pl.multiple_of(core * half, half), half), :]
    partner_ref[...] = gated_ref[pl.ds(pl.multiple_of((1 - core) * half, half), half), :]


def conv_kernel(
    meta_ref, gated_ref, cross_ref, pairg_ref, taps_ref, gain_ref, mid_ref, sw_hbm,
    out_ref, win_ref, conv_ref, sw_vmem, sems,
):
    sw_copy = pltpu.make_async_copy(sw_hbm, sw_vmem, sems.at[0])
    sw_copy.start()
    half = cross_ref.shape[0]
    rows, model_width = mid_ref.shape
    first_core = meta_ref[1] == 0
    cross = cross_ref[...]
    win_ref[0:half, :] = jnp.where(first_core, cross, pairg_ref[0:half, :]).astype(jnp.float32)
    win_ref[half:half + rows, :] = gated_ref[...].astype(jnp.float32)
    win_ref[half + rows:2 * half + rows, :] = jnp.where(first_core, pairg_ref[half:2 * half, :], cross).astype(jnp.float32)
    reach = DILATION * (KERNEL - 1) // 2
    start = half - reach

    def chunk(c, carry):
        lanes = pl.ds(pl.multiple_of(c * LANES, LANES), LANES)
        acc = jnp.zeros((rows, LANES), jnp.float32)
        for tap in range(KERNEL):
            first = start + DILATION * tap
            acc = acc + taps_ref[tap:tap + 1, lanes] * win_ref[first:first + rows, lanes]
        conv_ref[:, lanes] = acc
        return carry

    lax.fori_loop(0, model_width // LANES, chunk, 0)
    inner = layer_norm(conv_ref[...], gain_ref[...])
    activated = (inner * sigmoid(inner)).astype(jnp.bfloat16)
    sw_copy.wait()
    shrunk = jnp.dot(activated, sw_vmem[...], preferred_element_type=jnp.float32)
    out_ref[...] = (mid_ref[...].astype(jnp.float32) + shrunk).astype(out_ref.dtype)


def on_device(
    frames_in,
    query_proj,
    key_proj,
    value_proj,
    utterance_lengths,
    bucket_table,
    bucket_bias,
    out_weight,
    norm_gain,
    expand_weight,
    depth_taps,
    inner_gain,
    shrink_weight,
):
    rows, att_width = query_proj.shape
    model_width = frames_in.shape[1]
    heads = bucket_bias.shape[1]
    core = lax.axis_index("core")
    cores = lax.axis_size("core")
    count = lax.axis_size("chip") * cores
    device_index = lax.axis_index("chip") * cores + core
    meta = jnp.stack([device_index * rows, core]).astype(jnp.int32)

    def lin_shift(value, steps):
        leading, last = (max(0, -steps), min(count, count - steps))
        return lax.ppermute(value, ("chip", "core"), [(s, s + steps) for s in range(leading, last)])

    line_len = -(-bucket_table.shape[0] // LANES) * LANES
    table = jnp.pad(bucket_table, (0, line_len - bucket_table.shape[0])).reshape(1, line_len)
    bias_t = bucket_bias.T

    packed = jnp.stack([key_proj, value_proj])
    from_prev = lin_shift(packed, REACH)
    from_next = lin_shift(packed, -REACH)
    own_pair = lax.all_gather(packed, "core", tiled=True)
    sel = jnp.where(core == 0, from_next, from_prev)
    sel_pair = lax.all_gather(sel, "core", tiled=True)
    order = list(range(-REACH, REACH + 1))

    half = rows // 2
    vmem = pl.BlockSpec(memory_space=pltpu.VMEM)
    smem = pl.BlockSpec(memory_space=pltpu.SMEM)
    anywhere = pl.BlockSpec(memory_space=pl.ANY)
    window = len(order) * rows
    attn_flops = 2 * 2 * heads * rows * window * LANES + 2 * rows * att_width * model_width + 2 * rows * model_width * 2 * model_width
    attn_bytes = 2 * (rows * att_width * (1 + 2 * len(order)) + rows * model_width * 2 + att_width * model_width + model_width * 2 * model_width)
    mid, gated, cross_send, partner_send = pl.pallas_call(
        attention_kernel,
        out_shape=(
            jax.ShapeDtypeStruct((rows, model_width), jnp.bfloat16),
            jax.ShapeDtypeStruct((rows, model_width), jnp.bfloat16),
            jax.ShapeDtypeStruct((half, model_width), jnp.bfloat16),
            jax.ShapeDtypeStruct((half, model_width), jnp.bfloat16),
        ),
        in_specs=[smem, smem, vmem, vmem, vmem] + [anywhere] * 4 + [vmem, vmem, anywhere, anywhere],
        out_specs=(vmem, vmem, vmem, vmem),
        scratch_shapes=[
            pltpu.VMEM((att_width, model_width), jnp.bfloat16),
            pltpu.VMEM((model_width, 2 * model_width), jnp.bfloat16),
            pltpu.SemaphoreType.DMA((7,)),
            pltpu.VMEM((rows, att_width), jnp.bfloat16),
            pltpu.VMEM((len(order) * packed.shape[0], rows, att_width), jnp.bfloat16),
        ],
        cost_estimate=pl.CostEstimate(
            flops=attn_flops, transcendentals=heads * rows * window + rows * model_width, bytes_accessed=attn_bytes
        ),
        name="attention_glu",
    )(
        meta, utterance_lengths, table, bias_t, query_proj, from_prev, from_next, own_pair, sel_pair,
        frames_in, norm_gain.reshape(1, -1), out_weight, expand_weight,
    )

    chips = count // cores
    inward = [(2 * c + 1, 2 * c + 2) for c in range(chips - 1)] + [(2 * c, 2 * c - 1) for c in range(1, chips)]
    cross_recv = lax.ppermute(cross_send, ("chip", "core"), inward)
    partner_recv = lax.all_gather(partner_send, "core", tiled=True)
    conv_flops = 2 * KERNEL * rows * model_width + 2 * rows * model_width * model_width
    conv_bytes = 2 * (4 * half * model_width + rows * model_width * 2 + model_width * model_width) + 4 * KERNEL * model_width
    return pl.pallas_call(
        conv_kernel,
        out_shape=jax.ShapeDtypeStruct((rows, model_width), jnp.bfloat16),
        in_specs=[smem] + [vmem] * 6 + [anywhere],
        out_specs=vmem,
        scratch_shapes=[
            pltpu.VMEM((rows + 2 * half, model_width), jnp.float32),
            pltpu.VMEM((rows, model_width), jnp.float32),
            pltpu.VMEM((model_width, model_width), jnp.bfloat16),
            pltpu.SemaphoreType.DMA((1,)),
        ],
        cost_estimate=pl.CostEstimate(
            flops=conv_flops, transcendentals=rows * model_width, bytes_accessed=conv_bytes
        ),
        name="conv_shrink",
    )(meta, gated, cross_recv, partner_recv, depth_taps, inner_gain.reshape(1, -1), mid, shrink_weight)


def solution(mesh):
    groups, seq = mesh.devices.shape
    chip_mesh = jax.sharding.Mesh(mesh.devices.reshape(groups, seq // 2, 2), ("groups", "chip", "core"))
    rows_spec = P(("groups", "chip", "core"), None)
    placed = (
        rows_spec,
        rows_spec,
        rows_spec,
        rows_spec,
        P("groups"),
        P(),
        P(),
        P(),
        P(),
        P(),
        P(),
        P(),
        P(),
    )
    return jax.shard_map(
        on_device, mesh=chip_mesh, in_specs=placed, out_specs=rows_spec, check_vma=False
    )
```

```python
import jax
import jax.numpy as jnp
from jax import lax
from jax.experimental import pallas as pl
from jax.experimental.pallas import tpu as pltpu
from jax.sharding import PartitionSpec as P

KERNEL = 31
DILATION = 4
REACH = 2
LANES = 128

norm_epsilon = 1e-05
masked_score = -1e30


def shifted(value, axis, steps):
    count = lax.axis_size(axis)
    leading, last = (max(0, -steps), min(count, count - steps))
    return lax.ppermute(value, axis, [(source, source + steps) for source in range(leading, last)])


def layer_norm(values, gain_vec):
    row_mean = jnp.mean(values, axis=-1, keepdims=True)
    centred = values - row_mean
    spread = jnp.mean(centred * centred, axis=-1, keepdims=True)
    return centred * lax.rsqrt(spread + norm_epsilon) * gain_vec


def sigmoid(values):
    return 1.0 / (1.0 + jnp.exp(-values))


def attention_kernel(
    meta_ref, len_ref, table_ref, bias_t_ref, q_ref,
    prev_hbm, next_hbm, own_hbm, partner_hbm, sel_hbm,
    x_ref, gain_ref, ow_hbm, ew_hbm,
    mid_ref, gated_ref, cross_ref, partner_ref,
    ow_vmem, ew_vmem, sems, att_ref, win_ref,
):
    base = meta_ref[0]
    core = meta_ref[1]
    planes = prev_hbm.shape[0]
    copies = [
        pltpu.make_async_copy(prev_hbm, win_ref.at[pl.ds(0, planes)], sems.at[2]),
        pltpu.make_async_copy(own_hbm, win_ref.at[pl.ds(2 * planes, planes)], sems.at[3]),
        pltpu.make_async_copy(next_hbm, win_ref.at[pl.ds(4 * planes, planes)], sems.at[4]),
        pltpu.make_async_copy(
            sel_hbm, win_ref.at[pl.ds(pl.multiple_of((1 + 2 * core) * planes, planes), planes)], sems.at[5]
        ),
        pltpu.make_async_copy(
            partner_hbm, win_ref.at[pl.ds(pl.multiple_of((3 - 2 * core) * planes, planes), planes)], sems.at[6]
        ),
    ]
    for copy in copies:
        copy.start()
    ow_copy = pltpu.make_async_copy(ow_hbm, ow_vmem, sems.at[0])
    ew_copy = pltpu.make_async_copy(ew_hbm, ew_vmem, sems.at[1])
    ow_copy.start()
    ew_copy.start()
    blocks = win_ref.shape[0] // planes
    rows, att_width = q_ref.shape
    heads = bias_t_ref.shape[0]
    buckets = bias_t_ref.shape[1]
    head_width = att_width // heads
    width = blocks * rows
    line_len = table_ref.shape[1]

    qpos = base + lax.broadcasted_iota(jnp.int32, (rows, 1), 0)
    kpos = base - REACH * rows + lax.broadcasted_iota(jnp.int32, (1, width), 1)

    def seg_step(u, carry):
        run, qs, ks = carry
        run = run + len_ref[u]
        return run, qs + (qpos >= run).astype(jnp.int32), ks + (kpos >= run).astype(jnp.int32)

    _, qseg, kseg = lax.fori_loop(
        0, len_ref.shape[0], seg_step,
        (jnp.int32(0), jnp.zeros((rows, 1), jnp.int32), jnp.zeros((1, width), jnp.int32)),
    )
    kseg = jnp.where(kpos < 0, -1, kseg)
    same = qseg == kseg

    table = table_ref[...]
    bias_t = bias_t_ref[...]
    line = jnp.zeros((heads, line_len), jnp.float32)
    for b in range(buckets):
        line = jnp.where(table == b, bias_t[:, b:b + 1], line)

    for copy in copies:
        copy.wait()
    scaling = head_width ** (-0.5)
    lane = lax.broadcasted_iota(jnp.int32, (rows, LANES), 1)
    per_pair = LANES // head_width
    for pair in range(att_width // LANES):
        cols = slice(pair * LANES, (pair + 1) * LANES)
        q_pair = q_ref[:, cols]
        k_pair = jnp.concatenate([win_ref[planes * j, :, cols] for j in range(blocks)], axis=0)
        v_pair = jnp.concatenate([win_ref[planes * j + 1, :, cols] for j in range(blocks)], axis=0)
        result = None
        for sub in range(per_pair):
            head = pair * per_pair + sub
            in_head = (lane >= sub * head_width) & (lane < (sub + 1) * head_width)
            q_head = jnp.where(in_head, q_pair, jnp.zeros_like(q_pair))
            spread = jnp.broadcast_to(line[head:head + 1, :], (rows, line_len))
            skew = pltpu.roll(spread, line_len - rows + 1, 1, stride=1, stride_axis=0)[:, :width]
            bias = jnp.where(same, skew, masked_score)
            scores = lax.dot_general(
                q_head, k_pair, (((1,), (1,)), ((), ())), preferred_element_type=jnp.float32
            )
            scores = scores * scaling + bias
            top = jnp.max(scores, axis=1, keepdims=True)
            weights = jnp.exp(scores - top)
            total = jnp.sum(weights, axis=1, keepdims=True)
            summed = jnp.dot(weights.astype(jnp.bfloat16), v_pair, preferred_element_type=jnp.float32)
            part = summed / total
            result = part if result is None else jnp.where(in_head, part, result)
        att_ref[:, cols] = result.astype(jnp.bfloat16)

    ow_copy.wait()
    projected = jnp.dot(att_ref[...], ow_vmem[...], preferred_element_type=jnp.float32)
    mid = (x_ref[...].astype(jnp.float32) + projected).astype(jnp.bfloat16)
    mid_ref[...] = mid
    normed = layer_norm(mid.astype(jnp.float32), gain_ref[...]).astype(jnp.bfloat16)
    model_width = mid.shape[1]
    ew_copy.wait()
    value_half = jnp.dot(normed, ew_vmem[:, :model_width], preferred_element_type=jnp.float32)
    gate_half = jnp.dot(normed, ew_vmem[:, model_width:], preferred_element_type=jnp.float32)
    gated = (value_half * sigmoid(gate_half)).astype(jnp.bfloat16)
    gated_ref[...] = gated
    half = cross_ref.shape[0]
    cross_ref[...] = gated_ref[pl.ds(pl.multiple_of(core * half, half), half), :]
    partner_ref[...] = gated_ref[pl.ds(pl.multiple_of((1 - core) * half, half), half), :]


def conv_kernel(
    meta_ref, gated_ref, cross_ref, pairg_ref, taps_ref, gain_ref, mid_ref, sw_hbm,
    out_ref, win_ref, conv_ref, sw_vmem, sems,
):
    sw_copy = pltpu.make_async_copy(sw_hbm, sw_vmem, sems.at[0])
    sw_copy.start()
    half = cross_ref.shape[0]
    rows, model_width = mid_ref.shape
    first_core = meta_ref[1] == 0
    cross = cross_ref[...]
    partner = pairg_ref[...]
    win_ref[0:half, :] = jnp.where(first_core, cross, partner).astype(jnp.float32)
    win_ref[half:half + rows, :] = gated_ref[...].astype(jnp.float32)
    win_ref[half + rows:2 * half + rows, :] = jnp.where(first_core, partner, cross).astype(jnp.float32)
    reach = DILATION * (KERNEL - 1) // 2
    start = half - reach

    def chunk(c, carry):
        lanes = pl.ds(pl.multiple_of(c * LANES, LANES), LANES)
        acc = jnp.zeros((rows, LANES), jnp.float32)
        for tap in range(KERNEL):
            first = start + DILATION * tap
            acc = acc + taps_ref[tap:tap + 1, lanes] * win_ref[first:first + rows, lanes]
        conv_ref[:, lanes] = acc
        return carry

    lax.fori_loop(0, model_width // LANES, chunk, 0)
    inner = layer_norm(conv_ref[...], gain_ref[...])
    activated = (inner * sigmoid(inner)).astype(jnp.bfloat16)
    sw_copy.wait()
    shrunk = jnp.dot(activated, sw_vmem[...], preferred_element_type=jnp.float32)
    out_ref[...] = (mid_ref[...].astype(jnp.float32) + shrunk).astype(out_ref.dtype)


def on_device(
    frames_in,
    query_proj,
    key_proj,
    value_proj,
    utterance_lengths,
    bucket_table,
    bucket_bias,
    out_weight,
    norm_gain,
    expand_weight,
    depth_taps,
    inner_gain,
    shrink_weight,
):
    rows, att_width = query_proj.shape
    model_width = frames_in.shape[1]
    heads = bucket_bias.shape[1]
    core = lax.axis_index("core")
    cores = lax.axis_size("core")
    count = lax.axis_size("chip") * cores
    device_index = lax.axis_index("chip") * cores + core
    meta = jnp.stack([device_index * rows, core]).astype(jnp.int32)

    def lin_shift(value, steps):
        leading, last = (max(0, -steps), min(count, count - steps))
        return lax.ppermute(value, ("chip", "core"), [(s, s + steps) for s in range(leading, last)])

    line_len = -(-bucket_table.shape[0] // LANES) * LANES
    table = jnp.pad(bucket_table, (0, line_len - bucket_table.shape[0])).reshape(1, line_len)
    bias_t = bucket_bias.T

    packed = jnp.stack([key_proj, value_proj])
    from_prev = lin_shift(packed, REACH)
    from_next = lin_shift(packed, -REACH)
    swap = [(0, 1), (1, 0)]
    partner = lax.ppermute(packed, "core", swap)
    sel = jnp.where(core == 0, from_next, from_prev)
    partner_sel = lax.ppermute(sel, "core", swap)
    order = list(range(-REACH, REACH + 1))

    half = rows // 2
    vmem = pl.BlockSpec(memory_space=pltpu.VMEM)
    smem = pl.BlockSpec(memory_space=pltpu.SMEM)
    anywhere = pl.BlockSpec(memory_space=pl.ANY)
    window = len(order) * rows
    attn_flops = 2 * 2 * heads * rows * window * LANES + 2 * rows * att_width * model_width + 2 * rows * model_width * 2 * model_width
    attn_bytes = 2 * (rows * att_width * (1 + 2 * len(order)) + rows * model_width * 2 + att_width * model_width + model_width * 2 * model_width)
    mid, gated, cross_send, partner_send = pl.pallas_call(
        attention_kernel,
        out_shape=(
            jax.ShapeDtypeStruct((rows, model_width), jnp.bfloat16),
            jax.ShapeDtypeStruct((rows, model_width), jnp.bfloat16),
            jax.ShapeDtypeStruct((half, model_width), jnp.bfloat16),
            jax.ShapeDtypeStruct((half, model_width), jnp.bfloat16),
        ),
        in_specs=[smem, smem, vmem, vmem, vmem] + [anywhere] * 5 + [vmem, vmem, anywhere, anywhere],
        out_specs=(vmem, vmem, vmem, vmem),
        scratch_shapes=[
            pltpu.VMEM((att_width, model_width), jnp.bfloat16),
            pltpu.VMEM((model_width, 2 * model_width), jnp.bfloat16),
            pltpu.SemaphoreType.DMA((7,)),
            pltpu.VMEM((rows, att_width), jnp.bfloat16),
            pltpu.VMEM((len(order) * packed.shape[0], rows, att_width), jnp.bfloat16),
        ],
        cost_estimate=pl.CostEstimate(
            flops=attn_flops, transcendentals=heads * rows * window + rows * model_width, bytes_accessed=attn_bytes
        ),
        name="attention_glu",
    )(
        meta, utterance_lengths, table, bias_t, query_proj, from_prev, from_next, packed, partner, partner_sel,
        frames_in, norm_gain.reshape(1, -1), out_weight, expand_weight,
    )

    chips = count // cores
    inward = [(2 * c + 1, 2 * c + 2) for c in range(chips - 1)] + [(2 * c, 2 * c - 1) for c in range(1, chips)]
    cross_recv = lax.ppermute(cross_send, ("chip", "core"), inward)
    partner_recv = lax.ppermute(partner_send, "core", swap)
    conv_flops = 2 * KERNEL * rows * model_width + 2 * rows * model_width * model_width
    conv_bytes = 2 * (4 * half * model_width + rows * model_width * 2 + model_width * model_width) + 4 * KERNEL * model_width
    return pl.pallas_call(
        conv_kernel,
        out_shape=jax.ShapeDtypeStruct((rows, model_width), jnp.bfloat16),
        in_specs=[smem] + [vmem] * 6 + [anywhere],
        out_specs=vmem,
        scratch_shapes=[
            pltpu.VMEM((rows + 2 * half, model_width), jnp.float32),
            pltpu.VMEM((rows, model_width), jnp.float32),
            pltpu.VMEM((model_width, model_width), jnp.bfloat16),
            pltpu.SemaphoreType.DMA((1,)),
        ],
        cost_estimate=pl.CostEstimate(
            flops=conv_flops, transcendentals=rows * model_width, bytes_accessed=conv_bytes
        ),
        name="conv_shrink",
    )(meta, gated, cross_recv, partner_recv, depth_taps, inner_gain.reshape(1, -1), mid, shrink_weight)


def solution(mesh):
    groups, seq = mesh.devices.shape
    chip_mesh = jax.sharding.Mesh(mesh.devices.reshape(groups, seq // 2, 2), ("groups", "chip", "core"))
    rows_spec = P(("groups", "chip", "core"), None)
    placed = (
        rows_spec,
        rows_spec,
        rows_spec,
        rows_spec,
        P("groups"),
        P(),
        P(),
        P(),
        P(),
        P(),
        P(),
        P(),
        P(),
    )
    return jax.shard_map(
        on_device, mesh=chip_mesh, in_specs=placed, out_specs=rows_spec, check_vma=False
    )
```

```python
import jax
import jax.numpy as jnp
from jax import lax
from jax.experimental import pallas as pl
from jax.experimental.pallas import tpu as pltpu
from jax.sharding import PartitionSpec as P

KERNEL = 31
DILATION = 4
REACH = 2
LANES = 128

norm_epsilon = 1e-05
masked_score = -1e30


def shifted(value, axis, steps):
    count = lax.axis_size(axis)
    leading, last = (max(0, -steps), min(count, count - steps))
    return lax.ppermute(value, axis, [(source, source + steps) for source in range(leading, last)])


def layer_norm(values, gain_vec):
    row_mean = jnp.mean(values, axis=-1, keepdims=True)
    centred = values - row_mean
    spread = jnp.mean(centred * centred, axis=-1, keepdims=True)
    return centred * lax.rsqrt(spread + norm_epsilon) * gain_vec


def sigmoid(values):
    return 1.0 / (1.0 + jnp.exp(-values))


def attention_kernel(
    meta_ref, len_ref, table_ref, bias_t_ref, q_hbm,
    prev_hbm, next_hbm, own_hbm, partner_hbm, sel_hbm,
    x_hbm, gain_ref, ow_hbm, ew_hbm,
    mid_ref, gated_ref, cross_ref, partner_ref,
    ow_vmem, ew_vmem, sems, att_ref, win_ref, q_ref, x_ref,
):
    q_copy = pltpu.make_async_copy(q_hbm, q_ref, sems.at[7])
    q_copy.start()
    base = meta_ref[0]
    core = meta_ref[1]
    planes = prev_hbm.shape[0]
    copies = [
        pltpu.make_async_copy(prev_hbm, win_ref.at[pl.ds(0, planes)], sems.at[2]),
        pltpu.make_async_copy(own_hbm, win_ref.at[pl.ds(2 * planes, planes)], sems.at[3]),
        pltpu.make_async_copy(next_hbm, win_ref.at[pl.ds(4 * planes, planes)], sems.at[4]),
        pltpu.make_async_copy(
            sel_hbm, win_ref.at[pl.ds(pl.multiple_of((1 + 2 * core) * planes, planes), planes)], sems.at[5]
        ),
        pltpu.make_async_copy(
            partner_hbm, win_ref.at[pl.ds(pl.multiple_of((3 - 2 * core) * planes, planes), planes)], sems.at[6]
        ),
    ]
    for copy in copies:
        copy.start()
    ow_copy = pltpu.make_async_copy(ow_hbm, ow_vmem, sems.at[0])
    ew_copy = pltpu.make_async_copy(ew_hbm, ew_vmem, sems.at[1])
    x_copy = pltpu.make_async_copy(x_hbm, x_ref, sems.at[8])
    ow_copy.start()
    x_copy.start()
    ew_copy.start()
    blocks = win_ref.shape[0] // planes
    rows, att_width = q_ref.shape
    heads = bias_t_ref.shape[0]
    buckets = bias_t_ref.shape[1]
    head_width = att_width // heads
    width = blocks * rows
    line_len = table_ref.shape[1]

    qpos = base + lax.broadcasted_iota(jnp.int32, (rows, 1), 0)
    kpos = base - REACH * rows + lax.broadcasted_iota(jnp.int32, (1, width), 1)

    def seg_step(u, carry):
        run, qs, ks = carry
        run = run + len_ref[u]
        return run, qs + (qpos >= run).astype(jnp.int32), ks + (kpos >= run).astype(jnp.int32)

    _, qseg, kseg = lax.fori_loop(
        0, len_ref.shape[0], seg_step,
        (jnp.int32(0), jnp.zeros((rows, 1), jnp.int32), jnp.zeros((1, width), jnp.int32)),
    )
    kseg = jnp.where(kpos < 0, -1, kseg)
    same = qseg == kseg

    table = table_ref[...]
    bias_t = bias_t_ref[...]
    line = jnp.zeros((heads, line_len), jnp.float32)
    for b in range(buckets):
        line = jnp.where(table == b, bias_t[:, b:b + 1], line)

    for copy in copies:
        copy.wait()
    q_copy.wait()
    scaling = head_width ** (-0.5)
    lane = lax.broadcasted_iota(jnp.int32, (rows, LANES), 1)
    per_pair = LANES // head_width
    for pair in range(att_width // LANES):
        cols = slice(pair * LANES, (pair + 1) * LANES)
        q_pair = q_ref[:, cols]
        k_pair = jnp.concatenate([win_ref[planes * j, :, cols] for j in range(blocks)], axis=0)
        v_pair = jnp.concatenate([win_ref[planes * j + 1, :, cols] for j in range(blocks)], axis=0)
        result = None
        for sub in range(per_pair):
            head = pair * per_pair + sub
            in_head = (lane >= sub * head_width) & (lane < (sub + 1) * head_width)
            q_head = jnp.where(in_head, q_pair, jnp.zeros_like(q_pair))
            spread = jnp.broadcast_to(line[head:head + 1, :], (rows, line_len))
            skew = pltpu.roll(spread, line_len - rows + 1, 1, stride=1, stride_axis=0)[:, :width]
            bias = jnp.where(same, skew, masked_score)
            scores = lax.dot_general(
                q_head, k_pair, (((1,), (1,)), ((), ())), preferred_element_type=jnp.float32
            )
            scores = scores * scaling + bias
            top = jnp.max(scores, axis=1, keepdims=True)
            weights = jnp.exp(scores - top)
            total = jnp.sum(weights, axis=1, keepdims=True)
            summed = jnp.dot(weights.astype(jnp.bfloat16), v_pair, preferred_element_type=jnp.float32)
            part = summed / total
            result = part if result is None else jnp.where(in_head, part, result)
        att_ref[:, cols] = result.astype(jnp.bfloat16)

    ow_copy.wait()
    x_copy.wait()
    projected = jnp.dot(att_ref[...], ow_vmem[...], preferred_element_type=jnp.float32)
    mid = (x_ref[...].astype(jnp.float32) + projected).astype(jnp.bfloat16)
    mid_ref[...] = mid
    normed = layer_norm(mid.astype(jnp.float32), gain_ref[...]).astype(jnp.bfloat16)
    model_width = mid.shape[1]
    ew_copy.wait()
    value_half = jnp.dot(normed, ew_vmem[:, :model_width], preferred_element_type=jnp.float32)
    gate_half = jnp.dot(normed, ew_vmem[:, model_width:], preferred_element_type=jnp.float32)
    gated = (value_half * sigmoid(gate_half)).astype(jnp.bfloat16)
    gated_ref[...] = gated
    half = cross_ref.shape[0]
    cross_ref[...] = gated_ref[pl.ds(pl.multiple_of(core * half, half), half), :]
    partner_ref[...] = gated_ref[pl.ds(pl.multiple_of((1 - core) * half, half), half), :]


def conv_kernel(
    meta_ref, gated_hbm, cross_hbm, pairg_hbm, taps_ref, gain_ref, mid_hbm, sw_hbm,
    out_ref, win_ref, conv_ref, sw_vmem, sems, gated_ref, cross_ref, pairg_ref, mid_ref,
):
    loads = [
        pltpu.make_async_copy(gated_hbm, gated_ref, sems.at[1]),
        pltpu.make_async_copy(cross_hbm, cross_ref, sems.at[2]),
        pltpu.make_async_copy(pairg_hbm, pairg_ref, sems.at[3]),
    ]
    for load in loads:
        load.start()
    sw_copy = pltpu.make_async_copy(sw_hbm, sw_vmem, sems.at[0])
    mid_copy = pltpu.make_async_copy(mid_hbm, mid_ref, sems.at[4])
    sw_copy.start()
    mid_copy.start()
    for load in loads:
        load.wait()
    half = cross_ref.shape[0]
    rows, model_width = mid_ref.shape
    first_core = meta_ref[1] == 0
    cross = cross_ref[...]
    partner = pairg_ref[...]
    win_ref[0:half, :] = jnp.where(first_core, cross, partner).astype(jnp.float32)
    win_ref[half:half + rows, :] = gated_ref[...].astype(jnp.float32)
    win_ref[half + rows:2 * half + rows, :] = jnp.where(first_core, partner, cross).astype(jnp.float32)
    reach = DILATION * (KERNEL - 1) // 2
    start = half - reach

    def chunk(c, carry):
        lanes = pl.ds(pl.multiple_of(c * LANES, LANES), LANES)
        acc = jnp.zeros((rows, LANES), jnp.float32)
        for tap in range(KERNEL):
            first = start + DILATION * tap
            acc = acc + taps_ref[tap:tap + 1, lanes] * win_ref[first:first + rows, lanes]
        conv_ref[:, lanes] = acc
        return carry

    lax.fori_loop(0, model_width // LANES, chunk, 0)
    inner = layer_norm(conv_ref[...], gain_ref[...])
    activated = (inner * sigmoid(inner)).astype(jnp.bfloat16)
    sw_copy.wait()
    mid_copy.wait()
    shrunk = jnp.dot(activated, sw_vmem[...], preferred_element_type=jnp.float32)
    out_ref[...] = (mid_ref[...].astype(jnp.float32) + shrunk).astype(out_ref.dtype)


def on_device(
    frames_in,
    query_proj,
    key_proj,
    value_proj,
    utterance_lengths,
    bucket_table,
    bucket_bias,
    out_weight,
    norm_gain,
    expand_weight,
    depth_taps,
    inner_gain,
    shrink_weight,
):
    rows, att_width = query_proj.shape
    model_width = frames_in.shape[1]
    heads = bucket_bias.shape[1]
    core = lax.axis_index("core")
    cores = lax.axis_size("core")
    count = lax.axis_size("chip") * cores
    device_index = lax.axis_index("chip") * cores + core
    meta = jnp.stack([device_index * rows, core]).astype(jnp.int32)

    def lin_shift(value, steps):
        leading, last = (max(0, -steps), min(count, count - steps))
        return lax.ppermute(value, ("chip", "core"), [(s, s + steps) for s in range(leading, last)])

    line_len = -(-bucket_table.shape[0] // LANES) * LANES
    table = jnp.pad(bucket_table, (0, line_len - bucket_table.shape[0])).reshape(1, line_len)
    bias_t = bucket_bias.T

    packed = jnp.stack([key_proj, value_proj])
    from_prev = lin_shift(packed, REACH)
    from_next = lin_shift(packed, -REACH)
    swap = [(0, 1), (1, 0)]
    partner = lax.ppermute(packed, "core", swap)
    sel = jnp.where(core == 0, from_next, from_prev)
    partner_sel = lax.ppermute(sel, "core", swap)
    order = list(range(-REACH, REACH + 1))

    half = rows // 2
    vmem = pl.BlockSpec(memory_space=pltpu.VMEM)
    smem = pl.BlockSpec(memory_space=pltpu.SMEM)
    anywhere = pl.BlockSpec(memory_space=pl.ANY)
    window = len(order) * rows
    attn_flops = 2 * 2 * heads * rows * window * LANES + 2 * rows * att_width * model_width + 2 * rows * model_width * 2 * model_width
    attn_bytes = 2 * (rows * att_width * (1 + 2 * len(order)) + rows * model_width * 2 + att_width * model_width + model_width * 2 * model_width)
    mid, gated, cross_send, partner_send = pl.pallas_call(
        attention_kernel,
        out_shape=(
            jax.ShapeDtypeStruct((rows, model_width), jnp.bfloat16),
            jax.ShapeDtypeStruct((rows, model_width), jnp.bfloat16),
            jax.ShapeDtypeStruct((half, model_width), jnp.bfloat16),
            jax.ShapeDtypeStruct((half, model_width), jnp.bfloat16),
        ),
        in_specs=[smem, smem, vmem, vmem, anywhere] + [anywhere] * 5 + [anywhere, vmem, anywhere, anywhere],
        out_specs=(vmem, vmem, vmem, vmem),
        scratch_shapes=[
            pltpu.VMEM((att_width, model_width), jnp.bfloat16),
            pltpu.VMEM((model_width, 2 * model_width), jnp.bfloat16),
            pltpu.SemaphoreType.DMA((9,)),
            pltpu.VMEM((rows, att_width), jnp.bfloat16),
            pltpu.VMEM((len(order) * packed.shape[0], rows, att_width), jnp.bfloat16),
            pltpu.VMEM((rows, att_width), jnp.bfloat16),
            pltpu.VMEM((rows, model_width), jnp.bfloat16),
        ],
        cost_estimate=pl.CostEstimate(
            flops=attn_flops, transcendentals=heads * rows * window + rows * model_width, bytes_accessed=attn_bytes
        ),
        name="attention_glu",
    )(
        meta, utterance_lengths, table, bias_t, query_proj, from_prev, from_next, packed, partner, partner_sel,
        frames_in, norm_gain.reshape(1, -1), out_weight, expand_weight,
    )

    chips = count // cores
    inward = [(2 * c + 1, 2 * c + 2) for c in range(chips - 1)] + [(2 * c, 2 * c - 1) for c in range(1, chips)]
    cross_recv = lax.ppermute(cross_send, ("chip", "core"), inward)
    partner_recv = lax.ppermute(partner_send, "core", swap)
    conv_flops = 2 * KERNEL * rows * model_width + 2 * rows * model_width * model_width
    conv_bytes = 2 * (4 * half * model_width + rows * model_width * 2 + model_width * model_width) + 4 * KERNEL * model_width
    return pl.pallas_call(
        conv_kernel,
        out_shape=jax.ShapeDtypeStruct((rows, model_width), jnp.bfloat16),
        in_specs=[smem, anywhere, anywhere, anywhere, vmem, vmem, anywhere, anywhere],
        out_specs=vmem,
        scratch_shapes=[
            pltpu.VMEM((rows + 2 * half, model_width), jnp.float32),
            pltpu.VMEM((rows, model_width), jnp.float32),
            pltpu.VMEM((model_width, model_width), jnp.bfloat16),
            pltpu.SemaphoreType.DMA((5,)),
            pltpu.VMEM((rows, model_width), jnp.bfloat16),
            pltpu.VMEM((half, model_width), jnp.bfloat16),
            pltpu.VMEM((half, model_width), jnp.bfloat16),
            pltpu.VMEM((rows, model_width), jnp.bfloat16),
        ],
        cost_estimate=pl.CostEstimate(
            flops=conv_flops, transcendentals=rows * model_width, bytes_accessed=conv_bytes
        ),
        name="conv_shrink",
    )(meta, gated, cross_recv, partner_recv, depth_taps, inner_gain.reshape(1, -1), mid, shrink_weight)


def solution(mesh):
    groups, seq = mesh.devices.shape
    chip_mesh = jax.sharding.Mesh(mesh.devices.reshape(groups, seq // 2, 2), ("groups", "chip", "core"))
    rows_spec = P(("groups", "chip", "core"), None)
    placed = (
        rows_spec,
        rows_spec,
        rows_spec,
        rows_spec,
        P("groups"),
        P(),
        P(),
        P(),
        P(),
        P(),
        P(),
        P(),
        P(),
    )
    return jax.shard_map(
        on_device, mesh=chip_mesh, in_specs=placed, out_specs=rows_spec, check_vma=False
    )
```

```python
import jax
import jax.numpy as jnp
from jax import lax
from jax.experimental import pallas as pl
from jax.experimental.pallas import tpu as pltpu
from jax.sharding import PartitionSpec as P

KERNEL = 31
DILATION = 4
REACH = 2
LANES = 128

norm_epsilon = 1e-05
masked_score = -1e30


def shifted(value, axis, steps):
    count = lax.axis_size(axis)
    leading, last = (max(0, -steps), min(count, count - steps))
    return lax.ppermute(value, axis, [(source, source + steps) for source in range(leading, last)])


def layer_norm(values, gain_vec):
    row_mean = jnp.mean(values, axis=-1, keepdims=True)
    centred = values - row_mean
    spread = jnp.mean(centred * centred, axis=-1, keepdims=True)
    return centred * lax.rsqrt(spread + norm_epsilon) * gain_vec


def sigmoid(values):
    return 1.0 / (1.0 + jnp.exp(-values))


def attention_kernel(
    meta_ref, len_ref, table_ref, bias_t_ref, q_ref,
    prev_hbm, next_hbm, own_hbm, partner_hbm, sel_hbm,
    x_ref, gain_ref, ow_hbm, ew_hbm,
    mid_ref, gated_ref, cross_ref, partner_ref,
    ow_vmem, ew_vmem, sems, att_ref, win_ref,
):
    ow_copy = pltpu.make_async_copy(ow_hbm, ow_vmem, sems.at[0])
    ew_copy = pltpu.make_async_copy(ew_hbm, ew_vmem, sems.at[1])
    ow_copy.start()
    ew_copy.start()
    base = meta_ref[0]
    core = meta_ref[1]
    planes = prev_hbm.shape[0]
    copies = [
        pltpu.make_async_copy(prev_hbm, win_ref.at[pl.ds(0, planes)], sems.at[2]),
        pltpu.make_async_copy(own_hbm, win_ref.at[pl.ds(2 * planes, planes)], sems.at[3]),
        pltpu.make_async_copy(next_hbm, win_ref.at[pl.ds(4 * planes, planes)], sems.at[4]),
        pltpu.make_async_copy(
            sel_hbm, win_ref.at[pl.ds(pl.multiple_of((1 + 2 * core) * planes, planes), planes)], sems.at[5]
        ),
        pltpu.make_async_copy(
            partner_hbm, win_ref.at[pl.ds(pl.multiple_of((3 - 2 * core) * planes, planes), planes)], sems.at[6]
        ),
    ]
    for copy in copies:
        copy.start()
    blocks = win_ref.shape[0] // planes
    rows, att_width = q_ref.shape
    heads = bias_t_ref.shape[0]
    buckets = bias_t_ref.shape[1]
    head_width = att_width // heads
    width = blocks * rows
    line_len = table_ref.shape[1]

    qpos = base + lax.broadcasted_iota(jnp.int32, (rows, 1), 0)
    kpos = base - REACH * rows + lax.broadcasted_iota(jnp.int32, (1, width), 1)

    def seg_step(u, carry):
        run, qs, ks = carry
        run = run + len_ref[u]
        return run, qs + (qpos >= run).astype(jnp.int32), ks + (kpos >= run).astype(jnp.int32)

    _, qseg, kseg = lax.fori_loop(
        0, len_ref.shape[0], seg_step,
        (jnp.int32(0), jnp.zeros((rows, 1), jnp.int32), jnp.zeros((1, width), jnp.int32)),
    )
    kseg = jnp.where(kpos < 0, -1, kseg)
    same = qseg == kseg

    table = table_ref[...]
    bias_t = bias_t_ref[...]
    line = jnp.zeros((heads, line_len), jnp.float32)
    for b in range(buckets):
        line = jnp.where(table == b, bias_t[:, b:b + 1], line)

    for copy in copies:
        copy.wait()
    scaling = head_width ** (-0.5)
    lane = lax.broadcasted_iota(jnp.int32, (rows, LANES), 1)
    per_pair = LANES // head_width
    for pair in range(att_width // LANES):
        cols = slice(pair * LANES, (pair + 1) * LANES)
        q_pair = q_ref[:, cols]
        k_pair = jnp.concatenate([win_ref[planes * j, :, cols] for j in range(blocks)], axis=0)
        v_pair = jnp.concatenate([win_ref[planes * j + 1, :, cols] for j in range(blocks)], axis=0)
        result = None
        for sub in range(per_pair):
            head = pair * per_pair + sub
            in_head = (lane >= sub * head_width) & (lane < (sub + 1) * head_width)
            q_head = jnp.where(in_head, q_pair, jnp.zeros_like(q_pair))
            spread = jnp.broadcast_to(line[head:head + 1, :], (rows, line_len))
            skew = pltpu.roll(spread, line_len - rows + 1, 1, stride=1, stride_axis=0)[:, :width]
            bias = jnp.where(same, skew, masked_score)
            scores = lax.dot_general(
                q_head, k_pair, (((1,), (1,)), ((), ())), preferred_element_type=jnp.float32
            )
            scores = scores * scaling + bias
            top = jnp.max(scores, axis=1, keepdims=True)
            weights = jnp.exp(scores - top)
            total = jnp.sum(weights, axis=1, keepdims=True)
            summed = jnp.dot(weights.astype(jnp.bfloat16), v_pair, preferred_element_type=jnp.float32)
            part = summed / total
            result = part if result is None else jnp.where(in_head, part, result)
        att_ref[:, cols] = result.astype(jnp.bfloat16)

    ow_copy.wait()
    projected = jnp.dot(att_ref[...], ow_vmem[...], preferred_element_type=jnp.float32)
    mid = (x_ref[...].astype(jnp.float32) + projected).astype(jnp.bfloat16)
    mid_ref[...] = mid
    normed = layer_norm(mid.astype(jnp.float32), gain_ref[...]).astype(jnp.bfloat16)
    model_width = mid.shape[1]
    ew_copy.wait()
    value_half = jnp.dot(normed, ew_vmem[:, :model_width], preferred_element_type=jnp.float32)
    gate_half = jnp.dot(normed, ew_vmem[:, model_width:], preferred_element_type=jnp.float32)
    gated = (value_half * sigmoid(gate_half)).astype(jnp.bfloat16)
    gated_ref[...] = gated
    half = cross_ref.shape[0]
    cross_ref[...] = gated_ref[pl.ds(pl.multiple_of(core * half, half), half), :]
    partner_ref[...] = gated_ref[pl.ds(pl.multiple_of((1 - core) * half, half), half), :]


def conv_kernel(
    meta_ref, gated_ref, cross_ref, pairg_ref, taps_ref, gain_ref, mid_ref, sw_vmem,
    out_ref, win_ref, conv_ref,
):
    half = cross_ref.shape[0]
    rows, model_width = mid_ref.shape
    first_core = meta_ref[1] == 0
    cross = cross_ref[...]
    partner = pairg_ref[...]
    win_ref[0:half, :] = jnp.where(first_core, cross, partner).astype(jnp.float32)
    win_ref[half:half + rows, :] = gated_ref[...].astype(jnp.float32)
    win_ref[half + rows:2 * half + rows, :] = jnp.where(first_core, partner, cross).astype(jnp.float32)
    reach = DILATION * (KERNEL - 1) // 2
    start = half - reach

    def chunk(c, carry):
        lanes = pl.ds(pl.multiple_of(c * LANES, LANES), LANES)
        acc = jnp.zeros((rows, LANES), jnp.float32)
        for tap in range(KERNEL):
            first = start + DILATION * tap
            acc = acc + taps_ref[tap:tap + 1, lanes] * win_ref[first:first + rows, lanes]
        conv_ref[:, lanes] = acc
        return carry

    lax.fori_loop(0, model_width // LANES, chunk, 0)
    inner = layer_norm(conv_ref[...], gain_ref[...])
    activated = (inner * sigmoid(inner)).astype(jnp.bfloat16)
    shrunk = jnp.dot(activated, sw_vmem[...], preferred_element_type=jnp.float32)
    out_ref[...] = (mid_ref[...].astype(jnp.float32) + shrunk).astype(out_ref.dtype)


def on_device(
    frames_in,
    query_proj,
    key_proj,
    value_proj,
    utterance_lengths,
    bucket_table,
    bucket_bias,
    out_weight,
    norm_gain,
    expand_weight,
    depth_taps,
    inner_gain,
    shrink_weight,
):
    rows, att_width = query_proj.shape
    model_width = frames_in.shape[1]
    heads = bucket_bias.shape[1]
    core = lax.axis_index("core")
    cores = lax.axis_size("core")
    count = lax.axis_size("chip") * cores
    device_index = lax.axis_index("chip") * cores + core
    meta = jnp.stack([device_index * rows, core]).astype(jnp.int32)

    def lin_shift(value, steps):
        leading, last = (max(0, -steps), min(count, count - steps))
        return lax.ppermute(value, ("chip", "core"), [(s, s + steps) for s in range(leading, last)])

    line_len = -(-bucket_table.shape[0] // LANES) * LANES
    table = jnp.pad(bucket_table, (0, line_len - bucket_table.shape[0])).reshape(1, line_len)
    bias_t = bucket_bias.T

    packed = jnp.stack([key_proj, value_proj])
    from_prev = lin_shift(packed, REACH)
    from_next = lin_shift(packed, -REACH)
    swap = [(0, 1), (1, 0)]
    partner = lax.ppermute(packed, "core", swap)
    sel = jnp.where(core == 0, from_next, from_prev)
    partner_sel = lax.ppermute(sel, "core", swap)
    order = list(range(-REACH, REACH + 1))

    half = rows // 2
    vmem = pl.BlockSpec(memory_space=pltpu.VMEM)
    smem = pl.BlockSpec(memory_space=pltpu.SMEM)
    anywhere = pl.BlockSpec(memory_space=pl.ANY)
    window = len(order) * rows
    attn_flops = 2 * 2 * heads * rows * window * LANES + 2 * rows * att_width * model_width + 2 * rows * model_width * 2 * model_width
    attn_bytes = 2 * (rows * att_width * (1 + 2 * len(order)) + rows * model_width * 2 + att_width * model_width + model_width * 2 * model_width)
    mid, gated, cross_send, partner_send = pl.pallas_call(
        attention_kernel,
        out_shape=(
            jax.ShapeDtypeStruct((rows, model_width), jnp.bfloat16),
            jax.ShapeDtypeStruct((rows, model_width), jnp.bfloat16),
            jax.ShapeDtypeStruct((half, model_width), jnp.bfloat16),
            jax.ShapeDtypeStruct((half, model_width), jnp.bfloat16),
        ),
        in_specs=[smem, smem, vmem, vmem, vmem] + [anywhere] * 5 + [vmem, vmem, anywhere, anywhere],
        out_specs=(vmem, vmem, vmem, vmem),
        scratch_shapes=[
            pltpu.VMEM((att_width, model_width), jnp.bfloat16),
            pltpu.VMEM((model_width, 2 * model_width), jnp.bfloat16),
            pltpu.SemaphoreType.DMA((7,)),
            pltpu.VMEM((rows, att_width), jnp.bfloat16),
            pltpu.VMEM((len(order) * packed.shape[0], rows, att_width), jnp.bfloat16),
        ],
        cost_estimate=pl.CostEstimate(
            flops=attn_flops, transcendentals=heads * rows * window + rows * model_width, bytes_accessed=attn_bytes
        ),
        name="attention_glu",
    )(
        meta, utterance_lengths, table, bias_t, query_proj, from_prev, from_next, packed, partner, partner_sel,
        frames_in, norm_gain.reshape(1, -1),
        out_weight, expand_weight,
    )

    chips = count // cores
    inward = [(2 * c + 1, 2 * c + 2) for c in range(chips - 1)] + [(2 * c, 2 * c - 1) for c in range(1, chips)]
    cross_recv = lax.ppermute(cross_send, ("chip", "core"), inward)
    partner_recv = lax.ppermute(partner_send, "core", swap)
    conv_flops = 2 * KERNEL * rows * model_width + 2 * rows * model_width * model_width
    conv_bytes = 2 * (4 * half * model_width + rows * model_width * 2 + model_width * model_width) + 4 * KERNEL * model_width
    return pl.pallas_call(
        conv_kernel,
        out_shape=jax.ShapeDtypeStruct((rows, model_width), jnp.bfloat16),
        in_specs=[smem] + [vmem] * 7,
        out_specs=vmem,
        scratch_shapes=[
            pltpu.VMEM((rows + 2 * half, model_width), jnp.float32),
            pltpu.VMEM((rows, model_width), jnp.float32),
        ],
        cost_estimate=pl.CostEstimate(
            flops=conv_flops, transcendentals=rows * model_width, bytes_accessed=conv_bytes
        ),
        name="conv_shrink",
    )(
        meta, gated, cross_recv, partner_recv, depth_taps, inner_gain.reshape(1, -1), mid,
        pltpu.with_memory_space_constraint(shrink_weight, pltpu.VMEM),
    )


def solution(mesh):
    groups, seq = mesh.devices.shape
    chip_mesh = jax.sharding.Mesh(mesh.devices.reshape(groups, seq // 2, 2), ("groups", "chip", "core"))
    rows_spec = P(("groups", "chip", "core"), None)
    placed = (
        rows_spec,
        rows_spec,
        rows_spec,
        rows_spec,
        P("groups"),
        P(),
        P(),
        P(),
        P(),
        P(),
        P(),
        P(),
        P(),
    )
    return jax.shard_map(
        on_device, mesh=chip_mesh, in_specs=placed, out_specs=rows_spec, check_vma=False
    )
```

```python
import jax
import jax.numpy as jnp
from jax import lax
from jax.experimental import pallas as pl
from jax.experimental.pallas import tpu as pltpu
from jax.sharding import PartitionSpec as P

KERNEL = 31
DILATION = 4
REACH = 2
LANES = 128

norm_epsilon = 1e-05
masked_score = -1e30


def shifted(value, axis, steps):
    count = lax.axis_size(axis)
    leading, last = (max(0, -steps), min(count, count - steps))
    return lax.ppermute(value, axis, [(source, source + steps) for source in range(leading, last)])


def layer_norm(values, gain_vec):
    row_mean = jnp.mean(values, axis=-1, keepdims=True)
    centred = values - row_mean
    spread = jnp.mean(centred * centred, axis=-1, keepdims=True)
    return centred * lax.rsqrt(spread + norm_epsilon) * gain_vec


def sigmoid(values):
    return 1.0 / (1.0 + jnp.exp(-values))


def attention_kernel(
    meta_ref, len_ref, table_ref, bias_t_ref, q_ref,
    prev_hbm, next_hbm, own_hbm, partner_hbm, sel_hbm,
    x_ref, gain_ref, ow_hbm, ew_hbm,
    mid_ref, gated_ref, cross_ref, partner_ref,
    ow_vmem, ew_vmem, sems, att_ref, win_ref,
):
    base = meta_ref[0]
    core = meta_ref[1]
    planes = prev_hbm.shape[0]
    copies = [
        pltpu.make_async_copy(prev_hbm, win_ref.at[pl.ds(0, planes)], sems.at[2]),
        pltpu.make_async_copy(own_hbm, win_ref.at[pl.ds(2 * planes, planes)], sems.at[3]),
        pltpu.make_async_copy(next_hbm, win_ref.at[pl.ds(4 * planes, planes)], sems.at[4]),
        pltpu.make_async_copy(
            sel_hbm, win_ref.at[pl.ds(pl.multiple_of((1 + 2 * core) * planes, planes), planes)], sems.at[5]
        ),
        pltpu.make_async_copy(
            partner_hbm, win_ref.at[pl.ds(pl.multiple_of((3 - 2 * core) * planes, planes), planes)], sems.at[6]
        ),
    ]
    for copy in copies:
        copy.start()
    ow_copy = pltpu.make_async_copy(ow_hbm, ow_vmem, sems.at[0])
    ow_copy.start()
    model_width = ew_hbm.shape[0]
    pieces = 2
    piece = model_width // pieces
    ew_copies = []
    for j in range(pieces):
        pair_copies = []
        for part in range(2):
            cols = pl.ds(part * model_width + j * piece, piece)
            copy = pltpu.make_async_copy(ew_hbm.at[:, cols], ew_vmem.at[:, cols], sems.at[7 + 2 * j + part])
            copy.start()
            pair_copies.append(copy)
        ew_copies.append(pair_copies)
    blocks = win_ref.shape[0] // planes
    rows, att_width = q_ref.shape
    heads = bias_t_ref.shape[0]
    buckets = bias_t_ref.shape[1]
    head_width = att_width // heads
    width = blocks * rows
    line_len = table_ref.shape[1]

    qpos = base + lax.broadcasted_iota(jnp.int32, (rows, 1), 0)
    kpos = base - REACH * rows + lax.broadcasted_iota(jnp.int32, (1, width), 1)

    def seg_step(u, carry):
        run, qs, ks = carry
        run = run + len_ref[u]
        return run, qs + (qpos >= run).astype(jnp.int32), ks + (kpos >= run).astype(jnp.int32)

    _, qseg, kseg = lax.fori_loop(
        0, len_ref.shape[0], seg_step,
        (jnp.int32(0), jnp.zeros((rows, 1), jnp.int32), jnp.zeros((1, width), jnp.int32)),
    )
    kseg = jnp.where(kpos < 0, -1, kseg)
    same = qseg == kseg

    table = table_ref[...]
    bias_t = bias_t_ref[...]
    line = jnp.zeros((heads, line_len), jnp.float32)
    for b in range(buckets):
        line = jnp.where(table == b, bias_t[:, b:b + 1], line)

    for copy in copies:
        copy.wait()
    scaling = head_width ** (-0.5)
    lane = lax.broadcasted_iota(jnp.int32, (rows, LANES), 1)
    per_pair = LANES // head_width
    for pair in range(att_width // LANES):
        cols = slice(pair * LANES, (pair + 1) * LANES)
        q_pair = q_ref[:, cols]
        k_pair = jnp.concatenate([win_ref[planes * j, :, cols] for j in range(blocks)], axis=0)
        v_pair = jnp.concatenate([win_ref[planes * j + 1, :, cols] for j in range(blocks)], axis=0)
        result = None
        for sub in range(per_pair):
            head = pair * per_pair + sub
            in_head = (lane >= sub * head_width) & (lane < (sub + 1) * head_width)
            q_head = jnp.where(in_head, q_pair, jnp.zeros_like(q_pair))
            spread = jnp.broadcast_to(line[head:head + 1, :], (rows, line_len))
            skew = pltpu.roll(spread, line_len - rows + 1, 1, stride=1, stride_axis=0)[:, :width]
            bias = jnp.where(same, skew, masked_score)
            scores = lax.dot_general(
                q_head, k_pair, (((1,), (1,)), ((), ())), preferred_element_type=jnp.float32
            )
            scores = scores * scaling + bias
            top = jnp.max(scores, axis=1, keepdims=True)
            weights = jnp.exp(scores - top)
            total = jnp.sum(weights, axis=1, keepdims=True)
            summed = jnp.dot(weights.astype(jnp.bfloat16), v_pair, preferred_element_type=jnp.float32)
            part = summed / total
            result = part if result is None else jnp.where(in_head, part, result)
        att_ref[:, cols] = result.astype(jnp.bfloat16)

    ow_copy.wait()
    projected = jnp.dot(att_ref[...], ow_vmem[...], preferred_element_type=jnp.float32)
    mid = (x_ref[...].astype(jnp.float32) + projected).astype(jnp.bfloat16)
    mid_ref[...] = mid
    normed = layer_norm(mid.astype(jnp.float32), gain_ref[...]).astype(jnp.bfloat16)
    for j in range(pieces):
        for copy in ew_copies[j]:
            copy.wait()
        cols = slice(j * piece, (j + 1) * piece)
        gate_cols = slice(model_width + j * piece, model_width + (j + 1) * piece)
        value_half = jnp.dot(normed, ew_vmem[:, cols], preferred_element_type=jnp.float32)
        gate_half = jnp.dot(normed, ew_vmem[:, gate_cols], preferred_element_type=jnp.float32)
        gated_ref[:, cols] = (value_half * sigmoid(gate_half)).astype(jnp.bfloat16)
    half = cross_ref.shape[0]
    cross_ref[...] = gated_ref[pl.ds(pl.multiple_of(core * half, half), half), :]
    partner_ref[...] = gated_ref[pl.ds(pl.multiple_of((1 - core) * half, half), half), :]


def conv_kernel(
    meta_ref, gated_ref, cross_ref, pairg_ref, taps_ref, gain_ref, mid_ref, sw_hbm,
    out_ref, win_ref, conv_ref, sw_vmem, sems,
):
    pieces = 2
    piece = sw_hbm.shape[1] // pieces
    sw_copies = []
    for j in range(pieces):
        cols = pl.ds(j * piece, piece)
        copy = pltpu.make_async_copy(sw_hbm.at[:, cols], sw_vmem.at[:, cols], sems.at[j])
        copy.start()
        sw_copies.append(copy)
    half = cross_ref.shape[0]
    rows, model_width = mid_ref.shape
    first_core = meta_ref[1] == 0
    cross = cross_ref[...]
    partner = pairg_ref[...]
    win_ref[0:half, :] = jnp.where(first_core, cross, partner).astype(jnp.float32)
    win_ref[half:half + rows, :] = gated_ref[...].astype(jnp.float32)
    win_ref[half + rows:2 * half + rows, :] = jnp.where(first_core, partner, cross).astype(jnp.float32)
    reach = DILATION * (KERNEL - 1) // 2
    start = half - reach

    def chunk(c, carry):
        lanes = pl.ds(pl.multiple_of(c * LANES, LANES), LANES)
        acc = jnp.zeros((rows, LANES), jnp.float32)
        for tap in range(KERNEL):
            first = start + DILATION * tap
            acc = acc + taps_ref[tap:tap + 1, lanes] * win_ref[first:first + rows, lanes]
        conv_ref[:, lanes] = acc
        return carry

    lax.fori_loop(0, model_width // LANES, chunk, 0)
    inner = layer_norm(conv_ref[...], gain_ref[...])
    activated = (inner * sigmoid(inner)).astype(jnp.bfloat16)
    for j in range(pieces):
        sw_copies[j].wait()
        cols = slice(j * piece, (j + 1) * piece)
        shrunk = jnp.dot(activated, sw_vmem[:, cols], preferred_element_type=jnp.float32)
        out_ref[:, cols] = (mid_ref[:, cols].astype(jnp.float32) + shrunk).astype(out_ref.dtype)


def on_device(
    frames_in,
    query_proj,
    key_proj,
    value_proj,
    utterance_lengths,
    bucket_table,
    bucket_bias,
    out_weight,
    norm_gain,
    expand_weight,
    depth_taps,
    inner_gain,
    shrink_weight,
):
    rows, att_width = query_proj.shape
    model_width = frames_in.shape[1]
    heads = bucket_bias.shape[1]
    core = lax.axis_index("core")
    cores = lax.axis_size("core")
    count = lax.axis_size("chip") * cores
    device_index = lax.axis_index("chip") * cores + core
    meta = jnp.stack([device_index * rows, core]).astype(jnp.int32)

    def lin_shift(value, steps):
        leading, last = (max(0, -steps), min(count, count - steps))
        return lax.ppermute(value, ("chip", "core"), [(s, s + steps) for s in range(leading, last)])

    line_len = -(-bucket_table.shape[0] // LANES) * LANES
    table = jnp.pad(bucket_table, (0, line_len - bucket_table.shape[0])).reshape(1, line_len)
    bias_t = bucket_bias.T

    packed = jnp.stack([key_proj, value_proj])
    from_prev = lin_shift(packed, REACH)
    from_next = lin_shift(packed, -REACH)
    swap = [(0, 1), (1, 0)]
    partner = lax.ppermute(packed, "core", swap)
    sel = jnp.where(core == 0, from_next, from_prev)
    partner_sel = lax.ppermute(sel, "core", swap)
    order = list(range(-REACH, REACH + 1))

    half = rows // 2
    vmem = pl.BlockSpec(memory_space=pltpu.VMEM)
    smem = pl.BlockSpec(memory_space=pltpu.SMEM)
    anywhere = pl.BlockSpec(memory_space=pl.ANY)
    window = len(order) * rows
    attn_flops = 2 * 2 * heads * rows * window * LANES + 2 * rows * att_width * model_width + 2 * rows * model_width * 2 * model_width
    attn_bytes = 2 * (rows * att_width * (1 + 2 * len(order)) + rows * model_width * 2 + att_width * model_width + model_width * 2 * model_width)
    mid, gated, cross_send, partner_send = pl.pallas_call(
        attention_kernel,
        out_shape=(
            jax.ShapeDtypeStruct((rows, model_width), jnp.bfloat16),
            jax.ShapeDtypeStruct((rows, model_width), jnp.bfloat16),
            jax.ShapeDtypeStruct((half, model_width), jnp.bfloat16),
            jax.ShapeDtypeStruct((half, model_width), jnp.bfloat16),
        ),
        in_specs=[smem, smem, vmem, vmem, vmem] + [anywhere] * 5 + [vmem, vmem, anywhere, anywhere],
        out_specs=(vmem, vmem, vmem, vmem),
        scratch_shapes=[
            pltpu.VMEM((att_width, model_width), jnp.bfloat16),
            pltpu.VMEM((model_width, 2 * model_width), jnp.bfloat16),
            pltpu.SemaphoreType.DMA((11,)),
            pltpu.VMEM((rows, att_width), jnp.bfloat16),
            pltpu.VMEM((len(order) * packed.shape[0], rows, att_width), jnp.bfloat16),
        ],
        cost_estimate=pl.CostEstimate(
            flops=attn_flops, transcendentals=heads * rows * window + rows * model_width, bytes_accessed=attn_bytes
        ),
        name="attention_glu",
    )(
        meta, utterance_lengths, table, bias_t, query_proj, from_prev, from_next, packed, partner, partner_sel,
        frames_in, norm_gain.reshape(1, -1), out_weight, expand_weight,
    )

    chips = count // cores
    inward = [(2 * c + 1, 2 * c + 2) for c in range(chips - 1)] + [(2 * c, 2 * c - 1) for c in range(1, chips)]
    cross_recv = lax.ppermute(cross_send, ("chip", "core"), inward)
    partner_recv = lax.ppermute(partner_send, "core", swap)
    conv_flops = 2 * KERNEL * rows * model_width + 2 * rows * model_width * model_width
    conv_bytes = 2 * (4 * half * model_width + rows * model_width * 2 + model_width * model_width) + 4 * KERNEL * model_width
    return pl.pallas_call(
        conv_kernel,
        out_shape=jax.ShapeDtypeStruct((rows, model_width), jnp.bfloat16),
        in_specs=[smem] + [vmem] * 6 + [anywhere],
        out_specs=vmem,
        scratch_shapes=[
            pltpu.VMEM((rows + 2 * half, model_width), jnp.float32),
            pltpu.VMEM((rows, model_width), jnp.float32),
            pltpu.VMEM((model_width, model_width), jnp.bfloat16),
            pltpu.SemaphoreType.DMA((2,)),
        ],
        cost_estimate=pl.CostEstimate(
            flops=conv_flops, transcendentals=rows * model_width, bytes_accessed=conv_bytes
        ),
        name="conv_shrink",
    )(meta, gated, cross_recv, partner_recv, depth_taps, inner_gain.reshape(1, -1), mid, shrink_weight)


def solution(mesh):
    groups, seq = mesh.devices.shape
    chip_mesh = jax.sharding.Mesh(mesh.devices.reshape(groups, seq // 2, 2), ("groups", "chip", "core"))
    rows_spec = P(("groups", "chip", "core"), None)
    placed = (
        rows_spec,
        rows_spec,
        rows_spec,
        rows_spec,
        P("groups"),
        P(),
        P(),
        P(),
        P(),
        P(),
        P(),
        P(),
        P(),
    )
    return jax.shard_map(
        on_device, mesh=chip_mesh, in_specs=placed, out_specs=rows_spec, check_vma=False
    )
```

```python
import jax
import jax.numpy as jnp
from jax import lax
from jax.experimental import pallas as pl
from jax.experimental.pallas import tpu as pltpu
from jax.sharding import PartitionSpec as P

KERNEL = 31
DILATION = 4
REACH = 2
LANES = 128

norm_epsilon = 1e-05
masked_score = -1e30


def shifted(value, axis, steps):
    count = lax.axis_size(axis)
    leading, last = (max(0, -steps), min(count, count - steps))
    return lax.ppermute(value, axis, [(source, source + steps) for source in range(leading, last)])


def layer_norm(values, gain_vec):
    row_mean = jnp.mean(values, axis=-1, keepdims=True)
    centred = values - row_mean
    spread = jnp.mean(centred * centred, axis=-1, keepdims=True)
    return centred * lax.rsqrt(spread + norm_epsilon) * gain_vec


def sigmoid(values):
    return 1.0 / (1.0 + jnp.exp(-values))


def attention_kernel(
    meta_ref, len_ref, table_ref, bias_t_ref, q_ref,
    prev_hbm, next_hbm, own_hbm, partner_hbm, sel_hbm,
    x_ref, gain_ref, ow_hbm, ew_hbm,
    mid_ref, gated_ref, cross_ref, partner_ref,
    ow_vmem, ew_vmem, sems, att_ref, win_ref,
):
    base = meta_ref[0]
    core = meta_ref[1]
    planes = prev_hbm.shape[0]
    copies = [
        pltpu.make_async_copy(prev_hbm, win_ref.at[pl.ds(0, planes)], sems.at[2]),
        pltpu.make_async_copy(own_hbm, win_ref.at[pl.ds(2 * planes, planes)], sems.at[3]),
        pltpu.make_async_copy(next_hbm, win_ref.at[pl.ds(4 * planes, planes)], sems.at[4]),
        pltpu.make_async_copy(
            sel_hbm, win_ref.at[pl.ds(pl.multiple_of((1 + 2 * core) * planes, planes), planes)], sems.at[5]
        ),
        pltpu.make_async_copy(
            partner_hbm, win_ref.at[pl.ds(pl.multiple_of((3 - 2 * core) * planes, planes), planes)], sems.at[6]
        ),
    ]
    for copy in copies:
        copy.start()
    ow_copy = pltpu.make_async_copy(ow_hbm, ow_vmem, sems.at[0])
    ew_copy = pltpu.make_async_copy(ew_hbm, ew_vmem, sems.at[1])
    ow_copy.start()
    ew_copy.start()
    blocks = win_ref.shape[0] // planes
    rows, att_width = q_ref.shape
    heads = bias_t_ref.shape[0]
    buckets = bias_t_ref.shape[1]
    head_width = att_width // heads
    width = blocks * rows
    line_len = table_ref.shape[1]

    qpos = base + lax.broadcasted_iota(jnp.int32, (rows, 1), 0)
    kpos = base - REACH * rows + lax.broadcasted_iota(jnp.int32, (1, width), 1)

    def seg_step(u, carry):
        run, qs, ks = carry
        run = run + len_ref[u]
        return run, qs + (qpos >= run).astype(jnp.int32), ks + (kpos >= run).astype(jnp.int32)

    _, qseg, kseg = lax.fori_loop(
        0, len_ref.shape[0], seg_step,
        (jnp.int32(0), jnp.zeros((rows, 1), jnp.int32), jnp.zeros((1, width), jnp.int32)),
    )
    kseg = jnp.where(kpos < 0, -1, kseg)
    same = qseg == kseg

    table = table_ref[...]
    bias_t = bias_t_ref[...]
    line = jnp.zeros((heads, line_len), jnp.float32)
    for b in range(buckets):
        line = jnp.where(table == b, bias_t[:, b:b + 1], line)

    for copy in copies:
        copy.wait()
    scaling = head_width ** (-0.5)
    lane = lax.broadcasted_iota(jnp.int32, (rows, LANES), 1)
    per_pair = LANES // head_width
    for pair in range(att_width // LANES):
        cols = slice(pair * LANES, (pair + 1) * LANES)
        q_pair = q_ref[:, cols]
        k_pair = jnp.concatenate([win_ref[planes * j, :, cols] for j in range(blocks)], axis=0)
        v_pair = jnp.concatenate([win_ref[planes * j + 1, :, cols] for j in range(blocks)], axis=0)
        result = None
        for sub in range(per_pair):
            head = pair * per_pair + sub
            in_head = (lane >= sub * head_width) & (lane < (sub + 1) * head_width)
            q_head = jnp.where(in_head, q_pair, jnp.zeros_like(q_pair))
            spread = jnp.broadcast_to(line[head:head + 1, :], (rows, line_len))
            skew = pltpu.roll(spread, line_len - rows + 1, 1, stride=1, stride_axis=0)[:, :width]
            bias = jnp.where(same, skew, masked_score)
            scores = lax.dot_general(
                q_head, k_pair, (((1,), (1,)), ((), ())), preferred_element_type=jnp.float32
            )
            scores = scores * scaling + bias
            top = jnp.max(scores, axis=1, keepdims=True)
            weights = jnp.exp(scores - top)
            total = jnp.sum(weights, axis=1, keepdims=True)
            summed = jnp.dot(weights.astype(jnp.bfloat16), v_pair, preferred_element_type=jnp.float32)
            part = summed / total
            result = part if result is None else jnp.where(in_head, part, result)
        att_ref[:, cols] = result.astype(jnp.bfloat16)

    ow_copy.wait()
    projected = jnp.dot(att_ref[...], ow_vmem[...], preferred_element_type=jnp.float32)
    mid = (x_ref[...].astype(jnp.float32) + projected).astype(jnp.bfloat16)
    mid_ref[...] = mid
    normed = layer_norm(mid.astype(jnp.float32), gain_ref[...]).astype(jnp.bfloat16)
    model_width = mid.shape[1]
    ew_copy.wait()
    value_half = jnp.dot(normed, ew_vmem[:, :model_width], preferred_element_type=jnp.float32)
    gate_half = jnp.dot(normed, ew_vmem[:, model_width:], preferred_element_type=jnp.float32)
    gated = (value_half * sigmoid(gate_half)).astype(jnp.bfloat16)
    gated_ref[...] = gated
    half = cross_ref.shape[0]
    cross_ref[...] = gated_ref[pl.ds(pl.multiple_of(core * half, half), half), :]
    partner_ref[...] = gated_ref[pl.ds(pl.multiple_of((1 - core) * half, half), half), :]


def conv_kernel(
    meta_ref, gated_ref, cross_ref, pairg_ref, taps_ref, gain_ref, mid_ref, sw_hbm,
    out_ref, win_ref, conv_ref, sw_vmem, sems,
):
    sw_copy = pltpu.make_async_copy(sw_hbm, sw_vmem, sems.at[0])
    sw_copy.start()
    half = cross_ref.shape[0]
    rows, model_width = mid_ref.shape
    first_core = meta_ref[1] == 0
    cross = cross_ref[...]
    partner = pairg_ref[...]
    win_ref[0:half, :] = jnp.where(first_core, cross, partner).astype(jnp.float32)
    win_ref[half:half + rows, :] = gated_ref[...].astype(jnp.float32)
    win_ref[half + rows:2 * half + rows, :] = jnp.where(first_core, partner, cross).astype(jnp.float32)
    reach = DILATION * (KERNEL - 1) // 2
    start = half - reach

    def chunk(c, carry):
        lanes = pl.ds(pl.multiple_of(c * LANES, LANES), LANES)
        acc = jnp.zeros((rows, LANES), jnp.float32)
        for tap in range(KERNEL):
            first = start + DILATION * tap
            acc = acc + taps_ref[tap:tap + 1, lanes] * win_ref[first:first + rows, lanes]
        conv_ref[:, lanes] = acc
        return carry

    lax.fori_loop(0, model_width // LANES, chunk, 0)
    inner = layer_norm(conv_ref[...], gain_ref[...])
    activated = (inner * sigmoid(inner)).astype(jnp.bfloat16)
    sw_copy.wait()
    shrunk = jnp.dot(activated, sw_vmem[...], preferred_element_type=jnp.float32)
    out_ref[...] = (mid_ref[...].astype(jnp.float32) + shrunk).astype(out_ref.dtype)


def on_device(
    frames_in,
    query_proj,
    key_proj,
    value_proj,
    utterance_lengths,
    bucket_table,
    bucket_bias,
    out_weight,
    norm_gain,
    expand_weight,
    depth_taps,
    inner_gain,
    shrink_weight,
):
    rows, att_width = query_proj.shape
    model_width = frames_in.shape[1]
    heads = bucket_bias.shape[1]
    core = lax.axis_index("core")
    cores = lax.axis_size("core")
    count = lax.axis_size("chip") * cores
    device_index = lax.axis_index("chip") * cores + core
    meta = jnp.stack([device_index * rows, core]).astype(jnp.int32)

    def lin_shift(value, steps):
        leading, last = (max(0, -steps), min(count, count - steps))
        return lax.ppermute(value, ("chip", "core"), [(s, s + steps) for s in range(leading, last)])

    line_len = -(-bucket_table.shape[0] // LANES) * LANES
    table = jnp.pad(bucket_table, (0, line_len - bucket_table.shape[0])).reshape(1, line_len)
    bias_t = bucket_bias.T

    packed = jnp.stack([key_proj, value_proj])
    from_prev = lin_shift(packed, REACH)
    from_next = lin_shift(packed, -REACH)
    swap = [(0, 1), (1, 0)]
    gated_input, table, meta, bias_t = lax.optimization_barrier((packed, table, meta, bias_t))
    partner = lax.ppermute(gated_input, "core", swap)
    sel = jnp.where(core == 0, from_next, from_prev)
    partner_sel = lax.ppermute(sel, "core", swap)
    order = list(range(-REACH, REACH + 1))

    half = rows // 2
    vmem = pl.BlockSpec(memory_space=pltpu.VMEM)
    smem = pl.BlockSpec(memory_space=pltpu.SMEM)
    anywhere = pl.BlockSpec(memory_space=pl.ANY)
    window = len(order) * rows
    attn_flops = 2 * 2 * heads * rows * window * LANES + 2 * rows * att_width * model_width + 2 * rows * model_width * 2 * model_width
    attn_bytes = 2 * (rows * att_width * (1 + 2 * len(order)) + rows * model_width * 2 + att_width * model_width + model_width * 2 * model_width)
    mid, gated, cross_send, partner_send = pl.pallas_call(
        attention_kernel,
        out_shape=(
            jax.ShapeDtypeStruct((rows, model_width), jnp.bfloat16),
            jax.ShapeDtypeStruct((rows, model_width), jnp.bfloat16),
            jax.ShapeDtypeStruct((half, model_width), jnp.bfloat16),
            jax.ShapeDtypeStruct((half, model_width), jnp.bfloat16),
        ),
        in_specs=[smem, smem, vmem, vmem, vmem] + [anywhere] * 5 + [vmem, vmem, anywhere, anywhere],
        out_specs=(vmem, vmem, vmem, vmem),
        scratch_shapes=[
            pltpu.VMEM((att_width, model_width), jnp.bfloat16),
            pltpu.VMEM((model_width, 2 * model_width), jnp.bfloat16),
            pltpu.SemaphoreType.DMA((7,)),
            pltpu.VMEM((rows, att_width), jnp.bfloat16),
            pltpu.VMEM((len(order) * packed.shape[0], rows, att_width), jnp.bfloat16),
        ],
        cost_estimate=pl.CostEstimate(
            flops=attn_flops, transcendentals=heads * rows * window + rows * model_width, bytes_accessed=attn_bytes
        ),
        name="attention_glu",
    )(
        meta, utterance_lengths, table, bias_t, query_proj, from_prev, from_next, packed, partner, partner_sel,
        frames_in, norm_gain.reshape(1, -1), out_weight, expand_weight,
    )

    chips = count // cores
    inward = [(2 * c + 1, 2 * c + 2) for c in range(chips - 1)] + [(2 * c, 2 * c - 1) for c in range(1, chips)]
    cross_recv = lax.ppermute(cross_send, ("chip", "core"), inward)
    partner_recv = lax.ppermute(partner_send, "core", swap)
    conv_flops = 2 * KERNEL * rows * model_width + 2 * rows * model_width * model_width
    conv_bytes = 2 * (4 * half * model_width + rows * model_width * 2 + model_width * model_width) + 4 * KERNEL * model_width
    return pl.pallas_call(
        conv_kernel,
        out_shape=jax.ShapeDtypeStruct((rows, model_width), jnp.bfloat16),
        in_specs=[smem] + [vmem] * 6 + [anywhere],
        out_specs=vmem,
        scratch_shapes=[
            pltpu.VMEM((rows + 2 * half, model_width), jnp.float32),
            pltpu.VMEM((rows, model_width), jnp.float32),
            pltpu.VMEM((model_width, model_width), jnp.bfloat16),
            pltpu.SemaphoreType.DMA((1,)),
        ],
        cost_estimate=pl.CostEstimate(
            flops=conv_flops, transcendentals=rows * model_width, bytes_accessed=conv_bytes
        ),
        name="conv_shrink",
    )(meta, gated, cross_recv, partner_recv, depth_taps, inner_gain.reshape(1, -1), mid, shrink_weight)


def solution(mesh):
    groups, seq = mesh.devices.shape
    chip_mesh = jax.sharding.Mesh(mesh.devices.reshape(groups, seq // 2, 2), ("groups", "chip", "core"))
    rows_spec = P(("groups", "chip", "core"), None)
    placed = (
        rows_spec,
        rows_spec,
        rows_spec,
        rows_spec,
        P("groups"),
        P(),
        P(),
        P(),
        P(),
        P(),
        P(),
        P(),
        P(),
    )
    return jax.shard_map(
        on_device, mesh=chip_mesh, in_specs=placed, out_specs=rows_spec, check_vma=False
    )
```

```python
import jax
import jax.numpy as jnp
from jax import lax
from jax.experimental import pallas as pl
from jax.experimental.pallas import tpu as pltpu
from jax.sharding import PartitionSpec as P

KERNEL = 31
DILATION = 4
REACH = 2
LANES = 128

norm_epsilon = 1e-05
masked_score = -1e30


def shifted(value, axis, steps):
    count = lax.axis_size(axis)
    leading, last = (max(0, -steps), min(count, count - steps))
    return lax.ppermute(value, axis, [(source, source + steps) for source in range(leading, last)])


def layer_norm(values, gain_vec):
    row_mean = jnp.mean(values, axis=-1, keepdims=True)
    centred = values - row_mean
    spread = jnp.mean(centred * centred, axis=-1, keepdims=True)
    return centred * lax.rsqrt(spread + norm_epsilon) * gain_vec


def sigmoid(values):
    return 1.0 / (1.0 + jnp.exp(-values))


def attention_kernel(
    meta_ref, len_ref, table_ref, bias_t_ref, q_ref,
    prev_hbm, next_hbm, own_hbm, partner_hbm, sel_hbm,
    x_ref, gain_ref, ow_hbm, ew_hbm,
    mid_ref, gated_ref, cross_ref, partner_ref,
    ow_vmem, ew_vmem, sems, att_ref, win_ref,
):
    base = meta_ref[0]
    core = meta_ref[1]
    planes = prev_hbm.shape[0]
    copies = [
        pltpu.make_async_copy(prev_hbm, win_ref.at[pl.ds(0, planes)], sems.at[2]),
        pltpu.make_async_copy(own_hbm, win_ref.at[pl.ds(2 * planes, planes)], sems.at[3]),
        pltpu.make_async_copy(next_hbm, win_ref.at[pl.ds(4 * planes, planes)], sems.at[4]),
        pltpu.make_async_copy(
            sel_hbm, win_ref.at[pl.ds(pl.multiple_of((1 + 2 * core) * planes, planes), planes)], sems.at[5]
        ),
        pltpu.make_async_copy(
            partner_hbm, win_ref.at[pl.ds(pl.multiple_of((3 - 2 * core) * planes, planes), planes)], sems.at[6]
        ),
    ]
    for copy in copies:
        copy.start()
    ow_copy = pltpu.make_async_copy(ow_hbm, ow_vmem, sems.at[0])
    ew_copy = pltpu.make_async_copy(ew_hbm, ew_vmem, sems.at[1])
    ow_copy.start()
    ew_copy.start()
    blocks = win_ref.shape[0] // planes
    rows, att_width = q_ref.shape
    heads = bias_t_ref.shape[0]
    buckets = bias_t_ref.shape[1]
    head_width = att_width // heads
    width = blocks * rows
    line_len = table_ref.shape[1]

    qpos = base + lax.broadcasted_iota(jnp.int32, (rows, 1), 0)
    kpos = base - REACH * rows + lax.broadcasted_iota(jnp.int32, (1, width), 1)

    def seg_step(u, carry):
        run, qs, ks = carry
        run = run + len_ref[u]
        return run, qs + (qpos >= run).astype(jnp.int32), ks + (kpos >= run).astype(jnp.int32)

    _, qseg, kseg = lax.fori_loop(
        0, len_ref.shape[0], seg_step,
        (jnp.int32(0), jnp.zeros((rows, 1), jnp.int32), jnp.zeros((1, width), jnp.int32)),
    )
    kseg = jnp.where(kpos < 0, -1, kseg)
    same = qseg == kseg

    table = table_ref[...]
    bias_t = bias_t_ref[...]
    line = jnp.zeros((heads, line_len), jnp.float32)
    for b in range(buckets):
        line = jnp.where(table == b, bias_t[:, b:b + 1], line)

    for copy in copies:
        copy.wait()
    scaling = head_width ** (-0.5)
    lane = lax.broadcasted_iota(jnp.int32, (rows, LANES), 1)
    per_pair = LANES // head_width
    for pair in range(att_width // LANES):
        cols = slice(pair * LANES, (pair + 1) * LANES)
        q_pair = q_ref[:, cols]
        k_pair = jnp.concatenate([win_ref[planes * j, :, cols] for j in range(blocks)], axis=0)
        v_pair = jnp.concatenate([win_ref[planes * j + 1, :, cols] for j in range(blocks)], axis=0)
        result = None
        for sub in range(per_pair):
            head = pair * per_pair + sub
            in_head = (lane >= sub * head_width) & (lane < (sub + 1) * head_width)
            q_head = jnp.where(in_head, q_pair, jnp.zeros_like(q_pair))
            spread = jnp.broadcast_to(line[head:head + 1, :], (rows, line_len))
            skew = pltpu.roll(spread, line_len - rows + 1, 1, stride=1, stride_axis=0)[:, :width]
            bias = jnp.where(same, skew, masked_score)
            scores = lax.dot_general(
                q_head, k_pair, (((1,), (1,)), ((), ())), preferred_element_type=jnp.float32
            )
            scores = scores * scaling + bias
            top = jnp.max(scores, axis=1, keepdims=True)
            weights = jnp.exp(scores - top)
            total = jnp.sum(weights, axis=1, keepdims=True)
            summed = jnp.dot(weights.astype(jnp.bfloat16), v_pair, preferred_element_type=jnp.float32)
            part = summed / total
            result = part if result is None else jnp.where(in_head, part, result)
        att_ref[:, cols] = result.astype(jnp.bfloat16)

    ow_copy.wait()
    projected = jnp.dot(att_ref[...], ow_vmem[...], preferred_element_type=jnp.float32)
    mid = (x_ref[...].astype(jnp.float32) + projected).astype(jnp.bfloat16)
    mid_ref[...] = mid
    normed = layer_norm(mid.astype(jnp.float32), gain_ref[...]).astype(jnp.bfloat16)
    model_width = mid.shape[1]
    ew_copy.wait()
    value_half = jnp.dot(normed, ew_vmem[:, :model_width], preferred_element_type=jnp.float32)
    gate_half = jnp.dot(normed, ew_vmem[:, model_width:], preferred_element_type=jnp.float32)
    gated = (value_half * sigmoid(gate_half)).astype(jnp.bfloat16)
    gated_ref[...] = gated
    half = cross_ref.shape[0]
    cross_ref[...] = gated_ref[pl.ds(pl.multiple_of(core * half, half), half), :]
    partner_ref[...] = gated_ref[pl.ds(pl.multiple_of((1 - core) * half, half), half), :]


def conv_kernel(
    meta_ref, gated_ref, cross_ref, pairg_ref, taps_ref, gain_ref, mid_ref, sw_hbm,
    out_ref, win_ref, conv_ref, sw_vmem, sems,
):
    sw_copy = pltpu.make_async_copy(sw_hbm, sw_vmem, sems.at[0])
    sw_copy.start()
    half = cross_ref.shape[0]
    rows, model_width = mid_ref.shape
    first_core = meta_ref[1] == 0
    cross = cross_ref[...]
    partner = pairg_ref[...]
    win_ref[0:half, :] = jnp.where(first_core, cross, partner).astype(jnp.float32)
    win_ref[half:half + rows, :] = gated_ref[...].astype(jnp.float32)
    win_ref[half + rows:2 * half + rows, :] = jnp.where(first_core, partner, cross).astype(jnp.float32)
    reach = DILATION * (KERNEL - 1) // 2
    start = half - reach

    def chunk(c, carry):
        lanes = pl.ds(pl.multiple_of(c * LANES, LANES), LANES)
        acc = jnp.zeros((rows, LANES), jnp.float32)
        for tap in range(KERNEL):
            first = start + DILATION * tap
            acc = acc + taps_ref[tap:tap + 1, lanes] * win_ref[first:first + rows, lanes]
        conv_ref[:, lanes] = acc
        return carry

    lax.fori_loop(0, model_width // LANES, chunk, 0)
    inner = layer_norm(conv_ref[...], gain_ref[...])
    activated = (inner * sigmoid(inner)).astype(jnp.bfloat16)
    sw_copy.wait()
    shrunk = jnp.dot(activated, sw_vmem[...], preferred_element_type=jnp.float32)
    out_ref[...] = (mid_ref[...].astype(jnp.float32) + shrunk).astype(out_ref.dtype)


def on_device(
    frames_in,
    query_proj,
    key_proj,
    value_proj,
    utterance_lengths,
    bucket_table,
    bucket_bias,
    out_weight,
    norm_gain,
    expand_weight,
    depth_taps,
    inner_gain,
    shrink_weight,
):
    rows, att_width = query_proj.shape
    model_width = frames_in.shape[1]
    heads = bucket_bias.shape[1]
    core = lax.axis_index("core")
    cores = lax.axis_size("core")
    count = lax.axis_size("chip") * cores
    device_index = lax.axis_index("chip") * cores + core
    meta = jnp.stack([device_index * rows, core]).astype(jnp.int32)

    def lin_shift(value, steps):
        leading, last = (max(0, -steps), min(count, count - steps))
        return lax.ppermute(value, ("chip", "core"), [(s, s + steps) for s in range(leading, last)])

    line_len = -(-bucket_table.shape[0] // LANES) * LANES
    table = jnp.pad(bucket_table, (0, line_len - bucket_table.shape[0])).reshape(1, line_len)
    bias_t = bucket_bias.T

    packed = jnp.stack([key_proj, value_proj])
    from_prev = lin_shift(packed, REACH)
    from_next = lin_shift(packed, -REACH)
    swap = [(0, 1), (1, 0)]
    gated_input, table, meta, bias_t = lax.optimization_barrier((packed, table, meta, bias_t))
    partner = lax.ppermute(gated_input, "core", swap)
    sel = jnp.where(core == 0, from_next, from_prev)
    partner_sel = lax.ppermute(sel, "core", swap)
    order = list(range(-REACH, REACH + 1))

    half = rows // 2
    vmem = pl.BlockSpec(memory_space=pltpu.VMEM)
    smem = pl.BlockSpec(memory_space=pltpu.SMEM)
    anywhere = pl.BlockSpec(memory_space=pl.ANY)
    window = len(order) * rows
    attn_flops = 2 * 2 * heads * rows * window * LANES + 2 * rows * att_width * model_width + 2 * rows * model_width * 2 * model_width
    attn_bytes = 2 * (rows * att_width * (1 + 2 * len(order)) + rows * model_width * 2 + att_width * model_width + model_width * 2 * model_width)
    mid, gated, cross_send, partner_send = pl.pallas_call(
        attention_kernel,
        out_shape=(
            jax.ShapeDtypeStruct((rows, model_width), jnp.bfloat16),
            jax.ShapeDtypeStruct((rows, model_width), jnp.bfloat16),
            jax.ShapeDtypeStruct((half, model_width), jnp.bfloat16),
            jax.ShapeDtypeStruct((half, model_width), jnp.bfloat16),
        ),
        in_specs=[smem, smem, vmem, vmem, vmem] + [anywhere] * 5 + [vmem, vmem, anywhere, anywhere],
        out_specs=(vmem, vmem, vmem, vmem),
        scratch_shapes=[
            pltpu.VMEM((att_width, model_width), jnp.bfloat16),
            pltpu.VMEM((model_width, 2 * model_width), jnp.bfloat16),
            pltpu.SemaphoreType.DMA((7,)),
            pltpu.VMEM((rows, att_width), jnp.bfloat16),
            pltpu.VMEM((len(order) * packed.shape[0], rows, att_width), jnp.bfloat16),
        ],
        cost_estimate=pl.CostEstimate(
            flops=attn_flops, transcendentals=heads * rows * window + rows * model_width, bytes_accessed=attn_bytes
        ),
        name="attention_glu",
    )(
        meta, utterance_lengths, table, bias_t, query_proj, *[pltpu.with_memory_space_constraint(a, pltpu.VMEM) for a in (from_prev, from_next)], packed, *[pltpu.with_memory_space_constraint(a, pltpu.VMEM) for a in (partner, partner_sel)],
        frames_in, norm_gain.reshape(1, -1), out_weight, expand_weight,
    )

    chips = count // cores
    inward = [(2 * c + 1, 2 * c + 2) for c in range(chips - 1)] + [(2 * c, 2 * c - 1) for c in range(1, chips)]
    cross_recv = lax.ppermute(cross_send, ("chip", "core"), inward)
    partner_recv = lax.ppermute(partner_send, "core", swap)
    conv_flops = 2 * KERNEL * rows * model_width + 2 * rows * model_width * model_width
    conv_bytes = 2 * (4 * half * model_width + rows * model_width * 2 + model_width * model_width) + 4 * KERNEL * model_width
    return pl.pallas_call(
        conv_kernel,
        out_shape=jax.ShapeDtypeStruct((rows, model_width), jnp.bfloat16),
        in_specs=[smem] + [vmem] * 6 + [anywhere],
        out_specs=vmem,
        scratch_shapes=[
            pltpu.VMEM((rows + 2 * half, model_width), jnp.float32),
            pltpu.VMEM((rows, model_width), jnp.float32),
            pltpu.VMEM((model_width, model_width), jnp.bfloat16),
            pltpu.SemaphoreType.DMA((1,)),
        ],
        cost_estimate=pl.CostEstimate(
            flops=conv_flops, transcendentals=rows * model_width, bytes_accessed=conv_bytes
        ),
        name="conv_shrink",
    )(meta, gated, pltpu.with_memory_space_constraint(cross_recv, pltpu.VMEM), pltpu.with_memory_space_constraint(partner_recv, pltpu.VMEM), depth_taps, inner_gain.reshape(1, -1), mid, shrink_weight)


def solution(mesh):
    groups, seq = mesh.devices.shape
    chip_mesh = jax.sharding.Mesh(mesh.devices.reshape(groups, seq // 2, 2), ("groups", "chip", "core"))
    rows_spec = P(("groups", "chip", "core"), None)
    placed = (
        rows_spec,
        rows_spec,
        rows_spec,
        rows_spec,
        P("groups"),
        P(),
        P(),
        P(),
        P(),
        P(),
        P(),
        P(),
        P(),
    )
    return jax.shard_map(
        on_device, mesh=chip_mesh, in_specs=placed, out_specs=rows_spec, check_vma=False
    )
```

```python
import jax
import jax.numpy as jnp
from jax import lax
from jax.experimental import pallas as pl
from jax.experimental.pallas import tpu as pltpu
from jax.sharding import PartitionSpec as P

KERNEL = 31
DILATION = 4
REACH = 2
LANES = 128

norm_epsilon = 1e-05
masked_score = -1e30


def shifted(value, axis, steps):
    count = lax.axis_size(axis)
    leading, last = (max(0, -steps), min(count, count - steps))
    return lax.ppermute(value, axis, [(source, source + steps) for source in range(leading, last)])


def layer_norm(values, gain_vec):
    row_mean = jnp.mean(values, axis=-1, keepdims=True)
    centred = values - row_mean
    spread = jnp.mean(centred * centred, axis=-1, keepdims=True)
    return centred * lax.rsqrt(spread + norm_epsilon) * gain_vec


class row_chunks:
    def __init__(self, src, dst, sems, count):
        step = src.shape[0] // count
        self.copies = [
            pltpu.make_async_copy(src.at[pl.ds(i * step, step)], dst.at[pl.ds(i * step, step)], sems.at[i])
            for i in range(count)
        ]
        for copy in self.copies:
            copy.start()

    def wait(self):
        for copy in self.copies:
            copy.wait()


def sigmoid(values):
    return 1.0 / (1.0 + jnp.exp(-values))


def attention_kernel(
    meta_ref, len_ref, table_ref, bias_t_ref, q_ref,
    prev_hbm, next_hbm, own_hbm, partner_hbm, sel_hbm,
    x_ref, gain_ref, ow_hbm, ew_hbm,
    mid_ref, gated_ref, cross_ref, partner_ref,
    ow_vmem, ew_vmem, sems, att_ref, win_ref, chunk_sems,
):
    base = meta_ref[0]
    core = meta_ref[1]
    planes = prev_hbm.shape[0]
    copies = [
        pltpu.make_async_copy(prev_hbm, win_ref.at[pl.ds(0, planes)], sems.at[2]),
        pltpu.make_async_copy(own_hbm, win_ref.at[pl.ds(2 * planes, planes)], sems.at[3]),
        pltpu.make_async_copy(next_hbm, win_ref.at[pl.ds(4 * planes, planes)], sems.at[4]),
        pltpu.make_async_copy(
            sel_hbm, win_ref.at[pl.ds(pl.multiple_of((1 + 2 * core) * planes, planes), planes)], sems.at[5]
        ),
        pltpu.make_async_copy(
            partner_hbm, win_ref.at[pl.ds(pl.multiple_of((3 - 2 * core) * planes, planes), planes)], sems.at[6]
        ),
    ]
    for copy in copies:
        copy.start()
    ow_copy = row_chunks(ow_hbm, ow_vmem, chunk_sems.at[0], 2)
    ew_copy = row_chunks(ew_hbm, ew_vmem, chunk_sems.at[1], 4)
    blocks = win_ref.shape[0] // planes
    rows, att_width = q_ref.shape
    heads = bias_t_ref.shape[0]
    buckets = bias_t_ref.shape[1]
    head_width = att_width // heads
    width = blocks * rows
    line_len = table_ref.shape[1]

    qpos = base + lax.broadcasted_iota(jnp.int32, (rows, 1), 0)
    kpos = base - REACH * rows + lax.broadcasted_iota(jnp.int32, (1, width), 1)

    def seg_step(u, carry):
        run, qs, ks = carry
        run = run + len_ref[u]
        return run, qs + (qpos >= run).astype(jnp.int32), ks + (kpos >= run).astype(jnp.int32)

    _, qseg, kseg = lax.fori_loop(
        0, len_ref.shape[0], seg_step,
        (jnp.int32(0), jnp.zeros((rows, 1), jnp.int32), jnp.zeros((1, width), jnp.int32)),
    )
    kseg = jnp.where(kpos < 0, -1, kseg)
    same = qseg == kseg

    table = table_ref[...]
    bias_t = bias_t_ref[...]
    line = jnp.zeros((heads, line_len), jnp.float32)
    for b in range(buckets):
        line = jnp.where(table == b, bias_t[:, b:b + 1], line)

    for copy in copies:
        copy.wait()
    scaling = head_width ** (-0.5)
    lane = lax.broadcasted_iota(jnp.int32, (rows, LANES), 1)
    per_pair = LANES // head_width
    for pair in range(att_width // LANES):
        cols = slice(pair * LANES, (pair + 1) * LANES)
        q_pair = q_ref[:, cols]
        k_pair = jnp.concatenate([win_ref[planes * j, :, cols] for j in range(blocks)], axis=0)
        v_pair = jnp.concatenate([win_ref[planes * j + 1, :, cols] for j in range(blocks)], axis=0)
        result = None
        for sub in range(per_pair):
            head = pair * per_pair + sub
            in_head = (lane >= sub * head_width) & (lane < (sub + 1) * head_width)
            q_head = jnp.where(in_head, q_pair, jnp.zeros_like(q_pair))
            spread = jnp.broadcast_to(line[head:head + 1, :], (rows, line_len))
            skew = pltpu.roll(spread, line_len - rows + 1, 1, stride=1, stride_axis=0)[:, :width]
            bias = jnp.where(same, skew, masked_score)
            scores = lax.dot_general(
                q_head, k_pair, (((1,), (1,)), ((), ())), preferred_element_type=jnp.float32
            )
            scores = scores * scaling + bias
            top = jnp.max(scores, axis=1, keepdims=True)
            weights = jnp.exp(scores - top)
            total = jnp.sum(weights, axis=1, keepdims=True)
            summed = jnp.dot(weights.astype(jnp.bfloat16), v_pair, preferred_element_type=jnp.float32)
            part = summed / total
            result = part if result is None else jnp.where(in_head, part, result)
        att_ref[:, cols] = result.astype(jnp.bfloat16)

    ow_copy.wait()
    projected = jnp.dot(att_ref[...], ow_vmem[...], preferred_element_type=jnp.float32)
    mid = (x_ref[...].astype(jnp.float32) + projected).astype(jnp.bfloat16)
    mid_ref[...] = mid
    normed = layer_norm(mid.astype(jnp.float32), gain_ref[...]).astype(jnp.bfloat16)
    model_width = mid.shape[1]
    ew_copy.wait()
    value_half = jnp.dot(normed, ew_vmem[:, :model_width], preferred_element_type=jnp.float32)
    gate_half = jnp.dot(normed, ew_vmem[:, model_width:], preferred_element_type=jnp.float32)
    gated = (value_half * sigmoid(gate_half)).astype(jnp.bfloat16)
    gated_ref[...] = gated
    half = cross_ref.shape[0]
    cross_ref[...] = gated_ref[pl.ds(pl.multiple_of(core * half, half), half), :]
    partner_ref[...] = gated_ref[pl.ds(pl.multiple_of((1 - core) * half, half), half), :]


def conv_kernel(
    meta_ref, gated_ref, cross_ref, pairg_ref, taps_ref, gain_ref, mid_ref, sw_hbm,
    out_ref, win_ref, conv_ref, sw_vmem, sems,
):
    sw_copy = row_chunks(sw_hbm, sw_vmem, sems.at[0], 4)
    half = cross_ref.shape[0]
    rows, model_width = mid_ref.shape
    first_core = meta_ref[1] == 0
    cross = cross_ref[...]
    partner = pairg_ref[...]
    win_ref[0:half, :] = jnp.where(first_core, cross, partner).astype(jnp.float32)
    win_ref[half:half + rows, :] = gated_ref[...].astype(jnp.float32)
    win_ref[half + rows:2 * half + rows, :] = jnp.where(first_core, partner, cross).astype(jnp.float32)
    reach = DILATION * (KERNEL - 1) // 2
    start = half - reach

    def chunk(c, carry):
        lanes = pl.ds(pl.multiple_of(c * LANES, LANES), LANES)
        acc = jnp.zeros((rows, LANES), jnp.float32)
        for tap in range(KERNEL):
            first = start + DILATION * tap
            acc = acc + taps_ref[tap:tap + 1, lanes] * win_ref[first:first + rows, lanes]
        conv_ref[:, lanes] = acc
        return carry

    lax.fori_loop(0, model_width // LANES, chunk, 0)
    inner = layer_norm(conv_ref[...], gain_ref[...])
    activated = (inner * sigmoid(inner)).astype(jnp.bfloat16)
    sw_copy.wait()
    shrunk = jnp.dot(activated, sw_vmem[...], preferred_element_type=jnp.float32)
    out_ref[...] = (mid_ref[...].astype(jnp.float32) + shrunk).astype(out_ref.dtype)


def on_device(
    frames_in,
    query_proj,
    key_proj,
    value_proj,
    utterance_lengths,
    bucket_table,
    bucket_bias,
    out_weight,
    norm_gain,
    expand_weight,
    depth_taps,
    inner_gain,
    shrink_weight,
):
    rows, att_width = query_proj.shape
    model_width = frames_in.shape[1]
    heads = bucket_bias.shape[1]
    core = lax.axis_index("core")
    cores = lax.axis_size("core")
    count = lax.axis_size("chip") * cores
    device_index = lax.axis_index("chip") * cores + core
    meta = jnp.stack([device_index * rows, core]).astype(jnp.int32)

    def lin_shift(value, steps):
        leading, last = (max(0, -steps), min(count, count - steps))
        return lax.ppermute(value, ("chip", "core"), [(s, s + steps) for s in range(leading, last)])

    line_len = -(-bucket_table.shape[0] // LANES) * LANES
    table = jnp.pad(bucket_table, (0, line_len - bucket_table.shape[0])).reshape(1, line_len)
    bias_t = bucket_bias.T

    packed = jnp.stack([key_proj, value_proj])
    from_prev = lin_shift(packed, REACH)
    from_next = lin_shift(packed, -REACH)
    swap = [(0, 1), (1, 0)]
    gated_input, table, meta, bias_t = lax.optimization_barrier((packed, table, meta, bias_t))
    partner = lax.ppermute(gated_input, "core", swap)
    sel = jnp.where(core == 0, from_next, from_prev)
    partner_sel = lax.ppermute(sel, "core", swap)
    order = list(range(-REACH, REACH + 1))

    half = rows // 2
    vmem = pl.BlockSpec(memory_space=pltpu.VMEM)
    smem = pl.BlockSpec(memory_space=pltpu.SMEM)
    anywhere = pl.BlockSpec(memory_space=pl.ANY)
    window = len(order) * rows
    attn_flops = 2 * 2 * heads * rows * window * LANES + 2 * rows * att_width * model_width + 2 * rows * model_width * 2 * model_width
    attn_bytes = 2 * (rows * att_width * (1 + 2 * len(order)) + rows * model_width * 2 + att_width * model_width + model_width * 2 * model_width)
    mid, gated, cross_send, partner_send = pl.pallas_call(
        attention_kernel,
        out_shape=(
            jax.ShapeDtypeStruct((rows, model_width), jnp.bfloat16),
            jax.ShapeDtypeStruct((rows, model_width), jnp.bfloat16),
            jax.ShapeDtypeStruct((half, model_width), jnp.bfloat16),
            jax.ShapeDtypeStruct((half, model_width), jnp.bfloat16),
        ),
        in_specs=[smem, smem, vmem, vmem, vmem] + [anywhere] * 5 + [vmem, vmem, anywhere, anywhere],
        out_specs=(vmem, vmem, vmem, vmem),
        scratch_shapes=[
            pltpu.VMEM((att_width, model_width), jnp.bfloat16),
            pltpu.VMEM((model_width, 2 * model_width), jnp.bfloat16),
            pltpu.SemaphoreType.DMA((7,)),
            pltpu.VMEM((rows, att_width), jnp.bfloat16),
            pltpu.VMEM((len(order) * packed.shape[0], rows, att_width), jnp.bfloat16),
            pltpu.SemaphoreType.DMA((2, 4)),
        ],
        cost_estimate=pl.CostEstimate(
            flops=attn_flops, transcendentals=heads * rows * window + rows * model_width, bytes_accessed=attn_bytes
        ),
        name="attention_glu",
    )(
        meta, utterance_lengths, table, bias_t, query_proj, *[pltpu.with_memory_space_constraint(a, pltpu.VMEM) for a in (from_prev, from_next)], packed, *[pltpu.with_memory_space_constraint(a, pltpu.VMEM) for a in (partner, partner_sel)],
        frames_in, norm_gain.reshape(1, -1), out_weight, expand_weight,
    )

    chips = count // cores
    inward = [(2 * c + 1, 2 * c + 2) for c in range(chips - 1)] + [(2 * c, 2 * c - 1) for c in range(1, chips)]
    cross_recv = lax.ppermute(cross_send, ("chip", "core"), inward)
    partner_recv = lax.ppermute(partner_send, "core", swap)
    conv_flops = 2 * KERNEL * rows * model_width + 2 * rows * model_width * model_width
    conv_bytes = 2 * (4 * half * model_width + rows * model_width * 2 + model_width * model_width) + 4 * KERNEL * model_width
    return pl.pallas_call(
        conv_kernel,
        out_shape=jax.ShapeDtypeStruct((rows, model_width), jnp.bfloat16),
        in_specs=[smem] + [vmem] * 6 + [anywhere],
        out_specs=vmem,
        scratch_shapes=[
            pltpu.VMEM((rows + 2 * half, model_width), jnp.float32),
            pltpu.VMEM((rows, model_width), jnp.float32),
            pltpu.VMEM((model_width, model_width), jnp.bfloat16),
            pltpu.SemaphoreType.DMA((1, 4)),
        ],
        cost_estimate=pl.CostEstimate(
            flops=conv_flops, transcendentals=rows * model_width, bytes_accessed=conv_bytes
        ),
        name="conv_shrink",
    )(meta, gated, pltpu.with_memory_space_constraint(cross_recv, pltpu.VMEM), pltpu.with_memory_space_constraint(partner_recv, pltpu.VMEM), depth_taps, inner_gain.reshape(1, -1), mid, shrink_weight)


def solution(mesh):
    groups, seq = mesh.devices.shape
    chip_mesh = jax.sharding.Mesh(mesh.devices.reshape(groups, seq // 2, 2), ("groups", "chip", "core"))
    rows_spec = P(("groups", "chip", "core"), None)
    placed = (
        rows_spec,
        rows_spec,
        rows_spec,
        rows_spec,
        P("groups"),
        P(),
        P(),
        P(),
        P(),
        P(),
        P(),
        P(),
        P(),
    )
    return jax.shard_map(
        on_device, mesh=chip_mesh, in_specs=placed, out_specs=rows_spec, check_vma=False
    )
```

```python
import jax
import jax.numpy as jnp
from jax import lax
from jax.experimental import pallas as pl
from jax.experimental.pallas import tpu as pltpu
from jax.sharding import PartitionSpec as P

KERNEL = 31
DILATION = 4
REACH = 2
LANES = 128

norm_epsilon = 1e-05
masked_score = -1e30


def shifted(value, axis, steps):
    count = lax.axis_size(axis)
    leading, last = (max(0, -steps), min(count, count - steps))
    return lax.ppermute(value, axis, [(source, source + steps) for source in range(leading, last)])


def layer_norm(values, gain_vec):
    row_mean = jnp.mean(values, axis=-1, keepdims=True)
    centred = values - row_mean
    spread = jnp.mean(centred * centred, axis=-1, keepdims=True)
    return centred * lax.rsqrt(spread + norm_epsilon) * gain_vec


def sigmoid(values):
    return 1.0 / (1.0 + jnp.exp(-values))


def attention_kernel(
    meta_ref, len_ref, table_ref, bias_t_ref, q_ref,
    prev_hbm, next_hbm, own_hbm, partner_hbm, sel_hbm,
    x_ref, gain_ref, ow_hbm, value_hbm, gate_w,
    mid_ref, gated_ref, cross_ref, partner_ref,
    ow_vmem, value_w, sems, att_ref, win_ref,
):
    base = meta_ref[0]
    core = meta_ref[1]
    planes = prev_hbm.shape[0]
    copies = [
        pltpu.make_async_copy(prev_hbm, win_ref.at[pl.ds(0, planes)], sems.at[2]),
        pltpu.make_async_copy(own_hbm, win_ref.at[pl.ds(2 * planes, planes)], sems.at[3]),
        pltpu.make_async_copy(next_hbm, win_ref.at[pl.ds(4 * planes, planes)], sems.at[4]),
        pltpu.make_async_copy(
            sel_hbm, win_ref.at[pl.ds(pl.multiple_of((1 + 2 * core) * planes, planes), planes)], sems.at[5]
        ),
        pltpu.make_async_copy(
            partner_hbm, win_ref.at[pl.ds(pl.multiple_of((3 - 2 * core) * planes, planes), planes)], sems.at[6]
        ),
    ]
    for copy in copies:
        copy.start()
    ow_copy = pltpu.make_async_copy(ow_hbm, ow_vmem, sems.at[0])
    value_copy = pltpu.make_async_copy(value_hbm.at[:, pl.ds(0, value_w.shape[1])], value_w, sems.at[1])
    ow_copy.start()
    value_copy.start()
    blocks = win_ref.shape[0] // planes
    rows, att_width = q_ref.shape
    heads = bias_t_ref.shape[0]
    buckets = bias_t_ref.shape[1]
    head_width = att_width // heads
    width = blocks * rows
    line_len = table_ref.shape[1]

    qpos = base + lax.broadcasted_iota(jnp.int32, (rows, 1), 0)
    kpos = base - REACH * rows + lax.broadcasted_iota(jnp.int32, (1, width), 1)

    def seg_step(u, carry):
        run, qs, ks = carry
        run = run + len_ref[u]
        return run, qs + (qpos >= run).astype(jnp.int32), ks + (kpos >= run).astype(jnp.int32)

    _, qseg, kseg = lax.fori_loop(
        0, len_ref.shape[0], seg_step,
        (jnp.int32(0), jnp.zeros((rows, 1), jnp.int32), jnp.zeros((1, width), jnp.int32)),
    )
    kseg = jnp.where(kpos < 0, -1, kseg)
    same = qseg == kseg

    table = table_ref[...]
    bias_t = bias_t_ref[...]
    line = jnp.zeros((heads, line_len), jnp.float32)
    for b in range(buckets):
        line = jnp.where(table == b, bias_t[:, b:b + 1], line)

    for copy in copies:
        copy.wait()
    scaling = head_width ** (-0.5)
    lane = lax.broadcasted_iota(jnp.int32, (rows, LANES), 1)
    per_pair = LANES // head_width
    for pair in range(att_width // LANES):
        cols = slice(pair * LANES, (pair + 1) * LANES)
        q_pair = q_ref[:, cols]
        k_pair = jnp.concatenate([win_ref[planes * j, :, cols] for j in range(blocks)], axis=0)
        v_pair = jnp.concatenate([win_ref[planes * j + 1, :, cols] for j in range(blocks)], axis=0)
        result = None
        for sub in range(per_pair):
            head = pair * per_pair + sub
            in_head = (lane >= sub * head_width) & (lane < (sub + 1) * head_width)
            q_head = jnp.where(in_head, q_pair, jnp.zeros_like(q_pair))
            spread = jnp.broadcast_to(line[head:head + 1, :], (rows, line_len))
            skew = pltpu.roll(spread, line_len - rows + 1, 1, stride=1, stride_axis=0)[:, :width]
            bias = jnp.where(same, skew, masked_score)
            scores = lax.dot_general(
                q_head, k_pair, (((1,), (1,)), ((), ())), preferred_element_type=jnp.float32
            )
            scores = scores * scaling + bias
            top = jnp.max(scores, axis=1, keepdims=True)
            weights = jnp.exp(scores - top)
            total = jnp.sum(weights, axis=1, keepdims=True)
            summed = jnp.dot(weights.astype(jnp.bfloat16), v_pair, preferred_element_type=jnp.float32)
            part = summed / total
            result = part if result is None else jnp.where(in_head, part, result)
        att_ref[:, cols] = result.astype(jnp.bfloat16)

    ow_copy.wait()
    projected = jnp.dot(att_ref[...], ow_vmem[...], preferred_element_type=jnp.float32)
    mid = (x_ref[...].astype(jnp.float32) + projected).astype(jnp.bfloat16)
    mid_ref[...] = mid
    normed = layer_norm(mid.astype(jnp.float32), gain_ref[...]).astype(jnp.bfloat16)
    model_width = mid.shape[1]
    value_copy.wait()
    value_half = jnp.dot(normed, value_w[...], preferred_element_type=jnp.float32)
    gate_half = jnp.dot(normed, gate_w[...], preferred_element_type=jnp.float32)
    gated = (value_half * sigmoid(gate_half)).astype(jnp.bfloat16)
    gated_ref[...] = gated
    half = cross_ref.shape[0]
    cross_ref[...] = gated_ref[pl.ds(pl.multiple_of(core * half, half), half), :]
    partner_ref[...] = gated_ref[pl.ds(pl.multiple_of((1 - core) * half, half), half), :]


def conv_kernel(
    meta_ref, gated_ref, cross_ref, pairg_ref, taps_ref, gain_ref, mid_ref, sw_hbm,
    out_ref, win_ref, conv_ref, sw_vmem, sems,
):
    sw_copy = pltpu.make_async_copy(sw_hbm, sw_vmem, sems.at[0])
    sw_copy.start()
    half = cross_ref.shape[0]
    rows, model_width = mid_ref.shape
    first_core = meta_ref[1] == 0
    cross = cross_ref[...]
    partner = pairg_ref[...]
    win_ref[0:half, :] = jnp.where(first_core, cross, partner).astype(jnp.float32)
    win_ref[half:half + rows, :] = gated_ref[...].astype(jnp.float32)
    win_ref[half + rows:2 * half + rows, :] = jnp.where(first_core, partner, cross).astype(jnp.float32)
    reach = DILATION * (KERNEL - 1) // 2
    start = half - reach

    def chunk(c, carry):
        lanes = pl.ds(pl.multiple_of(c * LANES, LANES), LANES)
        acc = jnp.zeros((rows, LANES), jnp.float32)
        for tap in range(KERNEL):
            first = start + DILATION * tap
            acc = acc + taps_ref[tap:tap + 1, lanes] * win_ref[first:first + rows, lanes]
        conv_ref[:, lanes] = acc
        return carry

    lax.fori_loop(0, model_width // LANES, chunk, 0)
    inner = layer_norm(conv_ref[...], gain_ref[...])
    activated = (inner * sigmoid(inner)).astype(jnp.bfloat16)
    sw_copy.wait()
    shrunk = jnp.dot(activated, sw_vmem[...], preferred_element_type=jnp.float32)
    out_ref[...] = (mid_ref[...].astype(jnp.float32) + shrunk).astype(out_ref.dtype)


def on_device(
    frames_in,
    query_proj,
    key_proj,
    value_proj,
    utterance_lengths,
    bucket_table,
    bucket_bias,
    out_weight,
    norm_gain,
    expand_weight,
    depth_taps,
    inner_gain,
    shrink_weight,
):
    rows, att_width = query_proj.shape
    model_width = frames_in.shape[1]
    heads = bucket_bias.shape[1]
    core = lax.axis_index("core")
    cores = lax.axis_size("core")
    count = lax.axis_size("chip") * cores
    device_index = lax.axis_index("chip") * cores + core
    meta = jnp.stack([device_index * rows, core]).astype(jnp.int32)

    def lin_shift(value, steps):
        leading, last = (max(0, -steps), min(count, count - steps))
        return lax.ppermute(value, ("chip", "core"), [(s, s + steps) for s in range(leading, last)])

    line_len = -(-bucket_table.shape[0] // LANES) * LANES
    table = jnp.pad(bucket_table, (0, line_len - bucket_table.shape[0])).reshape(1, line_len)
    bias_t = bucket_bias.T

    packed = jnp.stack([key_proj, value_proj])
    from_prev = lin_shift(packed, REACH)
    from_next = lin_shift(packed, -REACH)
    swap = [(0, 1), (1, 0)]
    gated_input, table, meta, bias_t, gate_weight = lax.optimization_barrier((packed, table, meta, bias_t, expand_weight[:, model_width:]))
    partner = lax.ppermute(gated_input, "core", swap)
    sel = jnp.where(core == 0, from_next, from_prev)
    partner_sel = lax.ppermute(sel, "core", swap)
    order = list(range(-REACH, REACH + 1))

    half = rows // 2
    vmem = pl.BlockSpec(memory_space=pltpu.VMEM)
    smem = pl.BlockSpec(memory_space=pltpu.SMEM)
    anywhere = pl.BlockSpec(memory_space=pl.ANY)
    window = len(order) * rows
    attn_flops = 2 * 2 * heads * rows * window * LANES + 2 * rows * att_width * model_width + 2 * rows * model_width * 2 * model_width
    attn_bytes = 2 * (rows * att_width * (1 + 2 * len(order)) + rows * model_width * 2 + att_width * model_width + model_width * 2 * model_width)
    mid, gated, cross_send, partner_send = pl.pallas_call(
        attention_kernel,
        out_shape=(
            jax.ShapeDtypeStruct((rows, model_width), jnp.bfloat16),
            jax.ShapeDtypeStruct((rows, model_width), jnp.bfloat16),
            jax.ShapeDtypeStruct((half, model_width), jnp.bfloat16),
            jax.ShapeDtypeStruct((half, model_width), jnp.bfloat16),
        ),
        in_specs=[smem, smem, vmem, vmem, vmem] + [anywhere] * 5 + [vmem, vmem, anywhere, anywhere, vmem],
        out_specs=(vmem, vmem, vmem, vmem),
        scratch_shapes=[
            pltpu.VMEM((att_width, model_width), jnp.bfloat16),
            pltpu.VMEM((model_width, model_width), jnp.bfloat16),
            pltpu.SemaphoreType.DMA((7,)),
            pltpu.VMEM((rows, att_width), jnp.bfloat16),
            pltpu.VMEM((len(order) * packed.shape[0], rows, att_width), jnp.bfloat16),
        ],
        cost_estimate=pl.CostEstimate(
            flops=attn_flops, transcendentals=heads * rows * window + rows * model_width, bytes_accessed=attn_bytes
        ),
        name="attention_glu",
    )(
        meta, utterance_lengths, table, bias_t, query_proj, *[pltpu.with_memory_space_constraint(a, pltpu.VMEM) for a in (from_prev, from_next)], packed, *[pltpu.with_memory_space_constraint(a, pltpu.VMEM) for a in (partner, partner_sel)],
        frames_in, norm_gain.reshape(1, -1), out_weight,
        expand_weight,
        pltpu.with_memory_space_constraint(gate_weight, pltpu.VMEM),
    )

    chips = count // cores
    inward = [(2 * c + 1, 2 * c + 2) for c in range(chips - 1)] + [(2 * c, 2 * c - 1) for c in range(1, chips)]
    cross_recv = lax.ppermute(cross_send, ("chip", "core"), inward)
    partner_recv = lax.ppermute(partner_send, "core", swap)
    conv_flops = 2 * KERNEL * rows * model_width + 2 * rows * model_width * model_width
    conv_bytes = 2 * (4 * half * model_width + rows * model_width * 2 + model_width * model_width) + 4 * KERNEL * model_width
    return pl.pallas_call(
        conv_kernel,
        out_shape=jax.ShapeDtypeStruct((rows, model_width), jnp.bfloat16),
        in_specs=[smem] + [vmem] * 6 + [anywhere],
        out_specs=vmem,
        scratch_shapes=[
            pltpu.VMEM((rows + 2 * half, model_width), jnp.float32),
            pltpu.VMEM((rows, model_width), jnp.float32),
            pltpu.VMEM((model_width, model_width), jnp.bfloat16),
            pltpu.SemaphoreType.DMA((1,)),
        ],
        cost_estimate=pl.CostEstimate(
            flops=conv_flops, transcendentals=rows * model_width, bytes_accessed=conv_bytes
        ),
        name="conv_shrink",
    )(meta, gated, pltpu.with_memory_space_constraint(cross_recv, pltpu.VMEM), pltpu.with_memory_space_constraint(partner_recv, pltpu.VMEM), depth_taps, inner_gain.reshape(1, -1), mid, shrink_weight)


def solution(mesh):
    groups, seq = mesh.devices.shape
    chip_mesh = jax.sharding.Mesh(mesh.devices.reshape(groups, seq // 2, 2), ("groups", "chip", "core"))
    rows_spec = P(("groups", "chip", "core"), None)
    placed = (
        rows_spec,
        rows_spec,
        rows_spec,
        rows_spec,
        P("groups"),
        P(),
        P(),
        P(),
        P(),
        P(),
        P(),
        P(),
        P(),
    )
    return jax.shard_map(
        on_device, mesh=chip_mesh, in_specs=placed, out_specs=rows_spec, check_vma=False
    )
```

```python
import jax
import jax.numpy as jnp
from jax import lax
from jax.experimental import pallas as pl
from jax.experimental.pallas import tpu as pltpu
from jax.sharding import PartitionSpec as P

KERNEL = 31
DILATION = 4
REACH = 2
LANES = 128

norm_epsilon = 1e-05
masked_score = -1e30


def shifted(value, axis, steps):
    count = lax.axis_size(axis)
    leading, last = (max(0, -steps), min(count, count - steps))
    return lax.ppermute(value, axis, [(source, source + steps) for source in range(leading, last)])


def layer_norm(values, gain_vec):
    row_mean = jnp.mean(values, axis=-1, keepdims=True)
    centred = values - row_mean
    spread = jnp.mean(centred * centred, axis=-1, keepdims=True)
    return centred * lax.rsqrt(spread + norm_epsilon) * gain_vec


def sigmoid(values):
    return 1.0 / (1.0 + jnp.exp(-values))


def attention_kernel(
    meta_ref, len_ref, table_ref, bias_t_ref, q_ref,
    prev_hbm, next_hbm, own_hbm, partner_hbm, sel_hbm,
    x_ref, gain_ref, ow_hbm, value_hbm, gate_w,
    mid_ref, gated_ref, cross_ref, partner_ref,
    ow_vmem, value_w, sems, att_ref, win_ref,
):
    base = meta_ref[0]
    core = meta_ref[1]
    planes = prev_hbm.shape[0]
    copies = [
        pltpu.make_async_copy(prev_hbm, win_ref.at[pl.ds(0, planes)], sems.at[2]),
        pltpu.make_async_copy(own_hbm, win_ref.at[pl.ds(2 * planes, planes)], sems.at[3]),
        pltpu.make_async_copy(next_hbm, win_ref.at[pl.ds(4 * planes, planes)], sems.at[4]),
        pltpu.make_async_copy(
            sel_hbm, win_ref.at[pl.ds(pl.multiple_of((1 + 2 * core) * planes, planes), planes)], sems.at[5]
        ),
        pltpu.make_async_copy(
            partner_hbm, win_ref.at[pl.ds(pl.multiple_of((3 - 2 * core) * planes, planes), planes)], sems.at[6]
        ),
    ]
    for copy in copies:
        copy.start()
    ow_copy = pltpu.make_async_copy(ow_hbm, ow_vmem, sems.at[0])
    value_copy = pltpu.make_async_copy(value_hbm.at[:, pl.ds(0, value_w.shape[1])], value_w, sems.at[1])
    ow_copy.start()
    value_copy.start()
    blocks = win_ref.shape[0] // planes
    rows, att_width = q_ref.shape
    heads = bias_t_ref.shape[0]
    buckets = bias_t_ref.shape[1]
    head_width = att_width // heads
    width = blocks * rows
    line_len = table_ref.shape[1]

    qpos = base + lax.broadcasted_iota(jnp.int32, (rows, 1), 0)
    kpos = base - REACH * rows + lax.broadcasted_iota(jnp.int32, (1, width), 1)

    def seg_step(u, carry):
        run, qs, ks = carry
        run = run + len_ref[u]
        return run, qs + (qpos >= run).astype(jnp.int32), ks + (kpos >= run).astype(jnp.int32)

    _, qseg, kseg = lax.fori_loop(
        0, len_ref.shape[0], seg_step,
        (jnp.int32(0), jnp.zeros((rows, 1), jnp.int32), jnp.zeros((1, width), jnp.int32)),
    )
    kseg = jnp.where(kpos < 0, -1, kseg)
    same = qseg == kseg

    table = table_ref[...]
    bias_t = bias_t_ref[...]
    line = jnp.zeros((heads, line_len), jnp.float32)
    for b in range(buckets):
        line = jnp.where(table == b, bias_t[:, b:b + 1], line)

    for copy in copies:
        copy.wait()
    scaling = head_width ** (-0.5)
    lane = lax.broadcasted_iota(jnp.int32, (rows, LANES), 1)
    per_pair = LANES // head_width
    for pair in range(att_width // LANES):
        cols = slice(pair * LANES, (pair + 1) * LANES)
        q_pair = q_ref[:, cols]
        k_pair = jnp.concatenate([win_ref[planes * j, :, cols] for j in range(blocks)], axis=0)
        v_pair = jnp.concatenate([win_ref[planes * j + 1, :, cols] for j in range(blocks)], axis=0)
        result = None
        for sub in range(per_pair):
            head = pair * per_pair + sub
            in_head = (lane >= sub * head_width) & (lane < (sub + 1) * head_width)
            q_head = jnp.where(in_head, q_pair, jnp.zeros_like(q_pair))
            spread = jnp.broadcast_to(line[head:head + 1, :], (rows, line_len))
            skew = pltpu.roll(spread, line_len - rows + 1, 1, stride=1, stride_axis=0)[:, :width]
            bias = jnp.where(same, skew, masked_score)
            scores = lax.dot_general(
                q_head, k_pair, (((1,), (1,)), ((), ())), preferred_element_type=jnp.float32
            )
            scores = scores * scaling + bias
            top = jnp.max(scores, axis=1, keepdims=True)
            weights = jnp.exp(scores - top)
            total = jnp.sum(weights, axis=1, keepdims=True)
            summed = jnp.dot(weights.astype(jnp.bfloat16), v_pair, preferred_element_type=jnp.float32)
            part = summed / total
            result = part if result is None else jnp.where(in_head, part, result)
        att_ref[:, cols] = result.astype(jnp.bfloat16)

    ow_copy.wait()
    projected = jnp.dot(att_ref[...], ow_vmem[...], preferred_element_type=jnp.float32)
    mid = (x_ref[...].astype(jnp.float32) + projected).astype(jnp.bfloat16)
    mid_ref[...] = mid
    normed = layer_norm(mid.astype(jnp.float32), gain_ref[...]).astype(jnp.bfloat16)
    model_width = mid.shape[1]
    value_copy.wait()
    value_half = jnp.dot(normed, value_w[...], preferred_element_type=jnp.float32)
    gate_half = jnp.dot(normed, gate_w[...], preferred_element_type=jnp.float32)
    gated = (value_half * sigmoid(gate_half)).astype(jnp.bfloat16)
    gated_ref[...] = gated
    half = cross_ref.shape[0]
    cross_ref[...] = gated_ref[pl.ds(pl.multiple_of(core * half, half), half), :]
    partner_ref[...] = gated_ref[pl.ds(pl.multiple_of((1 - core) * half, half), half), :]


def conv_kernel(
    meta_ref, gated_ref, cross_ref, pairg_ref, taps_ref, gain_ref, mid_ref, sw_hbm,
    out_ref, win_ref, conv_ref, sw_vmem, sems,
):
    sw_copy = pltpu.make_async_copy(sw_hbm, sw_vmem, sems.at[0])
    sw_copy.start()
    half = cross_ref.shape[0]
    rows, model_width = mid_ref.shape
    first_core = meta_ref[1] == 0
    cross = cross_ref[...]
    partner = pairg_ref[...]
    win_ref[0:half, :] = jnp.where(first_core, cross, partner).astype(jnp.float32)
    win_ref[half:half + rows, :] = gated_ref[...].astype(jnp.float32)
    win_ref[half + rows:2 * half + rows, :] = jnp.where(first_core, partner, cross).astype(jnp.float32)
    reach = DILATION * (KERNEL - 1) // 2
    start = half - reach

    def chunk(c, carry):
        lanes = pl.ds(pl.multiple_of(c * LANES, LANES), LANES)
        acc = jnp.zeros((rows, LANES), jnp.float32)
        for tap in range(KERNEL):
            first = start + DILATION * tap
            acc = acc + taps_ref[tap:tap + 1, lanes] * win_ref[first:first + rows, lanes]
        conv_ref[:, lanes] = acc
        return carry

    lax.fori_loop(0, model_width // LANES, chunk, 0)
    inner = layer_norm(conv_ref[...], gain_ref[...])
    activated = (inner * sigmoid(inner)).astype(jnp.bfloat16)
    sw_copy.wait()
    shrunk = jnp.dot(activated, sw_vmem[...], preferred_element_type=jnp.float32)
    out_ref[...] = (mid_ref[...].astype(jnp.float32) + shrunk).astype(out_ref.dtype)


def on_device(
    frames_in,
    query_proj,
    key_proj,
    value_proj,
    utterance_lengths,
    bucket_table,
    bucket_bias,
    out_weight,
    norm_gain,
    expand_weight,
    depth_taps,
    inner_gain,
    shrink_weight,
):
    rows, att_width = query_proj.shape
    model_width = frames_in.shape[1]
    heads = bucket_bias.shape[1]
    core = lax.axis_index("core")
    cores = lax.axis_size("core")
    count = lax.axis_size("chip") * cores
    device_index = lax.axis_index("chip") * cores + core
    meta = jnp.stack([device_index * rows, core]).astype(jnp.int32)

    def lin_shift(value, steps):
        leading, last = (max(0, -steps), min(count, count - steps))
        return lax.ppermute(value, ("chip", "core"), [(s, s + steps) for s in range(leading, last)])

    line_len = -(-bucket_table.shape[0] // LANES) * LANES
    table = jnp.pad(bucket_table, (0, line_len - bucket_table.shape[0])).reshape(1, line_len)
    bias_t = bucket_bias.T

    packed = jnp.concatenate([key_proj, value_proj], axis=0).reshape(2, rows, att_width)
    from_prev = lin_shift(packed, REACH)
    from_next = lin_shift(packed, -REACH)
    swap = [(0, 1), (1, 0)]
    gated_input, table, meta, bias_t, gate_weight = lax.optimization_barrier((packed, table, meta, bias_t, expand_weight[:, model_width:]))
    partner = lax.ppermute(gated_input, "core", swap)
    sel = jnp.where(core == 0, from_next, from_prev)
    partner_sel = lax.ppermute(sel, "core", swap)
    order = list(range(-REACH, REACH + 1))

    half = rows // 2
    vmem = pl.BlockSpec(memory_space=pltpu.VMEM)
    smem = pl.BlockSpec(memory_space=pltpu.SMEM)
    anywhere = pl.BlockSpec(memory_space=pl.ANY)
    window = len(order) * rows
    attn_flops = 2 * 2 * heads * rows * window * LANES + 2 * rows * att_width * model_width + 2 * rows * model_width * 2 * model_width
    attn_bytes = 2 * (rows * att_width * (1 + 2 * len(order)) + rows * model_width * 2 + att_width * model_width + model_width * 2 * model_width)
    mid, gated, cross_send, partner_send = pl.pallas_call(
        attention_kernel,
        out_shape=(
            jax.ShapeDtypeStruct((rows, model_width), jnp.bfloat16),
            jax.ShapeDtypeStruct((rows, model_width), jnp.bfloat16),
            jax.ShapeDtypeStruct((half, model_width), jnp.bfloat16),
            jax.ShapeDtypeStruct((half, model_width), jnp.bfloat16),
        ),
        in_specs=[smem, smem, vmem, vmem, vmem] + [anywhere] * 5 + [vmem, vmem, anywhere, anywhere, vmem],
        out_specs=(vmem, vmem, vmem, vmem),
        scratch_shapes=[
            pltpu.VMEM((att_width, model_width), jnp.bfloat16),
            pltpu.VMEM((model_width, model_width), jnp.bfloat16),
            pltpu.SemaphoreType.DMA((7,)),
            pltpu.VMEM((rows, att_width), jnp.bfloat16),
            pltpu.VMEM((len(order) * packed.shape[0], rows, att_width), jnp.bfloat16),
        ],
        cost_estimate=pl.CostEstimate(
            flops=attn_flops, transcendentals=heads * rows * window + rows * model_width, bytes_accessed=attn_bytes
        ),
        name="attention_glu",
    )(
        meta, utterance_lengths, table, bias_t, query_proj, *[pltpu.with_memory_space_constraint(a, pltpu.VMEM) for a in (from_prev, from_next)], packed, *[pltpu.with_memory_space_constraint(a, pltpu.VMEM) for a in (partner, partner_sel)],
        frames_in, norm_gain.reshape(1, -1), out_weight,
        expand_weight,
        pltpu.with_memory_space_constraint(gate_weight, pltpu.VMEM),
    )

    chips = count // cores
    inward = [(2 * c + 1, 2 * c + 2) for c in range(chips - 1)] + [(2 * c, 2 * c - 1) for c in range(1, chips)]
    cross_recv = lax.ppermute(cross_send, ("chip", "core"), inward)
    partner_recv = lax.ppermute(partner_send, "core", swap)
    conv_flops = 2 * KERNEL * rows * model_width + 2 * rows * model_width * model_width
    conv_bytes = 2 * (4 * half * model_width + rows * model_width * 2 + model_width * model_width) + 4 * KERNEL * model_width
    return pl.pallas_call(
        conv_kernel,
        out_shape=jax.ShapeDtypeStruct((rows, model_width), jnp.bfloat16),
        in_specs=[smem] + [vmem] * 6 + [anywhere],
        out_specs=vmem,
        scratch_shapes=[
            pltpu.VMEM((rows + 2 * half, model_width), jnp.float32),
            pltpu.VMEM((rows, model_width), jnp.float32),
            pltpu.VMEM((model_width, model_width), jnp.bfloat16),
            pltpu.SemaphoreType.DMA((1,)),
        ],
        cost_estimate=pl.CostEstimate(
            flops=conv_flops, transcendentals=rows * model_width, bytes_accessed=conv_bytes
        ),
        name="conv_shrink",
    )(meta, gated, pltpu.with_memory_space_constraint(cross_recv, pltpu.VMEM), pltpu.with_memory_space_constraint(partner_recv, pltpu.VMEM), depth_taps, inner_gain.reshape(1, -1), mid, shrink_weight)


def solution(mesh):
    groups, seq = mesh.devices.shape
    chip_mesh = jax.sharding.Mesh(mesh.devices.reshape(groups, seq // 2, 2), ("groups", "chip", "core"))
    rows_spec = P(("groups", "chip", "core"), None)
    placed = (
        rows_spec,
        rows_spec,
        rows_spec,
        rows_spec,
        P("groups"),
        P(),
        P(),
        P(),
        P(),
        P(),
        P(),
        P(),
        P(),
    )
    return jax.shard_map(
        on_device, mesh=chip_mesh, in_specs=placed, out_specs=rows_spec, check_vma=False
    )
```

```python
import jax
import jax.numpy as jnp
from jax import lax
from jax.experimental import pallas as pl
from jax.experimental.pallas import tpu as pltpu
from jax.sharding import PartitionSpec as P

KERNEL = 31
DILATION = 4
REACH = 2
LANES = 128

norm_epsilon = 1e-05
masked_score = -1e30


def shifted(value, axis, steps):
    count = lax.axis_size(axis)
    leading, last = (max(0, -steps), min(count, count - steps))
    return lax.ppermute(value, axis, [(source, source + steps) for source in range(leading, last)])


def layer_norm(values, gain_vec):
    row_mean = jnp.mean(values, axis=-1, keepdims=True)
    centred = values - row_mean
    spread = jnp.mean(centred * centred, axis=-1, keepdims=True)
    return centred * lax.rsqrt(spread + norm_epsilon) * gain_vec


def sigmoid(values):
    return 0.5 * jnp.tanh(0.5 * values) + 0.5


def attention_kernel(
    meta_ref, len_ref, table_ref, bias_t_ref, q_ref,
    prev_hbm, next_hbm, own_hbm, partner_hbm, sel_hbm,
    x_ref, gain_ref, ow_hbm, value_hbm, gate_w,
    mid_ref, gated_ref, cross_ref, partner_ref,
    ow_vmem, value_w, sems, att_ref, win_ref,
):
    base = meta_ref[0]
    core = meta_ref[1]
    planes = prev_hbm.shape[0]
    copies = [
        pltpu.make_async_copy(prev_hbm, win_ref.at[pl.ds(0, planes)], sems.at[2]),
        pltpu.make_async_copy(own_hbm, win_ref.at[pl.ds(2 * planes, planes)], sems.at[3]),
        pltpu.make_async_copy(next_hbm, win_ref.at[pl.ds(4 * planes, planes)], sems.at[4]),
        pltpu.make_async_copy(
            sel_hbm, win_ref.at[pl.ds(pl.multiple_of((1 + 2 * core) * planes, planes), planes)], sems.at[5]
        ),
        pltpu.make_async_copy(
            partner_hbm, win_ref.at[pl.ds(pl.multiple_of((3 - 2 * core) * planes, planes), planes)], sems.at[6]
        ),
    ]
    for copy in copies:
        copy.start()
    ow_copy = pltpu.make_async_copy(ow_hbm, ow_vmem, sems.at[0])
    value_copy = pltpu.make_async_copy(value_hbm.at[:, pl.ds(0, value_w.shape[1])], value_w, sems.at[1])
    ow_copy.start()
    value_copy.start()
    blocks = win_ref.shape[0] // planes
    rows, att_width = q_ref.shape
    heads = bias_t_ref.shape[0]
    buckets = bias_t_ref.shape[1]
    head_width = att_width // heads
    width = blocks * rows
    line_len = table_ref.shape[1]

    qpos = base + lax.broadcasted_iota(jnp.int32, (rows, 1), 0)
    kpos = base - REACH * rows + lax.broadcasted_iota(jnp.int32, (1, width), 1)

    def seg_step(u, carry):
        run, qs, ks = carry
        run = run + len_ref[u]
        return run, qs + (qpos >= run).astype(jnp.int32), ks + (kpos >= run).astype(jnp.int32)

    _, qseg, kseg = lax.fori_loop(
        0, len_ref.shape[0], seg_step,
        (jnp.int32(0), jnp.zeros((rows, 1), jnp.int32), jnp.zeros((1, width), jnp.int32)),
    )
    kseg = jnp.where(kpos < 0, -1, kseg)
    same = qseg == kseg

    table = table_ref[...]
    bias_t = bias_t_ref[...]
    line = jnp.zeros((heads, line_len), jnp.float32)
    for b in range(buckets):
        line = jnp.where(table == b, bias_t[:, b:b + 1], line)

    for copy in copies:
        copy.wait()
    scaling = head_width ** (-0.5)
    lane = lax.broadcasted_iota(jnp.int32, (rows, LANES), 1)
    per_pair = LANES // head_width
    for pair in range(att_width // LANES):
        cols = slice(pair * LANES, (pair + 1) * LANES)
        q_pair = q_ref[:, cols]
        k_pair = jnp.concatenate([win_ref[planes * j, :, cols] for j in range(blocks)], axis=0)
        v_pair = jnp.concatenate([win_ref[planes * j + 1, :, cols] for j in range(blocks)], axis=0)
        result = None
        for sub in range(per_pair):
            head = pair * per_pair + sub
            in_head = (lane >= sub * head_width) & (lane < (sub + 1) * head_width)
            q_head = jnp.where(in_head, q_pair, jnp.zeros_like(q_pair))
            spread = jnp.broadcast_to(line[head:head + 1, :], (rows, line_len))
            skew = pltpu.roll(spread, line_len - rows + 1, 1, stride=1, stride_axis=0)[:, :width]
            bias = jnp.where(same, skew, masked_score)
            scores = lax.dot_general(
                q_head, k_pair, (((1,), (1,)), ((), ())), preferred_element_type=jnp.float32
            )
            scores = scores * scaling + bias
            top = jnp.max(scores, axis=1, keepdims=True)
            weights = jnp.exp(scores - top)
            total = jnp.sum(weights, axis=1, keepdims=True)
            summed = jnp.dot(weights.astype(jnp.bfloat16), v_pair, preferred_element_type=jnp.float32)
            part = summed * (1.0 / total)
            result = part if result is None else jnp.where(in_head, part, result)
        att_ref[:, cols] = result.astype(jnp.bfloat16)

    ow_copy.wait()
    projected = jnp.dot(att_ref[...], ow_vmem[...], preferred_element_type=jnp.float32)
    mid = (x_ref[...].astype(jnp.float32) + projected).astype(jnp.bfloat16)
    mid_ref[...] = mid
    normed = layer_norm(mid.astype(jnp.float32), gain_ref[...]).astype(jnp.bfloat16)
    model_width = mid.shape[1]
    value_copy.wait()
    value_half = jnp.dot(normed, value_w[...], preferred_element_type=jnp.float32)
    gate_half = jnp.dot(normed, gate_w[...], preferred_element_type=jnp.float32)
    gated = (value_half * sigmoid(gate_half)).astype(jnp.bfloat16)
    gated_ref[...] = gated
    half = cross_ref.shape[0]
    cross_ref[...] = gated_ref[pl.ds(pl.multiple_of(core * half, half), half), :]
    partner_ref[...] = gated_ref[pl.ds(pl.multiple_of((1 - core) * half, half), half), :]


def conv_kernel(
    meta_ref, gated_ref, cross_ref, pairg_ref, taps_ref, gain_ref, mid_ref, sw_hbm,
    out_ref, win_ref, conv_ref, sw_vmem, sems,
):
    sw_copy = pltpu.make_async_copy(sw_hbm, sw_vmem, sems.at[0])
    sw_copy.start()
    half = cross_ref.shape[0]
    rows, model_width = mid_ref.shape
    first_core = meta_ref[1] == 0
    cross = cross_ref[...]
    partner = pairg_ref[...]
    win_ref[0:half, :] = jnp.where(first_core, cross, partner).astype(jnp.float32)
    win_ref[half:half + rows, :] = gated_ref[...].astype(jnp.float32)
    win_ref[half + rows:2 * half + rows, :] = jnp.where(first_core, partner, cross).astype(jnp.float32)
    reach = DILATION * (KERNEL - 1) // 2
    start = half - reach

    def chunk(c, carry):
        lanes = pl.ds(pl.multiple_of(c * LANES, LANES), LANES)
        acc = jnp.zeros((rows, LANES), jnp.float32)
        for tap in range(KERNEL):
            first = start + DILATION * tap
            acc = acc + taps_ref[tap:tap + 1, lanes] * win_ref[first:first + rows, lanes]
        conv_ref[:, lanes] = acc
        return carry

    lax.fori_loop(0, model_width // LANES, chunk, 0)
    inner = layer_norm(conv_ref[...], gain_ref[...])
    activated = (inner * sigmoid(inner)).astype(jnp.bfloat16)
    sw_copy.wait()
    shrunk = jnp.dot(activated, sw_vmem[...], preferred_element_type=jnp.float32)
    out_ref[...] = (mid_ref[...].astype(jnp.float32) + shrunk).astype(out_ref.dtype)


def on_device(
    frames_in,
    query_proj,
    key_proj,
    value_proj,
    utterance_lengths,
    bucket_table,
    bucket_bias,
    out_weight,
    norm_gain,
    expand_weight,
    depth_taps,
    inner_gain,
    shrink_weight,
):
    rows, att_width = query_proj.shape
    model_width = frames_in.shape[1]
    heads = bucket_bias.shape[1]
    core = lax.axis_index("core")
    cores = lax.axis_size("core")
    count = lax.axis_size("chip") * cores
    device_index = lax.axis_index("chip") * cores + core
    meta = jnp.stack([device_index * rows, core]).astype(jnp.int32)

    def lin_shift(value, steps):
        leading, last = (max(0, -steps), min(count, count - steps))
        return lax.ppermute(value, ("chip", "core"), [(s, s + steps) for s in range(leading, last)])

    line_len = -(-bucket_table.shape[0] // LANES) * LANES
    table = jnp.pad(bucket_table, (0, line_len - bucket_table.shape[0])).reshape(1, line_len)
    bias_t = bucket_bias.T

    packed = jnp.stack([key_proj, value_proj])
    from_prev = lin_shift(packed, REACH)
    from_next = lin_shift(packed, -REACH)
    swap = [(0, 1), (1, 0)]
    gated_input, table, meta, bias_t, gate_weight = lax.optimization_barrier((packed, table, meta, bias_t, expand_weight[:, model_width:]))
    partner = lax.ppermute(gated_input, "core", swap)
    sel = jnp.where(core == 0, from_next, from_prev)
    partner_sel = lax.ppermute(sel, "core", swap)
    order = list(range(-REACH, REACH + 1))

    half = rows // 2
    vmem = pl.BlockSpec(memory_space=pltpu.VMEM)
    smem = pl.BlockSpec(memory_space=pltpu.SMEM)
    anywhere = pl.BlockSpec(memory_space=pl.ANY)
    window = len(order) * rows
    attn_flops = 2 * 2 * heads * rows * window * LANES + 2 * rows * att_width * model_width + 2 * rows * model_width * 2 * model_width
    attn_bytes = 2 * (rows * att_width * (1 + 2 * len(order)) + rows * model_width * 2 + att_width * model_width + model_width * 2 * model_width)
    mid, gated, cross_send, partner_send = pl.pallas_call(
        attention_kernel,
        out_shape=(
            jax.ShapeDtypeStruct((rows, model_width), jnp.bfloat16),
            jax.ShapeDtypeStruct((rows, model_width), jnp.bfloat16),
            jax.ShapeDtypeStruct((half, model_width), jnp.bfloat16),
            jax.ShapeDtypeStruct((half, model_width), jnp.bfloat16),
        ),
        in_specs=[smem, smem, vmem, vmem, vmem] + [anywhere] * 5 + [vmem, vmem, anywhere, anywhere, vmem],
        out_specs=(vmem, vmem, vmem, vmem),
        scratch_shapes=[
            pltpu.VMEM((att_width, model_width), jnp.bfloat16),
            pltpu.VMEM((model_width, model_width), jnp.bfloat16),
            pltpu.SemaphoreType.DMA((7,)),
            pltpu.VMEM((rows, att_width), jnp.bfloat16),
            pltpu.VMEM((len(order) * packed.shape[0], rows, att_width), jnp.bfloat16),
        ],
        cost_estimate=pl.CostEstimate(
            flops=attn_flops, transcendentals=heads * rows * window + rows * model_width, bytes_accessed=attn_bytes
        ),
        name="attention_glu",
    )(
        meta, utterance_lengths, table, bias_t, query_proj, *[pltpu.with_memory_space_constraint(a, pltpu.VMEM) for a in (from_prev, from_next)], packed, *[pltpu.with_memory_space_constraint(a, pltpu.VMEM) for a in (partner, partner_sel)],
        frames_in, norm_gain.reshape(1, -1), out_weight,
        expand_weight,
        pltpu.with_memory_space_constraint(gate_weight, pltpu.VMEM),
    )

    chips = count // cores
    inward = [(2 * c + 1, 2 * c + 2) for c in range(chips - 1)] + [(2 * c, 2 * c - 1) for c in range(1, chips)]
    cross_recv = lax.ppermute(cross_send, ("chip", "core"), inward)
    partner_recv = lax.ppermute(partner_send, "core", swap)
    conv_flops = 2 * KERNEL * rows * model_width + 2 * rows * model_width * model_width
    conv_bytes = 2 * (4 * half * model_width + rows * model_width * 2 + model_width * model_width) + 4 * KERNEL * model_width
    return pl.pallas_call(
        conv_kernel,
        out_shape=jax.ShapeDtypeStruct((rows, model_width), jnp.bfloat16),
        in_specs=[smem] + [vmem] * 6 + [anywhere],
        out_specs=vmem,
        scratch_shapes=[
            pltpu.VMEM((rows + 2 * half, model_width), jnp.float32),
            pltpu.VMEM((rows, model_width), jnp.float32),
            pltpu.VMEM((model_width, model_width), jnp.bfloat16),
            pltpu.SemaphoreType.DMA((1,)),
        ],
        cost_estimate=pl.CostEstimate(
            flops=conv_flops, transcendentals=rows * model_width, bytes_accessed=conv_bytes
        ),
        name="conv_shrink",
    )(meta, gated, pltpu.with_memory_space_constraint(cross_recv, pltpu.VMEM), pltpu.with_memory_space_constraint(partner_recv, pltpu.VMEM), depth_taps, inner_gain.reshape(1, -1), mid, shrink_weight)


def solution(mesh):
    groups, seq = mesh.devices.shape
    chip_mesh = jax.sharding.Mesh(mesh.devices.reshape(groups, seq // 2, 2), ("groups", "chip", "core"))
    rows_spec = P(("groups", "chip", "core"), None)
    placed = (
        rows_spec,
        rows_spec,
        rows_spec,
        rows_spec,
        P("groups"),
        P(),
        P(),
        P(),
        P(),
        P(),
        P(),
        P(),
        P(),
    )
    return jax.shard_map(
        on_device, mesh=chip_mesh, in_specs=placed, out_specs=rows_spec, check_vma=False
    )
```

```python
import jax
import jax.numpy as jnp
from jax import lax
from jax.experimental import pallas as pl
from jax.experimental.pallas import tpu as pltpu
from jax.sharding import PartitionSpec as P

KERNEL = 31
DILATION = 4
REACH = 2
LANES = 128

norm_epsilon = 1e-05
masked_score = -1e30


def shifted(value, axis, steps):
    count = lax.axis_size(axis)
    leading, last = (max(0, -steps), min(count, count - steps))
    return lax.ppermute(value, axis, [(source, source + steps) for source in range(leading, last)])


def layer_norm(values, gain_vec):
    row_mean = jnp.mean(values, axis=-1, keepdims=True)
    centred = values - row_mean
    spread = jnp.mean(centred * centred, axis=-1, keepdims=True)
    return centred * lax.rsqrt(spread + norm_epsilon) * gain_vec


def sigmoid(values):
    return 1.0 / (1.0 + jnp.exp(-values))


def attention_kernel(
    meta_ref, len_ref, table_ref, bias_t_ref, q_ref,
    prev_hbm, next_hbm, own_hbm, partner_hbm, sel_hbm,
    x_ref, gain_ref, ow_hbm, value_hbm, gate_w,
    mid_ref, cross_ref, partner_ref,
    ow_vmem, value_w, sems, att_ref, win_ref, gated_ref,
):
    base = meta_ref[0]
    core = meta_ref[1]
    planes = prev_hbm.shape[0]
    copies = [
        pltpu.make_async_copy(prev_hbm, win_ref.at[pl.ds(0, planes)], sems.at[2]),
        pltpu.make_async_copy(own_hbm, win_ref.at[pl.ds(2 * planes, planes)], sems.at[3]),
        pltpu.make_async_copy(next_hbm, win_ref.at[pl.ds(4 * planes, planes)], sems.at[4]),
        pltpu.make_async_copy(
            sel_hbm, win_ref.at[pl.ds(pl.multiple_of((1 + 2 * core) * planes, planes), planes)], sems.at[5]
        ),
        pltpu.make_async_copy(
            partner_hbm, win_ref.at[pl.ds(pl.multiple_of((3 - 2 * core) * planes, planes), planes)], sems.at[6]
        ),
    ]
    for copy in copies:
        copy.start()
    ow_copy = pltpu.make_async_copy(ow_hbm, ow_vmem, sems.at[0])
    value_copy = pltpu.make_async_copy(value_hbm.at[:, pl.ds(0, value_w.shape[1])], value_w, sems.at[1])
    ow_copy.start()
    value_copy.start()
    blocks = win_ref.shape[0] // planes
    rows, att_width = q_ref.shape
    heads = bias_t_ref.shape[0]
    buckets = bias_t_ref.shape[1]
    head_width = att_width // heads
    width = blocks * rows
    line_len = table_ref.shape[1]

    qpos = base + lax.broadcasted_iota(jnp.int32, (rows, 1), 0)
    kpos = base - REACH * rows + lax.broadcasted_iota(jnp.int32, (1, width), 1)

    def seg_step(u, carry):
        run, qs, ks = carry
        run = run + len_ref[u]
        return run, qs + (qpos >= run).astype(jnp.int32), ks + (kpos >= run).astype(jnp.int32)

    _, qseg, kseg = lax.fori_loop(
        0, len_ref.shape[0], seg_step,
        (jnp.int32(0), jnp.zeros((rows, 1), jnp.int32), jnp.zeros((1, width), jnp.int32)),
    )
    kseg = jnp.where(kpos < 0, -1, kseg)
    same = qseg == kseg

    table = table_ref[...]
    bias_t = bias_t_ref[...]
    line = jnp.zeros((heads, line_len), jnp.float32)
    for b in range(buckets):
        line = jnp.where(table == b, bias_t[:, b:b + 1], line)

    for copy in copies:
        copy.wait()
    scaling = head_width ** (-0.5)
    lane = lax.broadcasted_iota(jnp.int32, (rows, LANES), 1)
    per_pair = LANES // head_width
    for pair in range(att_width // LANES):
        cols = slice(pair * LANES, (pair + 1) * LANES)
        q_pair = q_ref[:, cols]
        k_pair = jnp.concatenate([win_ref[planes * j, :, cols] for j in range(blocks)], axis=0)
        v_pair = jnp.concatenate([win_ref[planes * j + 1, :, cols] for j in range(blocks)], axis=0)
        result = None
        for sub in range(per_pair):
            head = pair * per_pair + sub
            in_head = (lane >= sub * head_width) & (lane < (sub + 1) * head_width)
            q_head = jnp.where(in_head, q_pair, jnp.zeros_like(q_pair))
            spread = jnp.broadcast_to(line[head:head + 1, :], (rows, line_len))
            skew = pltpu.roll(spread, line_len - rows + 1, 1, stride=1, stride_axis=0)[:, :width]
            bias = jnp.where(same, skew, masked_score)
            scores = lax.dot_general(
                q_head, k_pair, (((1,), (1,)), ((), ())), preferred_element_type=jnp.float32
            )
            scores = scores * scaling + bias
            top = jnp.max(scores, axis=1, keepdims=True)
            weights = jnp.exp(scores - top)
            total = jnp.sum(weights, axis=1, keepdims=True)
            summed = jnp.dot(weights.astype(jnp.bfloat16), v_pair, preferred_element_type=jnp.float32)
            part = summed / total
            result = part if result is None else jnp.where(in_head, part, result)
        att_ref[:, cols] = result.astype(jnp.bfloat16)

    ow_copy.wait()
    projected = jnp.dot(att_ref[...], ow_vmem[...], preferred_element_type=jnp.float32)
    mid = (x_ref[...].astype(jnp.float32) + projected).astype(jnp.bfloat16)
    mid_ref[...] = mid
    normed = layer_norm(mid.astype(jnp.float32), gain_ref[...]).astype(jnp.bfloat16)
    model_width = mid.shape[1]
    value_copy.wait()
    value_half = jnp.dot(normed, value_w[...], preferred_element_type=jnp.float32)
    gate_half = jnp.dot(normed, gate_w[...], preferred_element_type=jnp.float32)
    gated = (value_half * sigmoid(gate_half)).astype(jnp.bfloat16)
    gated_ref[...] = gated
    half = cross_ref.shape[0]
    cross_ref[...] = gated_ref[pl.ds(pl.multiple_of(core * half, half), half), :]
    partner_ref[...] = gated_ref[pl.ds(pl.multiple_of((1 - core) * half, half), half), :]


def conv_kernel(
    meta_ref, own_cross_ref, own_partner_ref, cross_ref, pairg_ref, taps_ref, gain_ref, mid_ref, sw_hbm,
    out_ref, win_ref, conv_ref, sw_vmem, sems,
):
    sw_copy = pltpu.make_async_copy(sw_hbm, sw_vmem, sems.at[0])
    sw_copy.start()
    half = cross_ref.shape[0]
    rows, model_width = mid_ref.shape
    first_core = meta_ref[1] == 0
    cross = cross_ref[...]
    partner = pairg_ref[...]
    win_ref[0:half, :] = jnp.where(first_core, cross, partner).astype(jnp.float32)
    own_cross = own_cross_ref[...]
    own_partner = own_partner_ref[...]
    win_ref[half:2 * half, :] = jnp.where(first_core, own_cross, own_partner).astype(jnp.float32)
    win_ref[2 * half:3 * half, :] = jnp.where(first_core, own_partner, own_cross).astype(jnp.float32)
    win_ref[half + rows:2 * half + rows, :] = jnp.where(first_core, partner, cross).astype(jnp.float32)
    reach = DILATION * (KERNEL - 1) // 2
    start = half - reach

    def chunk(c, carry):
        lanes = pl.ds(pl.multiple_of(c * LANES, LANES), LANES)
        acc = jnp.zeros((rows, LANES), jnp.float32)
        for tap in range(KERNEL):
            first = start + DILATION * tap
            acc = acc + taps_ref[tap:tap + 1, lanes] * win_ref[first:first + rows, lanes]
        conv_ref[:, lanes] = acc
        return carry

    lax.fori_loop(0, model_width // LANES, chunk, 0)
    inner = layer_norm(conv_ref[...], gain_ref[...])
    activated = (inner * sigmoid(inner)).astype(jnp.bfloat16)
    sw_copy.wait()
    shrunk = jnp.dot(activated, sw_vmem[...], preferred_element_type=jnp.float32)
    out_ref[...] = (mid_ref[...].astype(jnp.float32) + shrunk).astype(out_ref.dtype)


def on_device(
    frames_in,
    query_proj,
    key_proj,
    value_proj,
    utterance_lengths,
    bucket_table,
    bucket_bias,
    out_weight,
    norm_gain,
    expand_weight,
    depth_taps,
    inner_gain,
    shrink_weight,
):
    rows, att_width = query_proj.shape
    model_width = frames_in.shape[1]
    heads = bucket_bias.shape[1]
    core = lax.axis_index("core")
    cores = lax.axis_size("core")
    count = lax.axis_size("chip") * cores
    device_index = lax.axis_index("chip") * cores + core
    meta = jnp.stack([device_index * rows, core]).astype(jnp.int32)

    def lin_shift(value, steps):
        leading, last = (max(0, -steps), min(count, count - steps))
        return lax.ppermute(value, ("chip", "core"), [(s, s + steps) for s in range(leading, last)])

    line_len = -(-bucket_table.shape[0] // LANES) * LANES
    table = jnp.pad(bucket_table, (0, line_len - bucket_table.shape[0])).reshape(1, line_len)
    bias_t = bucket_bias.T

    packed = jnp.stack([key_proj, value_proj])
    from_prev = lin_shift(packed, REACH)
    from_next = lin_shift(packed, -REACH)
    swap = [(0, 1), (1, 0)]
    gated_input, table, meta, bias_t, gate_weight = lax.optimization_barrier((packed, table, meta, bias_t, expand_weight[:, model_width:]))
    partner = lax.ppermute(gated_input, "core", swap)
    sel = jnp.where(core == 0, from_next, from_prev)
    partner_sel = lax.ppermute(sel, "core", swap)
    order = list(range(-REACH, REACH + 1))

    half = rows // 2
    vmem = pl.BlockSpec(memory_space=pltpu.VMEM)
    smem = pl.BlockSpec(memory_space=pltpu.SMEM)
    anywhere = pl.BlockSpec(memory_space=pl.ANY)
    window = len(order) * rows
    attn_flops = 2 * 2 * heads * rows * window * LANES + 2 * rows * att_width * model_width + 2 * rows * model_width * 2 * model_width
    attn_bytes = 2 * (rows * att_width * (1 + 2 * len(order)) + rows * model_width * 2 + att_width * model_width + model_width * 2 * model_width)
    mid, cross_send, partner_send = pl.pallas_call(
        attention_kernel,
        out_shape=(
            jax.ShapeDtypeStruct((rows, model_width), jnp.bfloat16),
            jax.ShapeDtypeStruct((half, model_width), jnp.bfloat16),
            jax.ShapeDtypeStruct((half, model_width), jnp.bfloat16),
        ),
        in_specs=[smem, smem, vmem, vmem, vmem] + [anywhere] * 5 + [vmem, vmem, anywhere, anywhere, vmem],
        out_specs=(vmem, vmem, vmem),
        scratch_shapes=[
            pltpu.VMEM((att_width, model_width), jnp.bfloat16),
            pltpu.VMEM((model_width, model_width), jnp.bfloat16),
            pltpu.SemaphoreType.DMA((7,)),
            pltpu.VMEM((rows, att_width), jnp.bfloat16),
            pltpu.VMEM((len(order) * packed.shape[0], rows, att_width), jnp.bfloat16),
            pltpu.VMEM((rows, model_width), jnp.bfloat16),
        ],
        cost_estimate=pl.CostEstimate(
            flops=attn_flops, transcendentals=heads * rows * window + rows * model_width, bytes_accessed=attn_bytes
        ),
        name="attention_glu",
    )(
        meta, utterance_lengths, table, bias_t, query_proj, *[pltpu.with_memory_space_constraint(a, pltpu.VMEM) for a in (from_prev, from_next)], packed, *[pltpu.with_memory_space_constraint(a, pltpu.VMEM) for a in (partner, partner_sel)],
        frames_in, norm_gain.reshape(1, -1), out_weight,
        expand_weight,
        pltpu.with_memory_space_constraint(gate_weight, pltpu.VMEM),
    )

    chips = count // cores
    inward = [(2 * c + 1, 2 * c + 2) for c in range(chips - 1)] + [(2 * c, 2 * c - 1) for c in range(1, chips)]
    cross_recv = lax.ppermute(cross_send, ("chip", "core"), inward)
    partner_recv = lax.ppermute(partner_send, "core", swap)
    conv_flops = 2 * KERNEL * rows * model_width + 2 * rows * model_width * model_width
    conv_bytes = 2 * (4 * half * model_width + rows * model_width * 2 + model_width * model_width) + 4 * KERNEL * model_width
    return pl.pallas_call(
        conv_kernel,
        out_shape=jax.ShapeDtypeStruct((rows, model_width), jnp.bfloat16),
        in_specs=[smem] + [vmem] * 7 + [anywhere],
        out_specs=vmem,
        scratch_shapes=[
            pltpu.VMEM((rows + 2 * half, model_width), jnp.float32),
            pltpu.VMEM((rows, model_width), jnp.float32),
            pltpu.VMEM((model_width, model_width), jnp.bfloat16),
            pltpu.SemaphoreType.DMA((1,)),
        ],
        cost_estimate=pl.CostEstimate(
            flops=conv_flops, transcendentals=rows * model_width, bytes_accessed=conv_bytes
        ),
        name="conv_shrink",
    )(meta, cross_send, partner_send, pltpu.with_memory_space_constraint(cross_recv, pltpu.VMEM), pltpu.with_memory_space_constraint(partner_recv, pltpu.VMEM), depth_taps, inner_gain.reshape(1, -1), mid, shrink_weight)


def solution(mesh):
    groups, seq = mesh.devices.shape
    chip_mesh = jax.sharding.Mesh(mesh.devices.reshape(groups, seq // 2, 2), ("groups", "chip", "core"))
    rows_spec = P(("groups", "chip", "core"), None)
    placed = (
        rows_spec,
        rows_spec,
        rows_spec,
        rows_spec,
        P("groups"),
        P(),
        P(),
        P(),
        P(),
        P(),
        P(),
        P(),
        P(),
    )
    return jax.shard_map(
        on_device, mesh=chip_mesh, in_specs=placed, out_specs=rows_spec, check_vma=False
    )
```

```python
import jax
import jax.numpy as jnp
from jax import lax
from jax.experimental import pallas as pl
from jax.experimental.pallas import tpu as pltpu
from jax.sharding import PartitionSpec as P

KERNEL = 31
DILATION = 4
REACH = 2
LANES = 128

norm_epsilon = 1e-05
masked_score = -1e30


def shifted(value, axis, steps):
    count = lax.axis_size(axis)
    leading, last = (max(0, -steps), min(count, count - steps))
    return lax.ppermute(value, axis, [(source, source + steps) for source in range(leading, last)])


def layer_norm(values, gain_vec):
    row_mean = jnp.mean(values, axis=-1, keepdims=True)
    centred = values - row_mean
    spread = jnp.mean(centred * centred, axis=-1, keepdims=True)
    return centred * lax.rsqrt(spread + norm_epsilon) * gain_vec


def sigmoid(values):
    return 1.0 / (1.0 + jnp.exp(-values))


def attention_kernel(
    meta_ref, len_ref, table_ref, bias_t_ref, q_ref,
    prev_hbm, next_hbm, own_hbm, partner_hbm, sel_hbm,
    x_ref, gain_ref, ow_hbm, value_hbm, gate_w,
    mid_ref, cross_ref, partner_ref,
    ow_vmem, value_w, sems, att_ref, win_ref, gated_ref,
):
    base = meta_ref[0]
    core = meta_ref[1]
    planes = prev_hbm.shape[0]
    copies = [
        pltpu.make_async_copy(prev_hbm, win_ref.at[pl.ds(0, planes)], sems.at[2]),
        pltpu.make_async_copy(own_hbm, win_ref.at[pl.ds(2 * planes, planes)], sems.at[3]),
        pltpu.make_async_copy(next_hbm, win_ref.at[pl.ds(4 * planes, planes)], sems.at[4]),
        pltpu.make_async_copy(
            sel_hbm, win_ref.at[pl.ds(pl.multiple_of((1 + 2 * core) * planes, planes), planes)], sems.at[5]
        ),
        pltpu.make_async_copy(
            partner_hbm, win_ref.at[pl.ds(pl.multiple_of((3 - 2 * core) * planes, planes), planes)], sems.at[6]
        ),
    ]
    for copy in copies:
        copy.start()
    ow_copy = pltpu.make_async_copy(ow_hbm, ow_vmem, sems.at[0])
    value_copy = pltpu.make_async_copy(value_hbm.at[:, pl.ds(0, value_w.shape[1])], value_w, sems.at[1])
    ow_copy.start()
    value_copy.start()
    blocks = win_ref.shape[0] // planes
    rows, att_width = q_ref.shape
    heads = bias_t_ref.shape[0]
    buckets = bias_t_ref.shape[1]
    head_width = att_width // heads
    width = blocks * rows
    line_len = table_ref.shape[1]

    qpos = base + lax.broadcasted_iota(jnp.int32, (rows, 1), 0)
    kpos = base - REACH * rows + lax.broadcasted_iota(jnp.int32, (1, width), 1)

    def seg_step(u, carry):
        run, qs, ks = carry
        run = run + len_ref[u]
        return run, qs + (qpos >= run).astype(jnp.int32), ks + (kpos >= run).astype(jnp.int32)

    _, qseg, kseg = lax.fori_loop(
        0, len_ref.shape[0], seg_step,
        (jnp.int32(0), jnp.zeros((rows, 1), jnp.int32), jnp.zeros((1, width), jnp.int32)),
    )
    kseg = jnp.where(kpos < 0, -1, kseg)
    same = qseg == kseg

    table = table_ref[...]
    bias_t = bias_t_ref[...]
    line = jnp.zeros((heads, line_len), jnp.float32)
    for b in range(buckets):
        line = jnp.where(table == b, bias_t[:, b:b + 1], line)

    for copy in copies:
        copy.wait()
    scaling = head_width ** (-0.5)
    lane = lax.broadcasted_iota(jnp.int32, (rows, LANES), 1)
    per_pair = LANES // head_width
    for pair in range(att_width // LANES):
        cols = slice(pair * LANES, (pair + 1) * LANES)
        q_pair = q_ref[:, cols]
        k_pair = jnp.concatenate([win_ref[planes * j, :, cols] for j in range(blocks)], axis=0)
        v_pair = jnp.concatenate([win_ref[planes * j + 1, :, cols] for j in range(blocks)], axis=0)
        result = None
        for sub in range(per_pair):
            head = pair * per_pair + sub
            in_head = (lane >= sub * head_width) & (lane < (sub + 1) * head_width)
            q_head = jnp.where(in_head, q_pair, jnp.zeros_like(q_pair))
            spread = jnp.broadcast_to(line[head:head + 1, :], (rows, line_len))
            skew = pltpu.roll(spread, line_len - rows + 1, 1, stride=1, stride_axis=0)[:, :width]
            bias = jnp.where(same, skew, masked_score)
            scores = lax.dot_general(
                q_head, k_pair, (((1,), (1,)), ((), ())), preferred_element_type=jnp.float32
            )
            scores = scores * scaling + bias
            top = jnp.max(scores, axis=1, keepdims=True)
            weights = jnp.exp(scores - top)
            total = jnp.sum(weights, axis=1, keepdims=True)
            summed = jnp.dot(weights.astype(jnp.bfloat16), v_pair, preferred_element_type=jnp.float32)
            part = summed / total
            result = part if result is None else jnp.where(in_head, part, result)
        att_ref[:, cols] = result.astype(jnp.bfloat16)

    ow_copy.wait()
    projected = jnp.dot(att_ref[...], ow_vmem[...], preferred_element_type=jnp.float32)
    mid = (x_ref[...].astype(jnp.float32) + projected).astype(jnp.bfloat16)
    mid_ref[...] = mid
    normed = layer_norm(mid.astype(jnp.float32), gain_ref[...]).astype(jnp.bfloat16)
    model_width = mid.shape[1]
    value_copy.wait()
    value_half = jnp.dot(normed, value_w[...], preferred_element_type=jnp.float32)
    gate_half = jnp.dot(normed, gate_w[...], preferred_element_type=jnp.float32)
    gated = (value_half * sigmoid(gate_half)).astype(jnp.bfloat16)
    gated_ref[...] = gated
    half = cross_ref.shape[0]
    cross_ref[...] = gated_ref[pl.ds(pl.multiple_of(core * half, half), half), :]
    partner_ref[...] = gated_ref[pl.ds(pl.multiple_of((1 - core) * half, half), half), :]


def conv_kernel(
    meta_ref, own_cross_ref, own_partner_ref, cross_ref, pairg_ref, taps_ref, gain_ref, mid_ref, sw_hbm,
    out_ref, win_ref, conv_ref, sw_vmem, sems,
):
    sw_copy = pltpu.make_async_copy(sw_hbm, sw_vmem, sems.at[0])
    sw_copy.start()
    half = cross_ref.shape[0]
    rows, model_width = mid_ref.shape
    first_core = meta_ref[1] == 0
    cross = cross_ref[...]
    partner = pairg_ref[...]
    win_ref[0:half, :] = jnp.where(first_core, cross, partner).astype(jnp.float32)
    own_cross = own_cross_ref[...]
    own_partner = own_partner_ref[...]
    win_ref[half:2 * half, :] = jnp.where(first_core, own_cross, own_partner).astype(jnp.float32)
    win_ref[2 * half:3 * half, :] = jnp.where(first_core, own_partner, own_cross).astype(jnp.float32)
    win_ref[half + rows:2 * half + rows, :] = jnp.where(first_core, partner, cross).astype(jnp.float32)
    reach = DILATION * (KERNEL - 1) // 2
    start = half - reach

    def chunk(c, carry):
        lanes = pl.ds(pl.multiple_of(c * LANES, LANES), LANES)
        acc = jnp.zeros((rows, LANES), jnp.float32)
        for tap in range(KERNEL):
            first = start + DILATION * tap
            acc = acc + taps_ref[tap:tap + 1, lanes] * win_ref[first:first + rows, lanes]
        conv_ref[:, lanes] = acc
        return carry

    lax.fori_loop(0, model_width // LANES, chunk, 0)
    inner = layer_norm(conv_ref[...], gain_ref[...])
    activated = (inner * sigmoid(inner)).astype(jnp.bfloat16)
    sw_copy.wait()
    shrunk = jnp.dot(activated, sw_vmem[...], preferred_element_type=jnp.float32)
    out_ref[...] = (mid_ref[...].astype(jnp.float32) + shrunk).astype(out_ref.dtype)


def on_device(
    frames_in,
    query_proj,
    key_proj,
    value_proj,
    utterance_lengths,
    bucket_table,
    bucket_bias,
    out_weight,
    norm_gain,
    expand_weight,
    depth_taps,
    inner_gain,
    shrink_weight,
):
    rows, att_width = query_proj.shape
    model_width = frames_in.shape[1]
    heads = bucket_bias.shape[1]
    core = lax.axis_index("core")
    cores = lax.axis_size("core")
    count = lax.axis_size("chip") * cores
    device_index = lax.axis_index("chip") * cores + core
    meta = jnp.stack([device_index * rows, core]).astype(jnp.int32)

    def lin_shift(value, steps):
        leading, last = (max(0, -steps), min(count, count - steps))
        return lax.ppermute(value, ("chip", "core"), [(s, s + steps) for s in range(leading, last)])

    line_len = -(-bucket_table.shape[0] // LANES) * LANES
    table = jnp.pad(bucket_table, (0, line_len - bucket_table.shape[0])).reshape(1, line_len)
    bias_t = bucket_bias.T

    packed = jnp.stack([key_proj, value_proj])
    from_prev = lin_shift(packed, REACH)
    from_next = lin_shift(packed, -REACH)
    swap = [(0, 1), (1, 0)]
    gated_input, table, meta, bias_t, gate_weight = lax.optimization_barrier((packed, table, meta, bias_t, expand_weight[:, model_width:]))
    partner = lax.ppermute(gated_input, "core", swap)
    sel = jnp.where(core == 0, from_next, from_prev)
    partner_sel = lax.ppermute(sel, "core", swap)
    order = list(range(-REACH, REACH + 1))

    half = rows // 2
    vmem = pl.BlockSpec(memory_space=pltpu.VMEM)
    smem = pl.BlockSpec(memory_space=pltpu.SMEM)
    anywhere = pl.BlockSpec(memory_space=pl.ANY)
    window = len(order) * rows
    attn_flops = 2 * 2 * heads * rows * window * LANES + 2 * rows * att_width * model_width + 2 * rows * model_width * 2 * model_width
    attn_bytes = 2 * (rows * att_width * (1 + 2 * len(order)) + rows * model_width * 2 + att_width * model_width + model_width * 2 * model_width)
    mid, cross_send, partner_send = pl.pallas_call(
        attention_kernel,
        out_shape=(
            jax.ShapeDtypeStruct((rows, model_width), jnp.bfloat16),
            jax.ShapeDtypeStruct((half, model_width), jnp.bfloat16),
            jax.ShapeDtypeStruct((half, model_width), jnp.bfloat16),
        ),
        in_specs=[smem, smem, vmem, vmem, vmem] + [anywhere] * 5 + [vmem, vmem, anywhere, anywhere, vmem],
        out_specs=(vmem, vmem, vmem),
        scratch_shapes=[
            pltpu.VMEM((att_width, model_width), jnp.bfloat16),
            pltpu.VMEM((model_width, model_width), jnp.bfloat16),
            pltpu.SemaphoreType.DMA((7,)),
            pltpu.VMEM((rows, att_width), jnp.bfloat16),
            pltpu.VMEM((len(order) * packed.shape[0], rows, att_width), jnp.bfloat16),
            pltpu.VMEM((rows, model_width), jnp.bfloat16),
        ],
        cost_estimate=pl.CostEstimate(
            flops=attn_flops, transcendentals=heads * rows * window + rows * model_width, bytes_accessed=attn_bytes
        ),
        name="attention_glu",
    )(
        meta, utterance_lengths, table, bias_t, query_proj, *[pltpu.with_memory_space_constraint(a, pltpu.VMEM) for a in (from_prev, from_next)], packed, *[pltpu.with_memory_space_constraint(a, pltpu.VMEM) for a in (partner, partner_sel)],
        frames_in, norm_gain.reshape(1, -1), out_weight,
        expand_weight,
        pltpu.with_memory_space_constraint(gate_weight, pltpu.VMEM),
    )

    chips = count // cores
    inward = [(2 * c + 1, 2 * c + 2) for c in range(chips - 1)] + [(2 * c, 2 * c - 1) for c in range(1, chips)]
    cross_recv = lax.ppermute(cross_send, ("chip", "core"), inward)
    partner_recv = lax.ppermute(partner_send, "core", swap)
    conv_flops = 2 * KERNEL * rows * model_width + 2 * rows * model_width * model_width
    conv_bytes = 2 * (4 * half * model_width + rows * model_width * 2 + model_width * model_width) + 4 * KERNEL * model_width
    return pl.pallas_call(
        conv_kernel,
        out_shape=jax.ShapeDtypeStruct((rows, model_width), jnp.bfloat16),
        in_specs=[smem] + [vmem] * 7 + [anywhere],
        out_specs=vmem,
        scratch_shapes=[
            pltpu.VMEM((rows + 2 * half, model_width), jnp.float32),
            pltpu.VMEM((rows, model_width), jnp.float32),
            pltpu.VMEM((model_width, model_width), jnp.bfloat16),
            pltpu.SemaphoreType.DMA((1,)),
        ],
        cost_estimate=pl.CostEstimate(
            flops=conv_flops, transcendentals=rows * model_width, bytes_accessed=conv_bytes
        ),
        name="conv_shrink",
    )(meta, cross_send, partner_send, pltpu.with_memory_space_constraint(cross_recv, pltpu.VMEM), pltpu.with_memory_space_constraint(partner_recv, pltpu.VMEM), pltpu.with_memory_space_constraint(depth_taps, pltpu.VMEM), pltpu.with_memory_space_constraint(inner_gain.reshape(1, -1), pltpu.VMEM), mid, shrink_weight)


def solution(mesh):
    groups, seq = mesh.devices.shape
    chip_mesh = jax.sharding.Mesh(mesh.devices.reshape(groups, seq // 2, 2), ("groups", "chip", "core"))
    rows_spec = P(("groups", "chip", "core"), None)
    placed = (
        rows_spec,
        rows_spec,
        rows_spec,
        rows_spec,
        P("groups"),
        P(),
        P(),
        P(),
        P(),
        P(),
        P(),
        P(),
        P(),
    )
    return jax.shard_map(
        on_device, mesh=chip_mesh, in_specs=placed, out_specs=rows_spec, check_vma=False
    )
```

```python
import jax
import jax.numpy as jnp
from jax import lax
from jax.experimental import pallas as pl
from jax.experimental.pallas import tpu as pltpu
from jax.sharding import PartitionSpec as P

KERNEL = 31
DILATION = 4
REACH = 2
LANES = 128

norm_epsilon = 1e-05
masked_score = -1e30


def shifted(value, axis, steps):
    count = lax.axis_size(axis)
    leading, last = (max(0, -steps), min(count, count - steps))
    return lax.ppermute(value, axis, [(source, source + steps) for source in range(leading, last)])


def layer_norm(values, gain_vec):
    row_mean = jnp.mean(values, axis=-1, keepdims=True)
    centred = values - row_mean
    spread = jnp.mean(centred * centred, axis=-1, keepdims=True)
    return centred * lax.rsqrt(spread + norm_epsilon) * gain_vec


def sigmoid(values):
    return 1.0 / (1.0 + jnp.exp(-values))


def attention_kernel(
    meta_ref, len_ref, table_ref, bias_t_ref, q_ref,
    prev_hbm, next_hbm, own_hbm, partner_hbm, sel_hbm,
    x_ref, gain_ref, ow_hbm, value_hbm, gate_w,
    mid_ref, cross_ref, partner_ref,
    ow_vmem, value_w, sems, att_ref, win_ref, gated_ref,
):
    base = meta_ref[0]
    core = meta_ref[1]
    planes = prev_hbm.shape[0]
    copies = [
        pltpu.make_async_copy(prev_hbm, win_ref.at[pl.ds(0, planes)], sems.at[2]),
        pltpu.make_async_copy(own_hbm, win_ref.at[pl.ds(2 * planes, planes)], sems.at[3]),
        pltpu.make_async_copy(next_hbm, win_ref.at[pl.ds(4 * planes, planes)], sems.at[4]),
        pltpu.make_async_copy(
            sel_hbm, win_ref.at[pl.ds(pl.multiple_of((1 + 2 * core) * planes, planes), planes)], sems.at[5]
        ),
        pltpu.make_async_copy(
            partner_hbm, win_ref.at[pl.ds(pl.multiple_of((3 - 2 * core) * planes, planes), planes)], sems.at[6]
        ),
    ]
    for copy in copies:
        copy.start()
    ow_copy = pltpu.make_async_copy(ow_hbm, ow_vmem, sems.at[0])
    value_copy = pltpu.make_async_copy(value_hbm.at[:, pl.ds(0, value_w.shape[1])], value_w, sems.at[1])
    ow_copy.start()
    value_copy.start()
    blocks = win_ref.shape[0] // planes
    rows, att_width = q_ref.shape
    heads = bias_t_ref.shape[0]
    buckets = bias_t_ref.shape[1]
    head_width = att_width // heads
    width = blocks * rows
    line_len = table_ref.shape[1]

    qpos = base + lax.broadcasted_iota(jnp.int32, (rows, 1), 0)
    kpos = base - REACH * rows + lax.broadcasted_iota(jnp.int32, (1, width), 1)

    def seg_step(u, carry):
        run, qs, ks = carry
        run = run + len_ref[u]
        return run, qs + (qpos >= run).astype(jnp.int32), ks + (kpos >= run).astype(jnp.int32)

    _, qseg, kseg = lax.fori_loop(
        0, len_ref.shape[0], seg_step,
        (jnp.int32(0), jnp.zeros((rows, 1), jnp.int32), jnp.zeros((1, width), jnp.int32)),
    )
    kseg = jnp.where(kpos < 0, -1, kseg)
    same = qseg == kseg

    table = table_ref[...]
    bias_t = bias_t_ref[...]
    line = jnp.zeros((heads, line_len), jnp.float32)
    for b in range(buckets):
        line = jnp.where(table == b, bias_t[:, b:b + 1], line)

    for copy in copies:
        copy.wait()
    scaling = head_width ** (-0.5)
    band = rows // 2
    band_lane = lax.broadcasted_iota(jnp.int32, (band, LANES), 1)
    per_pair = LANES // head_width
    for pair in range(att_width // LANES):
        cols = slice(pair * LANES, (pair + 1) * LANES)
        q_pair = q_ref[:, cols]
        k_pair = jnp.concatenate([win_ref[planes * j, :, cols] for j in range(blocks)], axis=0)
        v_pair = jnp.concatenate([win_ref[planes * j + 1, :, cols] for j in range(blocks)], axis=0)
        for first in range(0, rows, band):
            band_rows = slice(first, first + band)
            result = None
            for sub in range(per_pair):
                head = pair * per_pair + sub
                in_head = (band_lane >= sub * head_width) & (band_lane < (sub + 1) * head_width)
                q_head = jnp.where(in_head, q_pair[band_rows], jnp.zeros_like(q_pair[band_rows]))
                spread = jnp.broadcast_to(line[head:head + 1, :], (band, line_len))
                skew = pltpu.roll(spread, (line_len - rows + 1 + first) % line_len, 1, stride=1, stride_axis=0)[:, :width]
                bias = jnp.where(same[band_rows], skew, masked_score)
                scores = lax.dot_general(
                    q_head, k_pair, (((1,), (1,)), ((), ())), preferred_element_type=jnp.float32
                )
                scores = scores * scaling + bias
                top = jnp.max(scores, axis=1, keepdims=True)
                weights = jnp.exp(scores - top)
                total = jnp.sum(weights, axis=1, keepdims=True)
                summed = jnp.dot(weights.astype(jnp.bfloat16), v_pair, preferred_element_type=jnp.float32)
                part = summed / total
                result = part if result is None else jnp.where(in_head, part, result)
            att_ref[band_rows, cols] = result.astype(jnp.bfloat16)

    ow_copy.wait()
    projected = jnp.dot(att_ref[...], ow_vmem[...], preferred_element_type=jnp.float32)
    mid = (x_ref[...].astype(jnp.float32) + projected).astype(jnp.bfloat16)
    mid_ref[...] = mid
    normed = layer_norm(mid.astype(jnp.float32), gain_ref[...]).astype(jnp.bfloat16)
    model_width = mid.shape[1]
    value_copy.wait()
    value_half = jnp.dot(normed, value_w[...], preferred_element_type=jnp.float32)
    gate_half = jnp.dot(normed, gate_w[...], preferred_element_type=jnp.float32)
    gated = (value_half * sigmoid(gate_half)).astype(jnp.bfloat16)
    gated_ref[...] = gated
    half = cross_ref.shape[0]
    cross_ref[...] = gated_ref[pl.ds(pl.multiple_of(core * half, half), half), :]
    partner_ref[...] = gated_ref[pl.ds(pl.multiple_of((1 - core) * half, half), half), :]


def conv_kernel(
    meta_ref, own_cross_ref, own_partner_ref, cross_ref, pairg_ref, taps_ref, gain_ref, mid_ref, sw_hbm,
    out_ref, win_ref, conv_ref, sw_vmem, sems,
):
    sw_copy = pltpu.make_async_copy(sw_hbm, sw_vmem, sems.at[0])
    sw_copy.start()
    half = cross_ref.shape[0]
    rows, model_width = mid_ref.shape
    first_core = meta_ref[1] == 0
    cross = cross_ref[...]
    partner = pairg_ref[...]
    win_ref[0:half, :] = jnp.where(first_core, cross, partner).astype(jnp.float32)
    own_cross = own_cross_ref[...]
    own_partner = own_partner_ref[...]
    win_ref[half:2 * half, :] = jnp.where(first_core, own_cross, own_partner).astype(jnp.float32)
    win_ref[2 * half:3 * half, :] = jnp.where(first_core, own_partner, own_cross).astype(jnp.float32)
    win_ref[half + rows:2 * half + rows, :] = jnp.where(first_core, partner, cross).astype(jnp.float32)
    reach = DILATION * (KERNEL - 1) // 2
    start = half - reach

    def chunk(c, carry):
        lanes = pl.ds(pl.multiple_of(c * LANES, LANES), LANES)
        acc = jnp.zeros((rows, LANES), jnp.float32)
        for tap in range(KERNEL):
            first = start + DILATION * tap
            acc = acc + taps_ref[tap:tap + 1, lanes] * win_ref[first:first + rows, lanes]
        conv_ref[:, lanes] = acc
        return carry

    lax.fori_loop(0, model_width // LANES, chunk, 0)
    inner = layer_norm(conv_ref[...], gain_ref[...])
    activated = (inner * sigmoid(inner)).astype(jnp.bfloat16)
    sw_copy.wait()
    shrunk = jnp.dot(activated, sw_vmem[...], preferred_element_type=jnp.float32)
    out_ref[...] = (mid_ref[...].astype(jnp.float32) + shrunk).astype(out_ref.dtype)


def on_device(
    frames_in,
    query_proj,
    key_proj,
    value_proj,
    utterance_lengths,
    bucket_table,
    bucket_bias,
    out_weight,
    norm_gain,
    expand_weight,
    depth_taps,
    inner_gain,
    shrink_weight,
):
    rows, att_width = query_proj.shape
    model_width = frames_in.shape[1]
    heads = bucket_bias.shape[1]
    core = lax.axis_index("core")
    cores = lax.axis_size("core")
    count = lax.axis_size("chip") * cores
    device_index = lax.axis_index("chip") * cores + core
    meta = jnp.stack([device_index * rows, core]).astype(jnp.int32)

    def lin_shift(value, steps):
        leading, last = (max(0, -steps), min(count, count - steps))
        return lax.ppermute(value, ("chip", "core"), [(s, s + steps) for s in range(leading, last)])

    line_len = -(-bucket_table.shape[0] // LANES) * LANES
    table = jnp.pad(bucket_table, (0, line_len - bucket_table.shape[0])).reshape(1, line_len)
    bias_t = bucket_bias.T

    packed = jnp.stack([key_proj, value_proj])
    from_prev = lin_shift(packed, REACH)
    from_next = lin_shift(packed, -REACH)
    swap = [(0, 1), (1, 0)]
    gated_input, table, meta, bias_t, gate_weight = lax.optimization_barrier((packed, table, meta, bias_t, expand_weight[:, model_width:]))
    partner = lax.ppermute(gated_input, "core", swap)
    sel = jnp.where(core == 0, from_next, from_prev)
    partner_sel = lax.ppermute(sel, "core", swap)
    order = list(range(-REACH, REACH + 1))

    half = rows // 2
    vmem = pl.BlockSpec(memory_space=pltpu.VMEM)
    smem = pl.BlockSpec(memory_space=pltpu.SMEM)
    anywhere = pl.BlockSpec(memory_space=pl.ANY)
    window = len(order) * rows
    attn_flops = 2 * 2 * heads * rows * window * LANES + 2 * rows * att_width * model_width + 2 * rows * model_width * 2 * model_width
    attn_bytes = 2 * (rows * att_width * (1 + 2 * len(order)) + rows * model_width * 2 + att_width * model_width + model_width * 2 * model_width)
    mid, cross_send, partner_send = pl.pallas_call(
        attention_kernel,
        out_shape=(
            jax.ShapeDtypeStruct((rows, model_width), jnp.bfloat16),
            jax.ShapeDtypeStruct((half, model_width), jnp.bfloat16),
            jax.ShapeDtypeStruct((half, model_width), jnp.bfloat16),
        ),
        in_specs=[smem, smem, vmem, vmem, vmem] + [anywhere] * 5 + [vmem, vmem, anywhere, anywhere, vmem],
        out_specs=(vmem, vmem, vmem),
        scratch_shapes=[
            pltpu.VMEM((att_width, model_width), jnp.bfloat16),
            pltpu.VMEM((model_width, model_width), jnp.bfloat16),
            pltpu.SemaphoreType.DMA((7,)),
            pltpu.VMEM((rows, att_width), jnp.bfloat16),
            pltpu.VMEM((len(order) * packed.shape[0], rows, att_width), jnp.bfloat16),
            pltpu.VMEM((rows, model_width), jnp.bfloat16),
        ],
        cost_estimate=pl.CostEstimate(
            flops=attn_flops, transcendentals=heads * rows * window + rows * model_width, bytes_accessed=attn_bytes
        ),
        name="attention_glu",
    )(
        meta, utterance_lengths, table, bias_t, query_proj, *[pltpu.with_memory_space_constraint(a, pltpu.VMEM) for a in (from_prev, from_next)], packed, *[pltpu.with_memory_space_constraint(a, pltpu.VMEM) for a in (partner, partner_sel)],
        frames_in, norm_gain.reshape(1, -1), out_weight,
        expand_weight,
        pltpu.with_memory_space_constraint(gate_weight, pltpu.VMEM),
    )

    chips = count // cores
    inward = [(2 * c + 1, 2 * c + 2) for c in range(chips - 1)] + [(2 * c, 2 * c - 1) for c in range(1, chips)]
    cross_recv = lax.ppermute(cross_send, ("chip", "core"), inward)
    partner_recv = lax.ppermute(partner_send, "core", swap)
    conv_flops = 2 * KERNEL * rows * model_width + 2 * rows * model_width * model_width
    conv_bytes = 2 * (4 * half * model_width + rows * model_width * 2 + model_width * model_width) + 4 * KERNEL * model_width
    return pl.pallas_call(
        conv_kernel,
        out_shape=jax.ShapeDtypeStruct((rows, model_width), jnp.bfloat16),
        in_specs=[smem] + [vmem] * 7 + [anywhere],
        out_specs=vmem,
        scratch_shapes=[
            pltpu.VMEM((rows + 2 * half, model_width), jnp.float32),
            pltpu.VMEM((rows, model_width), jnp.float32),
            pltpu.VMEM((model_width, model_width), jnp.bfloat16),
            pltpu.SemaphoreType.DMA((1,)),
        ],
        cost_estimate=pl.CostEstimate(
            flops=conv_flops, transcendentals=rows * model_width, bytes_accessed=conv_bytes
        ),
        name="conv_shrink",
    )(meta, cross_send, partner_send, pltpu.with_memory_space_constraint(cross_recv, pltpu.VMEM), pltpu.with_memory_space_constraint(partner_recv, pltpu.VMEM), pltpu.with_memory_space_constraint(depth_taps, pltpu.VMEM), pltpu.with_memory_space_constraint(inner_gain.reshape(1, -1), pltpu.VMEM), mid, shrink_weight)


def solution(mesh):
    groups, seq = mesh.devices.shape
    chip_mesh = jax.sharding.Mesh(mesh.devices.reshape(groups, seq // 2, 2), ("groups", "chip", "core"))
    rows_spec = P(("groups", "chip", "core"), None)
    placed = (
        rows_spec,
        rows_spec,
        rows_spec,
        rows_spec,
        P("groups"),
        P(),
        P(),
        P(),
        P(),
        P(),
        P(),
        P(),
        P(),
    )
    return jax.shard_map(
        on_device, mesh=chip_mesh, in_specs=placed, out_specs=rows_spec, check_vma=False
    )
```

```python
import jax
import jax.numpy as jnp
from jax import lax
from jax.experimental import pallas as pl
from jax.experimental.pallas import tpu as pltpu
from jax.sharding import PartitionSpec as P

KERNEL = 31
DILATION = 4
REACH = 2
LANES = 128

norm_epsilon = 1e-05
masked_score = -1e30


def shifted(value, axis, steps):
    count = lax.axis_size(axis)
    leading, last = (max(0, -steps), min(count, count - steps))
    return lax.ppermute(value, axis, [(source, source + steps) for source in range(leading, last)])


def layer_norm(values, gain_vec):
    row_mean = jnp.mean(values, axis=-1, keepdims=True)
    centred = values - row_mean
    spread = jnp.mean(centred * centred, axis=-1, keepdims=True)
    return centred * lax.rsqrt(spread + norm_epsilon) * gain_vec


def sigmoid(values):
    return 1.0 / (1.0 + jnp.exp(-values))


def attention_kernel(
    meta_ref, len_ref, table_ref, bias_t_ref, q_ref,
    prev_hbm, next_hbm, own_hbm, partner_hbm, sel_hbm,
    x_ref, gain_ref, ow_hbm, value_hbm, gate_w,
    mid_ref, cross_ref, partner_ref,
    ow_vmem, value_w, sems, att_ref, win_ref, gated_ref,
):
    base = meta_ref[0]
    core = meta_ref[1]
    planes = prev_hbm.shape[0]
    copies = [
        pltpu.make_async_copy(prev_hbm, win_ref.at[pl.ds(0, planes)], sems.at[2]),
        pltpu.make_async_copy(own_hbm, win_ref.at[pl.ds(2 * planes, planes)], sems.at[3]),
        pltpu.make_async_copy(next_hbm, win_ref.at[pl.ds(4 * planes, planes)], sems.at[4]),
        pltpu.make_async_copy(
            sel_hbm, win_ref.at[pl.ds(pl.multiple_of((1 + 2 * core) * planes, planes), planes)], sems.at[5]
        ),
        pltpu.make_async_copy(
            partner_hbm, win_ref.at[pl.ds(pl.multiple_of((3 - 2 * core) * planes, planes), planes)], sems.at[6]
        ),
    ]
    for copy in copies:
        copy.start()
    ow_copy = pltpu.make_async_copy(ow_hbm, ow_vmem, sems.at[0])
    value_copy = pltpu.make_async_copy(value_hbm.at[:, pl.ds(0, value_w.shape[1])], value_w, sems.at[1])
    ow_copy.start()
    value_copy.start()
    blocks = win_ref.shape[0] // planes
    rows, att_width = q_ref.shape
    heads = bias_t_ref.shape[0]
    buckets = bias_t_ref.shape[1]
    head_width = att_width // heads
    width = blocks * rows
    line_len = table_ref.shape[1]

    qpos = base + lax.broadcasted_iota(jnp.int32, (rows, 1), 0)
    kpos = base - REACH * rows + lax.broadcasted_iota(jnp.int32, (1, width), 1)

    def seg_step(u, carry):
        run, qs, ks = carry
        run = run + len_ref[u]
        return run, qs + (qpos >= run).astype(jnp.int32), ks + (kpos >= run).astype(jnp.int32)

    _, qseg, kseg = lax.fori_loop(
        0, len_ref.shape[0], seg_step,
        (jnp.int32(0), jnp.zeros((rows, 1), jnp.int32), jnp.zeros((1, width), jnp.int32)),
    )
    kseg = jnp.where(kpos < 0, -1, kseg)
    same = qseg == kseg

    table = table_ref[...]
    bias_t = bias_t_ref[...]
    line = jnp.zeros((heads, line_len), jnp.float32)
    for b in range(buckets):
        line = jnp.where(table == b, bias_t[:, b:b + 1], line)

    for copy in copies:
        copy.wait()
    scaling = head_width ** (-0.5)
    lane = lax.broadcasted_iota(jnp.int32, (rows, LANES), 1)
    per_pair = LANES // head_width
    for pair in range(att_width // LANES):
        cols = slice(pair * LANES, (pair + 1) * LANES)
        q_pair = q_ref[:, cols]
        k_pair = jnp.concatenate([win_ref[planes * j, :, cols] for j in range(blocks)], axis=0)
        v_pair = jnp.concatenate([win_ref[planes * j + 1, :, cols] for j in range(blocks)], axis=0)
        q_rows, biases, masks = [], [], []
        for sub in range(per_pair):
            head = pair * per_pair + sub
            in_head = (lane >= sub * head_width) & (lane < (sub + 1) * head_width)
            q_rows.append(jnp.where(in_head, q_pair, jnp.zeros_like(q_pair)))
            spread = jnp.broadcast_to(line[head:head + 1, :], (rows, line_len))
            skew = pltpu.roll(spread, line_len - rows + 1, 1, stride=1, stride_axis=0)[:, :width]
            biases.append(jnp.where(same, skew, masked_score))
            masks.append(in_head)
        scores = lax.dot_general(
            jnp.concatenate(q_rows, axis=0), k_pair, (((1,), (1,)), ((), ())), preferred_element_type=jnp.float32
        )
        scores = scores * scaling + jnp.concatenate(biases, axis=0)
        top = jnp.max(scores, axis=1, keepdims=True)
        weights = jnp.exp(scores - top)
        total = jnp.sum(weights, axis=1, keepdims=True)
        summed = jnp.dot(weights.astype(jnp.bfloat16), v_pair, preferred_element_type=jnp.float32)
        part = summed / total
        result = part[0:rows]
        for sub in range(1, per_pair):
            result = jnp.where(masks[sub], part[sub * rows:(sub + 1) * rows], result)
        att_ref[:, cols] = result.astype(jnp.bfloat16)

    ow_copy.wait()
    projected = jnp.dot(att_ref[...], ow_vmem[...], preferred_element_type=jnp.float32)
    mid = (x_ref[...].astype(jnp.float32) + projected).astype(jnp.bfloat16)
    mid_ref[...] = mid
    normed = layer_norm(mid.astype(jnp.float32), gain_ref[...]).astype(jnp.bfloat16)
    model_width = mid.shape[1]
    value_copy.wait()
    value_half = jnp.dot(normed, value_w[...], preferred_element_type=jnp.float32)
    gate_half = jnp.dot(normed, gate_w[...], preferred_element_type=jnp.float32)
    gated = (value_half * sigmoid(gate_half)).astype(jnp.bfloat16)
    gated_ref[...] = gated
    half = cross_ref.shape[0]
    cross_ref[...] = gated_ref[pl.ds(pl.multiple_of(core * half, half), half), :]
    partner_ref[...] = gated_ref[pl.ds(pl.multiple_of((1 - core) * half, half), half), :]


def conv_kernel(
    meta_ref, own_cross_ref, own_partner_ref, cross_ref, pairg_ref, taps_ref, gain_ref, mid_ref, sw_hbm,
    out_ref, win_ref, conv_ref, sw_vmem, sems,
):
    sw_copy = pltpu.make_async_copy(sw_hbm, sw_vmem, sems.at[0])
    sw_copy.start()
    half = cross_ref.shape[0]
    rows, model_width = mid_ref.shape
    first_core = meta_ref[1] == 0
    cross = cross_ref[...]
    partner = pairg_ref[...]
    win_ref[0:half, :] = jnp.where(first_core, cross, partner).astype(jnp.float32)
    own_cross = own_cross_ref[...]
    own_partner = own_partner_ref[...]
    win_ref[half:2 * half, :] = jnp.where(first_core, own_cross, own_partner).astype(jnp.float32)
    win_ref[2 * half:3 * half, :] = jnp.where(first_core, own_partner, own_cross).astype(jnp.float32)
    win_ref[half + rows:2 * half + rows, :] = jnp.where(first_core, partner, cross).astype(jnp.float32)
    reach = DILATION * (KERNEL - 1) // 2
    start = half - reach

    def chunk(c, carry):
        lanes = pl.ds(pl.multiple_of(c * LANES, LANES), LANES)
        acc = jnp.zeros((rows, LANES), jnp.float32)
        for tap in range(KERNEL):
            first = start + DILATION * tap
            acc = acc + taps_ref[tap:tap + 1, lanes] * win_ref[first:first + rows, lanes]
        conv_ref[:, lanes] = acc
        return carry

    lax.fori_loop(0, model_width // LANES, chunk, 0)
    inner = layer_norm(conv_ref[...], gain_ref[...])
    activated = (inner * sigmoid(inner)).astype(jnp.bfloat16)
    sw_copy.wait()
    shrunk = jnp.dot(activated, sw_vmem[...], preferred_element_type=jnp.float32)
    out_ref[...] = (mid_ref[...].astype(jnp.float32) + shrunk).astype(out_ref.dtype)


def on_device(
    frames_in,
    query_proj,
    key_proj,
    value_proj,
    utterance_lengths,
    bucket_table,
    bucket_bias,
    out_weight,
    norm_gain,
    expand_weight,
    depth_taps,
    inner_gain,
    shrink_weight,
):
    rows, att_width = query_proj.shape
    model_width = frames_in.shape[1]
    heads = bucket_bias.shape[1]
    core = lax.axis_index("core")
    cores = lax.axis_size("core")
    count = lax.axis_size("chip") * cores
    device_index = lax.axis_index("chip") * cores + core
    meta = jnp.stack([device_index * rows, core]).astype(jnp.int32)

    def lin_shift(value, steps):
        leading, last = (max(0, -steps), min(count, count - steps))
        return lax.ppermute(value, ("chip", "core"), [(s, s + steps) for s in range(leading, last)])

    line_len = -(-bucket_table.shape[0] // LANES) * LANES
    table = jnp.pad(bucket_table, (0, line_len - bucket_table.shape[0])).reshape(1, line_len)
    bias_t = bucket_bias.T

    packed = jnp.stack([key_proj, value_proj])
    from_prev = lin_shift(packed, REACH)
    from_next = lin_shift(packed, -REACH)
    swap = [(0, 1), (1, 0)]
    gated_input, table, meta, bias_t, gate_weight = lax.optimization_barrier((packed, table, meta, bias_t, expand_weight[:, model_width:]))
    partner = lax.ppermute(gated_input, "core", swap)
    sel = jnp.where(core == 0, from_next, from_prev)
    partner_sel = lax.ppermute(sel, "core", swap)
    order = list(range(-REACH, REACH + 1))

    half = rows // 2
    vmem = pl.BlockSpec(memory_space=pltpu.VMEM)
    smem = pl.BlockSpec(memory_space=pltpu.SMEM)
    anywhere = pl.BlockSpec(memory_space=pl.ANY)
    window = len(order) * rows
    attn_flops = 2 * 2 * heads * rows * window * LANES + 2 * rows * att_width * model_width + 2 * rows * model_width * 2 * model_width
    attn_bytes = 2 * (rows * att_width * (1 + 2 * len(order)) + rows * model_width * 2 + att_width * model_width + model_width * 2 * model_width)
    mid, cross_send, partner_send = pl.pallas_call(
        attention_kernel,
        out_shape=(
            jax.ShapeDtypeStruct((rows, model_width), jnp.bfloat16),
            jax.ShapeDtypeStruct((half, model_width), jnp.bfloat16),
            jax.ShapeDtypeStruct((half, model_width), jnp.bfloat16),
        ),
        in_specs=[smem, smem, vmem, vmem, vmem] + [anywhere] * 5 + [vmem, vmem, anywhere, anywhere, vmem],
        out_specs=(vmem, vmem, vmem),
        scratch_shapes=[
            pltpu.VMEM((att_width, model_width), jnp.bfloat16),
            pltpu.VMEM((model_width, model_width), jnp.bfloat16),
            pltpu.SemaphoreType.DMA((7,)),
            pltpu.VMEM((rows, att_width), jnp.bfloat16),
            pltpu.VMEM((len(order) * packed.shape[0], rows, att_width), jnp.bfloat16),
            pltpu.VMEM((rows, model_width), jnp.bfloat16),
        ],
        cost_estimate=pl.CostEstimate(
            flops=attn_flops, transcendentals=heads * rows * window + rows * model_width, bytes_accessed=attn_bytes
        ),
        name="attention_glu",
    )(
        meta, utterance_lengths, table, bias_t, query_proj, *[pltpu.with_memory_space_constraint(a, pltpu.VMEM) for a in (from_prev, from_next)], packed, *[pltpu.with_memory_space_constraint(a, pltpu.VMEM) for a in (partner, partner_sel)],
        frames_in, norm_gain.reshape(1, -1), out_weight,
        expand_weight,
        pltpu.with_memory_space_constraint(gate_weight, pltpu.VMEM),
    )

    chips = count // cores
    inward = [(2 * c + 1, 2 * c + 2) for c in range(chips - 1)] + [(2 * c, 2 * c - 1) for c in range(1, chips)]
    cross_recv = lax.ppermute(cross_send, ("chip", "core"), inward)
    partner_recv = lax.ppermute(partner_send, "core", swap)
    conv_flops = 2 * KERNEL * rows * model_width + 2 * rows * model_width * model_width
    conv_bytes = 2 * (4 * half * model_width + rows * model_width * 2 + model_width * model_width) + 4 * KERNEL * model_width
    return pl.pallas_call(
        conv_kernel,
        out_shape=jax.ShapeDtypeStruct((rows, model_width), jnp.bfloat16),
        in_specs=[smem] + [vmem] * 7 + [anywhere],
        out_specs=vmem,
        scratch_shapes=[
            pltpu.VMEM((rows + 2 * half, model_width), jnp.float32),
            pltpu.VMEM((rows, model_width), jnp.float32),
            pltpu.VMEM((model_width, model_width), jnp.bfloat16),
            pltpu.SemaphoreType.DMA((1,)),
        ],
        cost_estimate=pl.CostEstimate(
            flops=conv_flops, transcendentals=rows * model_width, bytes_accessed=conv_bytes
        ),
        name="conv_shrink",
    )(meta, cross_send, partner_send, pltpu.with_memory_space_constraint(cross_recv, pltpu.VMEM), pltpu.with_memory_space_constraint(partner_recv, pltpu.VMEM), pltpu.with_memory_space_constraint(depth_taps, pltpu.VMEM), pltpu.with_memory_space_constraint(inner_gain.reshape(1, -1), pltpu.VMEM), mid, shrink_weight)


def solution(mesh):
    groups, seq = mesh.devices.shape
    chip_mesh = jax.sharding.Mesh(mesh.devices.reshape(groups, seq // 2, 2), ("groups", "chip", "core"))
    rows_spec = P(("groups", "chip", "core"), None)
    placed = (
        rows_spec,
        rows_spec,
        rows_spec,
        rows_spec,
        P("groups"),
        P(),
        P(),
        P(),
        P(),
        P(),
        P(),
        P(),
        P(),
    )
    return jax.shard_map(
        on_device, mesh=chip_mesh, in_specs=placed, out_specs=rows_spec, check_vma=False
    )
```

```python
import jax
import jax.numpy as jnp
from jax import lax
from jax.experimental import pallas as pl
from jax.experimental.pallas import tpu as pltpu
from jax.sharding import PartitionSpec as P

KERNEL = 31
DILATION = 4
REACH = 2
LANES = 128

norm_epsilon = 1e-05
masked_score = -1e30


def shifted(value, axis, steps):
    count = lax.axis_size(axis)
    leading, last = (max(0, -steps), min(count, count - steps))
    return lax.ppermute(value, axis, [(source, source + steps) for source in range(leading, last)])


def layer_norm(values, gain_vec):
    row_mean = jnp.mean(values, axis=-1, keepdims=True)
    centred = values - row_mean
    spread = jnp.mean(centred * centred, axis=-1, keepdims=True)
    return centred * lax.rsqrt(spread + norm_epsilon) * gain_vec


def sigmoid(values):
    return 1.0 / (1.0 + jnp.exp(-values))


def attention_kernel(
    meta_ref, len_ref, table_ref, bias_t_ref, q_ref,
    prev_hbm, next_hbm, own_hbm, partner_hbm, sel_hbm,
    x_ref, gain_ref, ow_hbm, value_hbm, gate_w,
    mid_ref, cross_ref, partner_ref,
    ow_vmem, value_w, sems, att_ref, win_ref, gated_ref,
):
    base = meta_ref[0]
    core = meta_ref[1]
    planes = prev_hbm.shape[0]
    copies = [
        pltpu.make_async_copy(prev_hbm, win_ref.at[pl.ds(0, planes)], sems.at[2]),
        pltpu.make_async_copy(own_hbm, win_ref.at[pl.ds(2 * planes, planes)], sems.at[3]),
        pltpu.make_async_copy(next_hbm, win_ref.at[pl.ds(4 * planes, planes)], sems.at[4]),
        pltpu.make_async_copy(
            sel_hbm, win_ref.at[pl.ds(pl.multiple_of((1 + 2 * core) * planes, planes), planes)], sems.at[5]
        ),
        pltpu.make_async_copy(
            partner_hbm, win_ref.at[pl.ds(pl.multiple_of((3 - 2 * core) * planes, planes), planes)], sems.at[6]
        ),
    ]
    for copy in copies:
        copy.start()
    ow_copy = pltpu.make_async_copy(ow_hbm, ow_vmem, sems.at[0])
    value_copy = pltpu.make_async_copy(value_hbm.at[:, pl.ds(0, value_w.shape[1])], value_w, sems.at[1])
    ow_copy.start()
    value_copy.start()
    blocks = win_ref.shape[0] // planes
    rows, att_width = q_ref.shape
    heads = bias_t_ref.shape[0]
    buckets = bias_t_ref.shape[1]
    head_width = att_width // heads
    width = blocks * rows
    line_len = table_ref.shape[1]

    qpos = base + lax.broadcasted_iota(jnp.int32, (rows, 1), 0)
    kpos = base - REACH * rows + lax.broadcasted_iota(jnp.int32, (1, width), 1)

    def seg_step(u, carry):
        run, qs, ks = carry
        run = run + len_ref[u]
        return run, qs + (qpos >= run).astype(jnp.int32), ks + (kpos >= run).astype(jnp.int32)

    _, qseg, kseg = lax.fori_loop(
        0, len_ref.shape[0], seg_step,
        (jnp.int32(0), jnp.zeros((rows, 1), jnp.int32), jnp.zeros((1, width), jnp.int32)),
    )
    kseg = jnp.where(kpos < 0, -1, kseg)
    same = qseg == kseg

    table = table_ref[...]
    bias_t = bias_t_ref[...]
    line = jnp.zeros((heads, line_len), jnp.float32)
    for b in range(buckets):
        line = jnp.where(table == b, bias_t[:, b:b + 1], line)

    for copy in copies:
        copy.wait()
    scaling = head_width ** (-0.5)
    lane = lax.broadcasted_iota(jnp.int32, (rows, LANES), 1)
    per_pair = LANES // head_width
    for pair in range(att_width // LANES):
        cols = slice(pair * LANES, (pair + 1) * LANES)
        q_pair = q_ref[:, cols]
        k_pair = jnp.concatenate([win_ref[planes * j, :, cols] for j in range(blocks)], axis=0)
        v_pair = jnp.concatenate([win_ref[planes * j + 1, :, cols] for j in range(blocks)], axis=0)
        q_rows, biases, masks = [], [], []
        for sub in range(per_pair):
            head = pair * per_pair + sub
            in_head = (lane >= sub * head_width) & (lane < (sub + 1) * head_width)
            q_rows.append(jnp.where(in_head, q_pair, jnp.zeros_like(q_pair)))
            spread = jnp.broadcast_to(line[head:head + 1, :], (rows, line_len))
            skew = pltpu.roll(spread, line_len - rows + 1, 1, stride=1, stride_axis=0)[:, :width]
            biases.append(jnp.where(same, skew, masked_score))
            masks.append(in_head)
        scores = lax.dot_general(
            jnp.concatenate(q_rows, axis=0), k_pair, (((1,), (1,)), ((), ())), preferred_element_type=jnp.float32
        )
        scores = scores * scaling + jnp.concatenate(biases, axis=0)
        top = jnp.max(scores, axis=1, keepdims=True)
        weights = jnp.exp(scores - top)
        total = jnp.sum(weights, axis=1, keepdims=True)
        summed = jnp.dot(weights.astype(jnp.bfloat16), v_pair, preferred_element_type=jnp.float32)
        part = summed / total
        result = part[0:rows]
        for sub in range(1, per_pair):
            result = jnp.where(masks[sub], part[sub * rows:(sub + 1) * rows], result)
        att_ref[:, cols] = result.astype(jnp.bfloat16)

    ow_copy.wait()
    projected = jnp.dot(att_ref[...], ow_vmem[...], preferred_element_type=jnp.float32)
    mid = (x_ref[...].astype(jnp.float32) + projected).astype(jnp.bfloat16)
    mid_ref[...] = mid
    normed = layer_norm(mid.astype(jnp.float32), gain_ref[...]).astype(jnp.bfloat16)
    model_width = mid.shape[1]
    value_copy.wait()
    value_half = jnp.dot(normed, value_w[...], preferred_element_type=jnp.float32)
    gate_half = jnp.dot(normed, gate_w[...], preferred_element_type=jnp.float32)
    gated = (value_half * sigmoid(gate_half)).astype(jnp.bfloat16)
    gated_ref[...] = gated
    half = cross_ref.shape[0]
    cross_ref[...] = gated_ref[pl.ds(pl.multiple_of(core * half, half), half), :]
    partner_ref[...] = gated_ref[pl.ds(pl.multiple_of((1 - core) * half, half), half), :]


def conv_kernel(
    meta_ref, own_cross_ref, own_partner_ref, cross_ref, pairg_ref, taps_ref, gain_ref, mid_ref, sw_hbm,
    out_ref, win_ref, conv_ref, sw_vmem, sems,
):
    sw_copy = pltpu.make_async_copy(sw_hbm, sw_vmem, sems.at[0])
    sw_copy.start()
    half = cross_ref.shape[0]
    rows, model_width = mid_ref.shape
    core = meta_ref[1]
    outer = rows + half

    def place(first, ref):
        win_ref[pl.ds(pl.multiple_of(first, half), half), :] = ref[...].astype(jnp.float32)

    place(core * outer, cross_ref)
    place((1 - core) * outer, pairg_ref)
    place(half + core * half, own_cross_ref)
    place(2 * half - core * half, own_partner_ref)
    reach = DILATION * (KERNEL - 1) // 2
    start = half - reach

    def chunk(c, carry):
        lanes = pl.ds(pl.multiple_of(c * LANES, LANES), LANES)
        acc = jnp.zeros((rows, LANES), jnp.float32)
        for tap in range(KERNEL):
            first = start + DILATION * tap
            acc = acc + taps_ref[tap:tap + 1, lanes] * win_ref[first:first + rows, lanes]
        conv_ref[:, lanes] = acc
        return carry

    lax.fori_loop(0, model_width // LANES, chunk, 0)
    inner = layer_norm(conv_ref[...], gain_ref[...])
    activated = (inner * sigmoid(inner)).astype(jnp.bfloat16)
    sw_copy.wait()
    shrunk = jnp.dot(activated, sw_vmem[...], preferred_element_type=jnp.float32)
    out_ref[...] = (mid_ref[...].astype(jnp.float32) + shrunk).astype(out_ref.dtype)


def on_device(
    frames_in,
    query_proj,
    key_proj,
    value_proj,
    utterance_lengths,
    bucket_table,
    bucket_bias,
    out_weight,
    norm_gain,
    expand_weight,
    depth_taps,
    inner_gain,
    shrink_weight,
):
    rows, att_width = query_proj.shape
    model_width = frames_in.shape[1]
    heads = bucket_bias.shape[1]
    core = lax.axis_index("core")
    cores = lax.axis_size("core")
    count = lax.axis_size("chip") * cores
    device_index = lax.axis_index("chip") * cores + core
    meta = jnp.stack([device_index * rows, core]).astype(jnp.int32)

    def lin_shift(value, steps):
        leading, last = (max(0, -steps), min(count, count - steps))
        return lax.ppermute(value, ("chip", "core"), [(s, s + steps) for s in range(leading, last)])

    line_len = -(-bucket_table.shape[0] // LANES) * LANES
    table = jnp.pad(bucket_table, (0, line_len - bucket_table.shape[0])).reshape(1, line_len)
    bias_t = bucket_bias.T

    packed = jnp.stack([key_proj, value_proj])
    from_prev = lin_shift(packed, REACH)
    from_next = lin_shift(packed, -REACH)
    swap = [(0, 1), (1, 0)]
    gated_input, table, meta, bias_t, gate_weight = lax.optimization_barrier((packed, table, meta, bias_t, expand_weight[:, model_width:]))
    partner = lax.ppermute(gated_input, "core", swap)
    sel = jnp.where(core == 0, from_next, from_prev)
    partner_sel = lax.ppermute(sel, "core", swap)
    order = list(range(-REACH, REACH + 1))

    half = rows // 2
    vmem = pl.BlockSpec(memory_space=pltpu.VMEM)
    smem = pl.BlockSpec(memory_space=pltpu.SMEM)
    anywhere = pl.BlockSpec(memory_space=pl.ANY)
    window = len(order) * rows
    attn_flops = 2 * 2 * heads * rows * window * LANES + 2 * rows * att_width * model_width + 2 * rows * model_width * 2 * model_width
    attn_bytes = 2 * (rows * att_width * (1 + 2 * len(order)) + rows * model_width * 2 + att_width * model_width + model_width * 2 * model_width)
    mid, cross_send, partner_send = pl.pallas_call(
        attention_kernel,
        out_shape=(
            jax.ShapeDtypeStruct((rows, model_width), jnp.bfloat16),
            jax.ShapeDtypeStruct((half, model_width), jnp.bfloat16),
            jax.ShapeDtypeStruct((half, model_width), jnp.bfloat16),
        ),
        in_specs=[smem, smem, vmem, vmem, vmem] + [anywhere] * 5 + [vmem, vmem, anywhere, anywhere, vmem],
        out_specs=(vmem, vmem, vmem),
        scratch_shapes=[
            pltpu.VMEM((att_width, model_width), jnp.bfloat16),
            pltpu.VMEM((model_width, model_width), jnp.bfloat16),
            pltpu.SemaphoreType.DMA((7,)),
            pltpu.VMEM((rows, att_width), jnp.bfloat16),
            pltpu.VMEM((len(order) * packed.shape[0], rows, att_width), jnp.bfloat16),
            pltpu.VMEM((rows, model_width), jnp.bfloat16),
        ],
        cost_estimate=pl.CostEstimate(
            flops=attn_flops, transcendentals=heads * rows * window + rows * model_width, bytes_accessed=attn_bytes
        ),
        name="attention_glu",
    )(
        meta, utterance_lengths, table, bias_t, query_proj, *[pltpu.with_memory_space_constraint(a, pltpu.VMEM) for a in (from_prev, from_next)], packed, *[pltpu.with_memory_space_constraint(a, pltpu.VMEM) for a in (partner, partner_sel)],
        frames_in, norm_gain.reshape(1, -1), out_weight,
        expand_weight,
        pltpu.with_memory_space_constraint(gate_weight, pltpu.VMEM),
    )

    chips = count // cores
    inward = [(2 * c + 1, 2 * c + 2) for c in range(chips - 1)] + [(2 * c, 2 * c - 1) for c in range(1, chips)]
    cross_recv = lax.ppermute(cross_send, ("chip", "core"), inward)
    partner_recv = lax.ppermute(partner_send, "core", swap)
    conv_flops = 2 * KERNEL * rows * model_width + 2 * rows * model_width * model_width
    conv_bytes = 2 * (4 * half * model_width + rows * model_width * 2 + model_width * model_width) + 4 * KERNEL * model_width
    return pl.pallas_call(
        conv_kernel,
        out_shape=jax.ShapeDtypeStruct((rows, model_width), jnp.bfloat16),
        in_specs=[smem] + [vmem] * 7 + [anywhere],
        out_specs=vmem,
        scratch_shapes=[
            pltpu.VMEM((rows + 2 * half, model_width), jnp.float32),
            pltpu.VMEM((rows, model_width), jnp.float32),
            pltpu.VMEM((model_width, model_width), jnp.bfloat16),
            pltpu.SemaphoreType.DMA((1,)),
        ],
        cost_estimate=pl.CostEstimate(
            flops=conv_flops, transcendentals=rows * model_width, bytes_accessed=conv_bytes
        ),
        name="conv_shrink",
    )(meta, cross_send, partner_send, pltpu.with_memory_space_constraint(cross_recv, pltpu.VMEM), pltpu.with_memory_space_constraint(partner_recv, pltpu.VMEM), pltpu.with_memory_space_constraint(depth_taps, pltpu.VMEM), pltpu.with_memory_space_constraint(inner_gain.reshape(1, -1), pltpu.VMEM), mid, shrink_weight)


def solution(mesh):
    groups, seq = mesh.devices.shape
    chip_mesh = jax.sharding.Mesh(mesh.devices.reshape(groups, seq // 2, 2), ("groups", "chip", "core"))
    rows_spec = P(("groups", "chip", "core"), None)
    placed = (
        rows_spec,
        rows_spec,
        rows_spec,
        rows_spec,
        P("groups"),
        P(),
        P(),
        P(),
        P(),
        P(),
        P(),
        P(),
        P(),
    )
    return jax.shard_map(
        on_device, mesh=chip_mesh, in_specs=placed, out_specs=rows_spec, check_vma=False
    )
```
